128 devices in a mesh: freq: 32 (over z, x_hi, y), dish: 4 (over x_lo, core).
Axes of the slice: x: 4 (x_hi: 2, x_lo: 2; x = x_hi * 2 + x_lo), y: 4, z: 4, core: 2. Of those that a mesh axis runs over, the one named last changes fastest.
Arguments:
- voltages: bfloat16 [256, 4, 2, 155648], P('freq', 'dish'), may hold values from -6 to 6
- feed_gains: bfloat16 [256, 4, 2, 8192], P('freq', 'dish'), may hold values from -4.1875 to 4.1875
- block_assign: int32 [32], replicated, may hold values from 0 to 31, each once
- grid_rows: int32 [4, 256], replicated, may hold values from 0 to 255, each once within a row
Outputs:
- beam_power: float32 [8192, 1024], P('freq', 'dish')
The draws below stay inside these ranges and needn't reach their ends.
Inputs may be any that keep to these rules, and one draw needn't show every extreme that they name: block_assign names every channel block once. Each row of grid_rows names every grid row once.
All inputs are finite; a program needn't handle non-finite values.
Results may differ from the reference program's by a relative error of at most 0.0042.
Values may be sent and summed in bfloat16 or wider, within the bound.
No kernel may reach another device: no remote copies, remote signals or barrier semaphores. Data moves between devices by JAX's collectives and lax.ppermute only.
A program may use at most 128 MiB of HBM per device.

```python
import math
import jax
import jax.numpy as jnp
import numpy as np
from jax import lax

DISHES = 1024
NCHAN = 8192
CHA = 64
CHB = 128
TAPS = 4
FRAMES = 16
GRIDLEN = 256
CBLOCK = 256
NBLOCKS = 32
SAMPLES = 155648
N_DISH = 4


def steps_of(own_key, shape, pieces, smallest, top_value):
    gain = 1.0
    for dim, blocks in pieces:
        steps = jax.random.uniform(jax.random.fold_in(jax.random.fold_in(own_key, 6), dim), (blocks,), jnp.float32, smallest / len(pieces), top_value / len(pieces))
        gain = gain * jnp.repeat(jnp.exp(steps), shape[dim] // blocks).reshape((-1,) + (1,) * (len(shape) - 1 - dim))
    return gain


def bell_draw(stream_key, dims, width, bound, split=(), kind=jnp.bfloat16):
    values = jax.random.normal(stream_key, dims, jnp.float32) * width
    if len(split) > 0:
        values = steps_of(stream_key, dims, split, -0.22, 0.18) * values
    return jnp.clip(values, min=-bound, max=bound).astype(kind)


def setup_inputs(seed: int = 0) -> dict:
    key_list = jax.random.split(jax.random.key(seed), 5)
    return {
        "voltages": bell_draw(key_list[0], (GRIDLEN, N_DISH, 2, SAMPLES), 1.0, 6.0, ((0, 32), (1, 4))),
        "feed_gains": bell_draw(key_list[1], (GRIDLEN, N_DISH, 2, NCHAN), 0.7, 4.1875, ((0, 32), (1, 4))),
        "block_assign": jax.random.permutation(key_list[2], NBLOCKS).astype(jnp.int32),
        "grid_rows": jax.vmap(lambda own: jax.random.permutation(own, GRIDLEN))(jax.random.split(key_list[3], N_DISH)).reshape((N_DISH, GRIDLEN)).astype(jnp.int32),
    }


full_turn = 2.0 * math.pi

def fourier_table(row_index, col_index, modulus, scaling):
    phases = row_index[:, None] * col_index[None, :] % modulus
    angles = full_turn / modulus * phases.astype(jnp.float32)
    cosine_table = (jnp.cos(angles) * scaling).astype(jnp.bfloat16)
    sine_table = (jnp.sin(angles) * scaling).astype(jnp.bfloat16)
    upper_rows = jnp.stack([cosine_table, -sine_table], axis=1)
    lower_rows = jnp.stack([sine_table, cosine_table], axis=1)
    return jnp.stack([upper_rows, lower_rows], axis=0)

def rotate(real_part, imag_part, angles):
    cosine_part = jnp.cos(angles)
    sine_part = jnp.sin(angles)
    return (real_part * cosine_part - imag_part * sine_part, real_part * sine_part + imag_part * cosine_part)

def filter_window():
    sample_index = jnp.arange(TAPS * NCHAN, dtype=jnp.float32)
    centred = (sample_index - TAPS * NCHAN / 2 + 0.5) / NCHAN
    taper_curve = 0.5 - 0.5 * jnp.cos(full_turn * (sample_index + 0.5) / (TAPS * NCHAN))
    shaped_window = (jnp.sinc(centred) * taper_curve).reshape(TAPS, NCHAN)
    energy = jnp.mean(lax.optimization_barrier(jnp.sum(shaped_window * shaped_window, axis=0)))
    return shaped_window / jnp.sqrt(energy)

def channelize(dish_volts, dish_gains):
    dish_rows = dish_volts.shape[0]
    window = filter_window()
    framed = dish_volts.reshape(dish_rows, 2, FRAMES + TAPS - 1, NCHAN).astype(jnp.float32)
    filtered = window[0] * framed[:, :, 0:FRAMES]
    for tap_index in range(1, TAPS):
        filtered = filtered + window[tap_index] * framed[:, :, tap_index:tap_index + FRAMES]
    filtered = filtered.astype(jnp.bfloat16)
    blocks = filtered.reshape(dish_rows, 2, FRAMES, CHA, CHB).astype(jnp.float32)
    first_index = jnp.arange(CHA, dtype=jnp.int32)
    second_index = jnp.arange(CHB, dtype=jnp.int32)
    first_table = fourier_table(first_index, first_index, CHA, 1.0 / math.sqrt(CHA)).astype(jnp.float32)
    section_one = jnp.einsum('rpfab,paqc->rfqcb', blocks, first_table, preferred_element_type=jnp.float32)
    angles = -(full_turn / NCHAN) * (first_index[:, None] * second_index[None, :] % NCHAN).astype(jnp.float32)
    real_part, imag_part = rotate(section_one[:, :, 0], section_one[:, :, 1], angles)
    turned = jnp.stack([real_part, imag_part], axis=2).astype(jnp.bfloat16).astype(jnp.float32)
    second_table = fourier_table(second_index, second_index, CHB, 1.0 / math.sqrt(CHB)).astype(jnp.float32)
    spectrum = jnp.einsum('rfqcb,qbse->rfsec', turned, second_table, preferred_element_type=jnp.float32)
    spectrum = spectrum.reshape(dish_rows, FRAMES, 2, NCHAN)
    gain_real = dish_gains[:, 0][:, None, :].astype(jnp.float32)
    gain_imag = dish_gains[:, 1][:, None, :].astype(jnp.float32)
    spectrum_real = spectrum[:, :, 0]
    spectrum_imag = spectrum[:, :, 1]
    out_real = spectrum_real * gain_real - spectrum_imag * gain_imag
    out_imag = spectrum_real * gain_imag + spectrum_imag * gain_real
    return jnp.stack([out_real, out_imag], axis=2).astype(jnp.bfloat16)

def reference(voltages, feed_gains, block_assign, grid_rows):

    def channel_group(members):
        return channelize(members[0], members[1])
    channelized = lax.map(channel_group, (voltages, feed_gains))
    dish_count = N_DISH
    grid_len = GRIDLEN
    positions = jnp.arange(grid_len, dtype=jnp.int32)

    def grid_table(grid_line):
        return fourier_table(grid_line, positions, grid_len, 1.0 / math.sqrt(grid_len))
    tables = jax.vmap(grid_table)(grid_rows).astype(jnp.float32)
    feed_index = jnp.arange(dish_count, dtype=jnp.int32)
    twist_angles = -(full_turn / DISHES) * (feed_index[:, None] * positions[None, :] % DISHES).astype(jnp.float32)
    cross_phases = full_turn / dish_count * (feed_index[:, None] * feed_index[None, :] % dish_count).astype(jnp.float32)
    cross_cos = jnp.cos(cross_phases) / math.sqrt(dish_count)
    cross_sin = jnp.sin(cross_phases) / math.sqrt(dish_count)
    bit_count = dish_count.bit_length() - 1
    reversal = np.array([sum(((member >> bit_index & 1) << bit_count - 1 - bit_index for bit_index in range(bit_count))) for member in range(dish_count)], dtype=np.int32)
    highest = lax.Precision.HIGHEST

    def form_beams(block_index):
        start_row = (block_assign[block_index] * CBLOCK).astype(jnp.int32)
        channel_block = lax.dynamic_slice_in_dim(channelized, start_row, CBLOCK, axis=4).astype(jnp.float32)
        local_sums = jnp.einsum('mdfpc,dpmqk->dfcqk', channel_block, tables, preferred_element_type=jnp.float32)
        real_part, imag_part = rotate(local_sums[:, :, :, 0], local_sums[:, :, :, 1], twist_angles[:, None, None, :])
        rounded = jnp.stack([real_part, imag_part], axis=3).astype(jnp.bfloat16)
        partial_value = lax.optimization_barrier(rounded).astype(jnp.float32)
        part_real = partial_value[:, :, :, 0]
        part_imag = partial_value[:, :, :, 1]
        beam_real = jnp.einsum('dk,dfcb->kfcb', cross_cos, part_real, precision=highest) + jnp.einsum('dk,dfcb->kfcb', cross_sin, part_imag, precision=highest)
        beam_imag = jnp.einsum('dk,dfcb->kfcb', cross_cos, part_imag, precision=highest) - jnp.einsum('dk,dfcb->kfcb', cross_sin, part_real, precision=highest)
        beam_power = lax.optimization_barrier(jnp.mean(beam_real * beam_real + beam_imag * beam_imag, axis=1))
        beam_power = beam_power[reversal]
        return jnp.transpose(beam_power, (1, 0, 2)).reshape(CBLOCK, DISHES)
    result = lax.map(form_beams, jnp.arange(NBLOCKS, dtype=jnp.int32))
    return result.reshape(NCHAN, DISHES)
```

```python
import math

import jax
import jax.numpy as jnp
from jax import lax
from jax.sharding import PartitionSpec as P

NCHAN = 8192
CHA = 64
CHB = 128
TAPS = 4
FRAMES = 16


full_turn = 2.0 * math.pi


def swapped(shard, axis, distance):
    return lax.ppermute(shard, axis, [(i, i ^ 1 << distance) for i in range(lax.axis_size(axis))])


def fourier_table(row_index, col_index, modulus, scaling):
    phases = row_index[:, None] * col_index[None, :] % modulus
    angles = full_turn / modulus * phases.astype(jnp.float32)
    cosine_table = (jnp.cos(angles) * scaling).astype(jnp.bfloat16)
    sine_table = (jnp.sin(angles) * scaling).astype(jnp.bfloat16)
    upper_rows = jnp.stack([cosine_table, -sine_table], axis=1)
    lower_rows = jnp.stack([sine_table, cosine_table], axis=1)
    return jnp.stack([upper_rows, lower_rows], axis=0)


def rotate(real_part, imag_part, angles):
    cosine_part = jnp.cos(angles)
    sine_part = jnp.sin(angles)
    return (
        real_part * cosine_part - imag_part * sine_part,
        real_part * sine_part + imag_part * cosine_part,
    )


def filter_window():
    sample_index = jnp.arange(TAPS * NCHAN, dtype=jnp.float32)
    centred = (sample_index - TAPS * NCHAN / 2 + 0.5) / NCHAN
    taper_curve = 0.5 - 0.5 * jnp.cos(full_turn * (sample_index + 0.5) / (TAPS * NCHAN))
    shaped_window = (jnp.sinc(centred) * taper_curve).reshape(TAPS, NCHAN)
    energy = jnp.mean(jnp.sum(shaped_window * shaped_window, axis=0))
    return shaped_window / jnp.sqrt(energy)


def channelize(dish_volts, dish_gains):
    dish_rows = dish_volts.shape[0]
    window = filter_window()
    framed = dish_volts.reshape(dish_rows, 2, FRAMES + TAPS - 1, NCHAN)
    filtered = window[0] * framed[:, :, 0:FRAMES]
    for tap_index in range(1, TAPS):
        filtered = filtered + window[tap_index] * framed[:, :, tap_index : tap_index + FRAMES]
    filtered = filtered.astype(jnp.bfloat16)
    blocks = filtered.reshape(dish_rows, 2, FRAMES, CHA, CHB)
    first_index = jnp.arange(CHA, dtype=jnp.int32)
    second_index = jnp.arange(CHB, dtype=jnp.int32)
    first_table = fourier_table(first_index, first_index, CHA, 1.0 / math.sqrt(CHA))
    section_one = jnp.einsum(
        "rpfab,paqc->rfqcb", blocks, first_table, preferred_element_type=jnp.float32
    )
    angles = -(full_turn / NCHAN) * (first_index[:, None] * second_index[None, :] % NCHAN).astype(
        jnp.float32
    )
    real_part, imag_part = rotate(section_one[:, :, 0], section_one[:, :, 1], angles)
    turned = jnp.stack([real_part, imag_part], axis=2).astype(jnp.bfloat16)
    second_table = fourier_table(second_index, second_index, CHB, 1.0 / math.sqrt(CHB))
    spectrum = jnp.einsum(
        "rfqcb,qbse->rfsec", turned, second_table, preferred_element_type=jnp.float32
    )
    spectrum = spectrum.reshape(dish_rows, FRAMES, 2, NCHAN)
    gain_real = dish_gains[:, 0][:, None, :].astype(jnp.float32)
    gain_imag = dish_gains[:, 1][:, None, :].astype(jnp.float32)
    spectrum_real = spectrum[:, :, 0]
    spectrum_imag = spectrum[:, :, 1]
    out_real = spectrum_real * gain_real - spectrum_imag * gain_imag
    out_imag = spectrum_real * gain_imag + spectrum_imag * gain_real
    return jnp.stack([out_real, out_imag], axis=2).astype(jnp.bfloat16)


def beam_tables(grid_line, grid_len):
    positions = jnp.arange(grid_len, dtype=jnp.int32)
    phases = positions[:, None] * grid_line[None, :] % grid_len
    angles = full_turn / grid_len * phases.astype(jnp.float32)
    scaling = 1.0 / math.sqrt(grid_len)
    cosine_table = (jnp.cos(angles) * scaling).astype(jnp.bfloat16)
    sine_table = (jnp.sin(angles) * scaling).astype(jnp.bfloat16)
    real_rows = jnp.stack([cosine_table, sine_table], axis=2)
    imag_rows = jnp.stack([-sine_table, cosine_table], axis=2)
    return jnp.stack([real_rows, imag_rows], axis=0).reshape(2 * grid_len, 2 * grid_len)


def body(voltages, feed_gains, block_assign, grid_rows):
    dish_rows = voltages.shape[0]
    channelized = channelize(voltages[:, 0], feed_gains[:, 0])
    block_count = lax.axis_size("freq")
    dish_count = lax.axis_size("dish")
    block_width = NCHAN // block_count
    quarter = block_width // dish_count
    split = channelized.reshape(dish_rows, FRAMES, 2, block_count, dish_count, quarter)
    ordered = jnp.take(split, block_assign, axis=3)
    ordered = jnp.transpose(ordered, (0, 2, 1, 4, 3, 5)).reshape(
        dish_rows, 2, FRAMES, dish_count * block_count, quarter
    )
    gathered = lax.all_to_all(ordered, ("dish", "freq"), 3, 0, tiled=True)
    grid_len = dish_rows * block_count
    total_dishes = grid_len * dish_count
    gathered = gathered.reshape(dish_count, grid_len * 2, FRAMES * quarter)
    tables = jax.vmap(lambda line: beam_tables(line, grid_len))(grid_rows)
    local_sums = jnp.einsum("dxy,dyz->dxz", tables, gathered, preferred_element_type=jnp.float32)
    local_sums = local_sums.reshape(dish_count, 2, grid_len, FRAMES, quarter)
    feed_index = jnp.arange(dish_count, dtype=jnp.int32)
    positions = jnp.arange(grid_len, dtype=jnp.int32)
    twist_angles = -(full_turn / total_dishes) * (
        feed_index[:, None] * positions[None, :] % total_dishes
    ).astype(jnp.float32)
    twist_angles = twist_angles[:, :, None, None]
    real_part, imag_part = rotate(local_sums[:, 0], local_sums[:, 1], twist_angles)
    part_real = real_part.astype(jnp.bfloat16).astype(jnp.float32)
    part_imag = imag_part.astype(jnp.bfloat16).astype(jnp.float32)
    a_re, b_re, c_re, d_re = part_real[0], part_real[1], part_real[2], part_real[3]
    a_im, b_im, c_im, d_im = part_imag[0], part_imag[1], part_imag[2], part_imag[3]
    beams = [
        (a_re + b_re + c_re + d_re, a_im + b_im + c_im + d_im),
        (a_re + b_im - c_re - d_im, a_im - b_re - c_im + d_re),
        (a_re - b_re + c_re - d_re, a_im - b_im + c_im - d_im),
        (a_re - b_im - c_re + d_im, a_im + b_re - c_im - d_re),
    ]
    reversal = [int(format(s, "0%db" % (dish_count.bit_length() - 1))[::-1], 2) for s in range(dish_count)]
    powers = []
    for s in range(dish_count):
        beam_real, beam_imag = beams[reversal[s]]
        power = jnp.mean(beam_real * beam_real + beam_imag * beam_imag, axis=1) * 0.25
        powers.append(jnp.transpose(power, (1, 0)))
    send = jnp.stack(powers, axis=0)
    received = lax.all_to_all(send, "dish", 0, 0, tiled=True)
    return received.reshape(block_width, grid_len)


def solution(mesh):
    placed = (P("freq", "dish", None, None), P("freq", "dish", None, None), P(), P())
    return jax.shard_map(
        body, mesh=mesh, in_specs=placed, out_specs=P("freq", "dish"), check_vma=False
    )
```

```python
import math

import jax
import jax.numpy as jnp
from jax import lax
from jax.experimental import pallas as pl
from jax.experimental.pallas import tpu as pltpu
from jax.sharding import PartitionSpec as P

NCHAN = 8192
CHA = 64
CHB = 128
TAPS = 4
FRAMES = 16


full_turn = 2.0 * math.pi


def fourier_table(row_index, col_index, modulus, scaling):
    phases = row_index[:, None] * col_index[None, :] % modulus
    angles = full_turn / modulus * phases.astype(jnp.float32)
    cosine_table = (jnp.cos(angles) * scaling).astype(jnp.bfloat16)
    sine_table = (jnp.sin(angles) * scaling).astype(jnp.bfloat16)
    upper_rows = jnp.stack([cosine_table, -sine_table], axis=1)
    lower_rows = jnp.stack([sine_table, cosine_table], axis=1)
    return jnp.stack([upper_rows, lower_rows], axis=0)


def filter_window():
    sample_index = jnp.arange(TAPS * NCHAN, dtype=jnp.float32)
    centred = (sample_index - TAPS * NCHAN / 2 + 0.5) / NCHAN
    taper_curve = 0.5 - 0.5 * jnp.cos(full_turn * (sample_index + 0.5) / (TAPS * NCHAN))
    shaped_window = (jnp.sinc(centred) * taper_curve).reshape(TAPS, NCHAN)
    energy = jnp.mean(jnp.sum(shaped_window * shaped_window, axis=0))
    return shaped_window / jnp.sqrt(energy)


def beam_tables(grid_line, grid_len, rows_per_device):
    positions = jnp.arange(grid_len, dtype=jnp.int32)
    phases = positions[:, None] * grid_line[None, :] % grid_len
    angles = full_turn / grid_len * phases.astype(jnp.float32)
    scaling = 1.0 / math.sqrt(grid_len)
    cosine_table = (jnp.cos(angles) * scaling).astype(jnp.bfloat16)
    sine_table = (jnp.sin(angles) * scaling).astype(jnp.bfloat16)
    real_rows = jnp.stack([cosine_table, sine_table], axis=2)
    imag_rows = jnp.stack([-sine_table, cosine_table], axis=2)
    table = jnp.stack([real_rows, imag_rows], axis=0)
    devices = grid_len // rows_per_device
    table = table.reshape(2, grid_len, devices, rows_per_device, 2)
    table = jnp.transpose(table, (0, 1, 3, 4, 2))
    return table.reshape(2 * grid_len, 2 * grid_len)


def channelize_kernel(v_ref, w_ref, t1_ref, tw_ref, t2_ref, g_ref, o_ref):
    cos_tw = tw_ref[0]
    sin_tw = tw_ref[1]
    t1 = t1_ref[...]
    t2_real = t2_ref[0]
    t2_imag = t2_ref[1]
    g_real = g_ref[0, 0]
    g_imag = g_ref[0, 1]
    half = t2_real.shape[0] // 2

    def one_frame(frame):
        acc = None
        for tap in range(TAPS):
            start = pl.multiple_of((frame + tap) * CHA, CHA)
            piece = v_ref[0, :, pl.ds(start, CHA), :].astype(jnp.float32)
            term = w_ref[tap][None] * piece
            acc = term if acc is None else acc + term
        block = acc.astype(jnp.bfloat16).reshape(2 * CHA, CHB)
        section = jnp.dot(t1, block, preferred_element_type=jnp.float32)
        sec_real = section[:CHA]
        sec_imag = section[CHA:]
        turned_real = sec_real * cos_tw - sec_imag * sin_tw
        turned_imag = sec_real * sin_tw + sec_imag * cos_tw
        return turned_real.astype(jnp.bfloat16), turned_imag.astype(jnp.bfloat16)

    def pair(step, carry):
        first_real, first_imag = one_frame(2 * step)
        second_real, second_imag = one_frame(2 * step + 1)
        both_real = jnp.concatenate([first_real, second_real], axis=0)
        both_imag = jnp.concatenate([first_imag, second_imag], axis=0)
        dims = (((1,), (1,)), ((), ()))
        spectrum = lax.dot_general(
            t2_real, both_real, dims, preferred_element_type=jnp.float32
        ) + lax.dot_general(t2_imag, both_imag, dims, preferred_element_type=jnp.float32)
        spec_real = spectrum[:half]
        spec_imag = spectrum[half:]
        out_real = spec_real * g_real - spec_imag * g_imag
        out_imag = spec_real * g_imag + spec_imag * g_real
        lanes = pl.ds(pl.multiple_of(step * 2 * CHA, 2 * CHA), 2 * CHA)
        o_ref[0, 0, :, lanes] = out_real.astype(o_ref.dtype)
        o_ref[0, 1, :, lanes] = out_imag.astype(o_ref.dtype)
        return carry

    lax.fori_loop(0, FRAMES // 2, pair, 0)


def beam_kernel(dish_count, x_ref, t_ref, c_ref, s_ref, o_ref, acc_ref):
    step = pl.program_id(0)
    rows = x_ref.shape[0] * x_ref.shape[1]
    devices = x_ref.shape[2] // dish_count
    grid_len = t_ref.shape[1] // 2

    @pl.when(step == 0)
    def _():
        acc_ref[...] = jnp.zeros_like(acc_ref)

    parts = []
    for d in range(dish_count):
        block = x_ref[:, :, pl.ds(d * devices, devices), :].reshape(rows * devices, x_ref.shape[3])
        sums = jnp.dot(t_ref[d], block, preferred_element_type=jnp.float32)
        sum_real = sums[:grid_len]
        sum_imag = sums[grid_len:]
        cos_d = c_ref[d]
        sin_d = s_ref[d]
        part_real = sum_real * cos_d - sum_imag * sin_d
        part_imag = sum_real * sin_d + sum_imag * cos_d
        parts.append(
            (
                part_real.astype(jnp.bfloat16).astype(jnp.float32),
                part_imag.astype(jnp.bfloat16).astype(jnp.float32),
            )
        )
    (a_re, a_im), (b_re, b_im), (c_re, c_im), (d_re, d_im) = parts
    beams = [
        (a_re + b_re + c_re + d_re, a_im + b_im + c_im + d_im),
        (a_re + b_im - c_re - d_im, a_im - b_re - c_im + d_re),
        (a_re - b_re + c_re - d_re, a_im - b_im + c_im - d_im),
        (a_re - b_im - c_re + d_im, a_im + b_re - c_im - d_re),
    ]
    for q in range(dish_count):
        beam_real, beam_imag = beams[q]
        acc_ref[q] += beam_real * beam_real + beam_imag * beam_imag

    @pl.when(step == pl.num_programs(0) - 1)
    def _():
        reversal = [
            int(format(s, "0%db" % (dish_count.bit_length() - 1))[::-1], 2)
            for s in range(dish_count)
        ]
        width = o_ref.shape[1]
        for s in range(dish_count):
            total = acc_ref[reversal[s]]
            total = total + pltpu.roll(total, width, 1)
            flipped = jnp.transpose(total, (1, 0))
            o_ref[s] = flipped[:width] * (0.25 / FRAMES)


def body(voltages, feed_gains, block_assign, grid_rows):
    dish_rows = voltages.shape[0]
    block_count = lax.axis_size("freq")
    dish_count = lax.axis_size("dish")
    block_width = NCHAN // block_count
    quarter = block_width // dish_count
    dests = block_count * dish_count
    grid_len = dish_rows * block_count
    total_dishes = grid_len * dish_count
    samples = voltages.shape[-1]

    dest = jnp.arange(dests, dtype=jnp.int32)
    dest_quarter = dest // block_count
    dest_block = jnp.take(block_assign, dest % block_count)
    dest_e = dest_block * dish_count + dest_quarter

    volts = voltages[:, 0].reshape(dish_rows, 2, samples // CHB, CHB)
    window = filter_window().reshape(TAPS, CHA, CHB)
    first_index = jnp.arange(CHA, dtype=jnp.int32)
    second_index = jnp.arange(CHB, dtype=jnp.int32)
    first_table = fourier_table(first_index, first_index, CHA, 1.0 / math.sqrt(CHA))
    first_table = jnp.transpose(first_table, (2, 3, 0, 1)).reshape(2 * CHA, 2 * CHA)
    angles = -(full_turn / NCHAN) * (first_index[:, None] * second_index[None, :] % NCHAN).astype(
        jnp.float32
    )
    twiddle = jnp.stack([jnp.cos(angles), jnp.sin(angles)], axis=0)
    second_table = fourier_table(second_index, second_index, CHB, 1.0 / math.sqrt(CHB))
    second_table = jnp.transpose(second_table, (0, 2, 3, 1))
    second_table = jnp.take(second_table, dest_e, axis=2).reshape(2, 2 * dests, CHB)
    gains = feed_gains[:, 0].reshape(dish_rows, 2, CHB, CHA).astype(jnp.float32)
    gains = jnp.take(gains, dest_e, axis=2)
    gains = jnp.concatenate([gains, gains], axis=3)

    channelized = pl.pallas_call(
        channelize_kernel,
        grid=(dish_rows,),
        in_specs=[
            pl.BlockSpec((1, 2, samples // CHB, CHB), lambda r: (r, 0, 0, 0)),
            pl.BlockSpec((TAPS, CHA, CHB), lambda r: (0, 0, 0)),
            pl.BlockSpec((2 * CHA, 2 * CHA), lambda r: (0, 0)),
            pl.BlockSpec((2, CHA, CHB), lambda r: (0, 0, 0)),
            pl.BlockSpec((2, 2 * dests, CHB), lambda r: (0, 0, 0)),
            pl.BlockSpec((1, 2, dests, 2 * CHA), lambda r: (r, 0, 0, 0)),
        ],
        out_specs=pl.BlockSpec((1, 2, dests, FRAMES * quarter), lambda r: (r, 0, 0, 0)),
        out_shape=jax.ShapeDtypeStruct((dish_rows, 2, dests, FRAMES * quarter), jnp.bfloat16),
    )(volts, window, first_table, twiddle, second_table, gains)

    gathered = lax.all_to_all(channelized, ("dish", "freq"), 2, 2, tiled=True)

    tables = jax.vmap(lambda line: beam_tables(line, grid_len, dish_rows))(grid_rows)
    feed_index = jnp.arange(dish_count, dtype=jnp.int32)
    positions = jnp.arange(grid_len, dtype=jnp.int32)
    twist_angles = -(full_turn / total_dishes) * (
        feed_index[:, None] * positions[None, :] % total_dishes
    ).astype(jnp.float32)
    twist_cos = jnp.cos(twist_angles)[:, :, None]
    twist_sin = jnp.sin(twist_angles)[:, :, None]
    lane_block = 2 * quarter
    steps = FRAMES * quarter // lane_block

    powers = pl.pallas_call(
        lambda *refs: beam_kernel(dish_count, *refs),
        grid=(steps,),
        in_specs=[
            pl.BlockSpec((dish_rows, 2, dests, lane_block), lambda f: (0, 0, 0, f)),
            pl.BlockSpec((dish_count, 2 * grid_len, 2 * grid_len), lambda f: (0, 0, 0)),
            pl.BlockSpec((dish_count, grid_len, 1), lambda f: (0, 0, 0)),
            pl.BlockSpec((dish_count, grid_len, 1), lambda f: (0, 0, 0)),
        ],
        out_specs=pl.BlockSpec((dish_count, quarter, grid_len), lambda f: (0, 0, 0)),
        out_shape=jax.ShapeDtypeStruct((dish_count, quarter, grid_len), jnp.float32),
        scratch_shapes=[pltpu.VMEM((dish_count, grid_len, lane_block), jnp.float32)],
    )(gathered, tables, twist_cos, twist_sin)

    received = lax.all_to_all(powers, "dish", 0, 0, tiled=True)
    return received.reshape(block_width, grid_len)


def solution(mesh):
    placed = (P("freq", "dish", None, None), P("freq", "dish", None, None), P(), P())
    return jax.shard_map(
        body, mesh=mesh, in_specs=placed, out_specs=P("freq", "dish"), check_vma=False
    )
```

```python
import functools
import math

import jax
import jax.numpy as jnp
from jax import lax
from jax.experimental import pallas as pl
from jax.experimental.pallas import tpu as pltpu
from jax.sharding import PartitionSpec as P

NCHAN = 8192
CHA = 64
CHB = 128
TAPS = 4
FRAMES = 16


full_turn = 2.0 * math.pi


def fourier_table(row_index, col_index, modulus, scaling):
    phases = row_index[:, None] * col_index[None, :] % modulus
    angles = full_turn / modulus * phases.astype(jnp.float32)
    cosine_table = (jnp.cos(angles) * scaling).astype(jnp.bfloat16)
    sine_table = (jnp.sin(angles) * scaling).astype(jnp.bfloat16)
    upper_rows = jnp.stack([cosine_table, -sine_table], axis=1)
    lower_rows = jnp.stack([sine_table, cosine_table], axis=1)
    return jnp.stack([upper_rows, lower_rows], axis=0)


def filter_window():
    sample_index = jnp.arange(TAPS * NCHAN, dtype=jnp.float32)
    centred = (sample_index - TAPS * NCHAN / 2 + 0.5) / NCHAN
    taper_curve = 0.5 - 0.5 * jnp.cos(full_turn * (sample_index + 0.5) / (TAPS * NCHAN))
    shaped_window = (jnp.sinc(centred) * taper_curve).reshape(TAPS, NCHAN)
    energy = jnp.mean(jnp.sum(shaped_window * shaped_window, axis=0))
    return shaped_window / jnp.sqrt(energy)


def beam_tables(grid_rows, grid_len, rows_per_device):
    positions = jnp.arange(grid_len, dtype=jnp.int32)
    phases = positions[:, None] * positions[None, :] % grid_len
    angles = full_turn / grid_len * phases.astype(jnp.float32)
    scaling = 1.0 / math.sqrt(grid_len)
    cosine_base = (jnp.cos(angles) * scaling).astype(jnp.bfloat16)
    sine_base = (jnp.sin(angles) * scaling).astype(jnp.bfloat16)
    devices = grid_len // rows_per_device
    ordered_rows = jnp.transpose(
        grid_rows.reshape(grid_rows.shape[0], devices, rows_per_device), (0, 2, 1)
    ).reshape(grid_rows.shape[0], grid_len)
    picks = (positions[None, :, None] == ordered_rows[:, None, :]).astype(jnp.bfloat16)
    cosine_table = jnp.einsum(
        "jg,dgm->djm", cosine_base, picks, preferred_element_type=jnp.float32
    ).astype(jnp.bfloat16)
    sine_table = jnp.einsum(
        "jg,dgm->djm", sine_base, picks, preferred_element_type=jnp.float32
    ).astype(jnp.bfloat16)
    real_rows = jnp.concatenate([cosine_table, sine_table], axis=2)
    imag_rows = jnp.concatenate([-sine_table, cosine_table], axis=2)
    return jnp.concatenate([real_rows, imag_rows], axis=1)


def channelize_kernel(first_pair, pairs, v_ref, w_ref, t1_ref, tw_ref, t2_ref, g_ref, o_ref):
    cos_tw = tw_ref[0]
    sin_tw = tw_ref[1]
    t1 = t1_ref[...]
    t2_real = t2_ref[0]
    t2_imag = t2_ref[1]
    g_real = g_ref[0, 0]
    g_imag = g_ref[0, 1]
    half = t2_real.shape[0] // 2

    def one_frame(frame):
        acc = None
        for tap in range(TAPS):
            start = pl.multiple_of((frame + tap) * CHA, CHA)
            piece = v_ref[0, :, pl.ds(start, CHA), :].astype(jnp.float32)
            term = w_ref[tap][None] * piece
            acc = term if acc is None else acc + term
        block = acc.astype(jnp.bfloat16).reshape(2 * CHA, CHB)
        section = jnp.dot(t1, block, preferred_element_type=jnp.float32)
        sec_real = section[:CHA]
        sec_imag = section[CHA:]
        turned_real = sec_real * cos_tw - sec_imag * sin_tw
        turned_imag = sec_real * sin_tw + sec_imag * cos_tw
        return turned_real.astype(jnp.bfloat16), turned_imag.astype(jnp.bfloat16)

    def pair(step, carry):
        first_real, first_imag = one_frame(2 * step)
        second_real, second_imag = one_frame(2 * step + 1)
        both_real = jnp.concatenate([first_real, second_real], axis=0)
        both_imag = jnp.concatenate([first_imag, second_imag], axis=0)
        dims = (((1,), (1,)), ((), ()))
        spectrum = lax.dot_general(
            t2_real, both_real, dims, preferred_element_type=jnp.float32
        ) + lax.dot_general(t2_imag, both_imag, dims, preferred_element_type=jnp.float32)
        spec_real = spectrum[:half]
        spec_imag = spectrum[half:]
        out_real = spec_real * g_real - spec_imag * g_imag
        out_imag = spec_real * g_imag + spec_imag * g_real
        lanes = pl.ds(pl.multiple_of((step - first_pair) * 2 * CHA, 2 * CHA), 2 * CHA)
        o_ref[0, 0, :, lanes] = out_real.astype(o_ref.dtype)
        o_ref[1, 0, :, lanes] = out_imag.astype(o_ref.dtype)
        return carry

    lax.fori_loop(first_pair, first_pair + pairs, pair, 0)


def beam_kernel(dish_count, carry_in, finish, *refs):
    if carry_in:
        x_ref, t_ref, c_ref, s_ref, init_ref, o_ref, acc_ref = refs
    else:
        x_ref, t_ref, c_ref, s_ref, o_ref, acc_ref = refs
    step = pl.program_id(0)
    rows = x_ref.shape[1]
    devices = x_ref.shape[2] // dish_count
    grid_len = t_ref.shape[1] // 2
    lanes = x_ref.shape[3]

    @pl.when(step == 0)
    def _():
        if carry_in:
            acc_ref[...] = init_ref[...]
        else:
            acc_ref[...] = jnp.zeros_like(acc_ref)

    parts = []
    for d in range(dish_count):
        block = x_ref[:, :, pl.ds(d * devices, devices), :].reshape(2 * rows * devices, lanes)
        sums = jnp.dot(t_ref[d], block, preferred_element_type=jnp.float32)
        sum_real = sums[:grid_len]
        sum_imag = sums[grid_len:]
        cos_d = c_ref[d]
        sin_d = s_ref[d]
        part_real = sum_real * cos_d - sum_imag * sin_d
        part_imag = sum_real * sin_d + sum_imag * cos_d
        parts.append(
            (
                part_real.astype(jnp.bfloat16).astype(jnp.float32),
                part_imag.astype(jnp.bfloat16).astype(jnp.float32),
            )
        )
    (a_re, a_im), (b_re, b_im), (c_re, c_im), (d_re, d_im) = parts
    beams = [
        (a_re + b_re + c_re + d_re, a_im + b_im + c_im + d_im),
        (a_re + b_im - c_re - d_im, a_im - b_re - c_im + d_re),
        (a_re - b_re + c_re - d_re, a_im - b_im + c_im - d_im),
        (a_re - b_im - c_re + d_im, a_im + b_re - c_im - d_re),
    ]
    for q in range(dish_count):
        beam_real, beam_imag = beams[q]
        acc_ref[q] += beam_real * beam_real + beam_imag * beam_imag

    @pl.when(step == pl.num_programs(0) - 1)
    def _():
        if not finish:
            o_ref[...] = acc_ref[...]
            return
        reversal = [
            int(format(s, "0%db" % (dish_count.bit_length() - 1))[::-1], 2)
            for s in range(dish_count)
        ]
        width = o_ref.shape[1]
        for s in range(dish_count):
            total = acc_ref[reversal[s]]
            total = total + pltpu.roll(total, width, 1)
            flipped = jnp.transpose(total, (1, 0))
            o_ref[s] = flipped[:width] * (0.25 / FRAMES)


def body(voltages, feed_gains, block_assign, grid_rows):
    dish_rows = voltages.shape[0]
    block_count = lax.axis_size("freq")
    dish_count = lax.axis_size("dish")
    block_width = NCHAN // block_count
    quarter = block_width // dish_count
    dests = block_count * dish_count
    grid_len = dish_rows * block_count
    total_dishes = grid_len * dish_count
    samples = voltages.shape[-1]

    dest = jnp.arange(dests, dtype=jnp.int32)
    dest_quarter = dest // block_count
    dest_block = jnp.take(block_assign, dest % block_count)
    dest_e = dest_block * dish_count + dest_quarter

    volts = voltages[:, 0].reshape(dish_rows, 2, samples // CHB, CHB)
    window = filter_window().reshape(TAPS, CHA, CHB)
    first_index = jnp.arange(CHA, dtype=jnp.int32)
    second_index = jnp.arange(CHB, dtype=jnp.int32)
    first_table = fourier_table(first_index, first_index, CHA, 1.0 / math.sqrt(CHA))
    first_table = jnp.transpose(first_table, (2, 3, 0, 1)).reshape(2 * CHA, 2 * CHA)
    angles = -(full_turn / NCHAN) * (first_index[:, None] * second_index[None, :] % NCHAN).astype(
        jnp.float32
    )
    twiddle = jnp.stack([jnp.cos(angles), jnp.sin(angles)], axis=0)
    second_table = fourier_table(second_index, second_index, CHB, 1.0 / math.sqrt(CHB))
    second_table = jnp.transpose(second_table, (0, 2, 3, 1))
    second_table = jnp.take(second_table, dest_e, axis=2).reshape(2, 2 * dests, CHB)
    gains = feed_gains[:, 0].reshape(dish_rows, 2, CHB, CHA).astype(jnp.float32)
    gains = jnp.take(gains, dest_e, axis=2)
    gains = jnp.concatenate([gains, gains], axis=3)

    chunks = 2
    pairs = FRAMES // 2 // chunks
    chunk_lanes = pairs * 2 * quarter
    tables = beam_tables(grid_rows, grid_len, dish_rows)
    feed_index = jnp.arange(dish_count, dtype=jnp.int32)
    positions = jnp.arange(grid_len, dtype=jnp.int32)
    twist_angles = -(full_turn / total_dishes) * (
        feed_index[:, None] * positions[None, :] % total_dishes
    ).astype(jnp.float32)
    twist_cos = jnp.cos(twist_angles)[:, :, None]
    twist_sin = jnp.sin(twist_angles)[:, :, None]
    lane_block = 2 * quarter

    def channelize_chunk(chunk):
        return pl.pallas_call(
            functools.partial(channelize_kernel, chunk * pairs, pairs),
            grid=(dish_rows,),
            in_specs=[
                pl.BlockSpec((1, 2, samples // CHB, CHB), lambda r: (r, 0, 0, 0)),
                pl.BlockSpec((TAPS, CHA, CHB), lambda r: (0, 0, 0)),
                pl.BlockSpec((2 * CHA, 2 * CHA), lambda r: (0, 0)),
                pl.BlockSpec((2, CHA, CHB), lambda r: (0, 0, 0)),
                pl.BlockSpec((2, 2 * dests, CHB), lambda r: (0, 0, 0)),
                pl.BlockSpec((1, 2, dests, 2 * CHA), lambda r: (r, 0, 0, 0)),
            ],
            out_specs=pl.BlockSpec((2, 1, dests, chunk_lanes), lambda r: (0, r, 0, 0)),
            out_shape=jax.ShapeDtypeStruct((2, dish_rows, dests, chunk_lanes), jnp.bfloat16),
            cost_estimate=pl.CostEstimate(
                flops=int(dish_rows * pairs * 2 * 2 * 128 * 128 * 128 * 3),
                bytes_accessed=int(voltages.size * 2 + 2 * dish_rows * dests * chunk_lanes * 2),
                transcendentals=0,
            ),
        )(volts, window, first_table, twiddle, second_table, gains)

    def beamform_chunk(received, carried, finish):
        carry_in = carried is not None
        in_specs = [
            pl.BlockSpec((2, dish_rows, dests, lane_block), lambda f: (0, 0, 0, f)),
            pl.BlockSpec((dish_count, 2 * grid_len, 2 * grid_len), lambda f: (0, 0, 0)),
            pl.BlockSpec((dish_count, grid_len, 1), lambda f: (0, 0, 0)),
            pl.BlockSpec((dish_count, grid_len, 1), lambda f: (0, 0, 0)),
        ]
        operands = [received, tables, twist_cos, twist_sin]
        if carry_in:
            in_specs.append(pl.BlockSpec((dish_count, grid_len, lane_block), lambda f: (0, 0, 0)))
            operands.append(carried)
        if finish:
            out_shape = (dish_count, quarter, grid_len)
        else:
            out_shape = (dish_count, grid_len, lane_block)
        return pl.pallas_call(
            functools.partial(beam_kernel, dish_count, carry_in, finish),
            grid=(chunk_lanes // lane_block,),
            in_specs=in_specs,
            out_specs=pl.BlockSpec(out_shape, lambda f: (0, 0, 0)),
            out_shape=jax.ShapeDtypeStruct(out_shape, jnp.float32),
            scratch_shapes=[pltpu.VMEM((dish_count, grid_len, lane_block), jnp.float32)],
            cost_estimate=pl.CostEstimate(
                flops=int(dish_count * 2 * 512 * 512 * chunk_lanes),
                bytes_accessed=int(received.size * 2 + tables.size * 2),
                transcendentals=0,
            ),
        )(*operands)

    sent = [channelize_chunk(c) for c in range(chunks)]
    arrived = [lax.all_to_all(s, ("dish", "freq"), 2, 2, tiled=True) for s in sent]
    carried = None
    for c in range(chunks):
        carried = beamform_chunk(arrived[c], carried, c == chunks - 1)
    powers = carried

    received = lax.all_to_all(powers, "dish", 0, 0, tiled=True)
    return received.reshape(block_width, grid_len)


def solution(mesh):
    placed = (P("freq", "dish", None, None), P("freq", "dish", None, None), P(), P())
    return jax.shard_map(
        body, mesh=mesh, in_specs=placed, out_specs=P("freq", "dish"), check_vma=False
    )
```

```python
import functools
import math

import jax
import jax.numpy as jnp
import ml_dtypes
import numpy as np
from jax import lax
from jax.experimental import pallas as pl
from jax.experimental.pallas import tpu as pltpu
from jax.sharding import PartitionSpec as P

NCHAN = 8192
CHA = 64
CHB = 128
TAPS = 4
FRAMES = 16


full_turn = 2.0 * math.pi


def table_constant(row_count, col_count, modulus, scaling):
    rows = np.arange(row_count, dtype=np.int64)[:, None]
    cols = np.arange(col_count, dtype=np.int64)[None, :]
    angles = np.float32(full_turn / modulus) * (rows * cols % modulus).astype(np.float32)
    cosine = (np.cos(angles.astype(np.float64)) * scaling).astype(ml_dtypes.bfloat16)
    sine = (np.sin(angles.astype(np.float64)) * scaling).astype(ml_dtypes.bfloat16)
    return cosine, sine


def window_constant():
    sample_index = np.arange(TAPS * NCHAN, dtype=np.float64)
    centred = (sample_index - TAPS * NCHAN / 2 + 0.5) / NCHAN
    taper_curve = 0.5 - 0.5 * np.cos(full_turn * (sample_index + 0.5) / (TAPS * NCHAN))
    shaped_window = (np.sinc(centred) * taper_curve).reshape(TAPS, NCHAN)
    energy = np.mean(np.sum(shaped_window * shaped_window, axis=0))
    return (shaped_window / np.sqrt(energy)).astype(np.float32)


def rotation_constant(row_count, col_count, modulus):
    rows = np.arange(row_count, dtype=np.int64)[:, None]
    cols = np.arange(col_count, dtype=np.int64)[None, :]
    angles = np.float32(-(full_turn / modulus)) * (rows * cols % modulus).astype(np.float32)
    angles = angles.astype(np.float64)
    return np.cos(angles).astype(np.float32), np.sin(angles).astype(np.float32)


def fourier_table(row_index, col_index, modulus, scaling):
    phases = row_index[:, None] * col_index[None, :] % modulus
    angles = full_turn / modulus * phases.astype(jnp.float32)
    cosine_table = (jnp.cos(angles) * scaling).astype(jnp.bfloat16)
    sine_table = (jnp.sin(angles) * scaling).astype(jnp.bfloat16)
    upper_rows = jnp.stack([cosine_table, -sine_table], axis=1)
    lower_rows = jnp.stack([sine_table, cosine_table], axis=1)
    return jnp.stack([upper_rows, lower_rows], axis=0)


def filter_window():
    sample_index = jnp.arange(TAPS * NCHAN, dtype=jnp.float32)
    centred = (sample_index - TAPS * NCHAN / 2 + 0.5) / NCHAN
    taper_curve = 0.5 - 0.5 * jnp.cos(full_turn * (sample_index + 0.5) / (TAPS * NCHAN))
    shaped_window = (jnp.sinc(centred) * taper_curve).reshape(TAPS, NCHAN)
    energy = jnp.mean(jnp.sum(shaped_window * shaped_window, axis=0))
    return shaped_window / jnp.sqrt(energy)


def beam_tables(grid_rows, grid_len, rows_per_device):
    positions = jnp.arange(grid_len, dtype=jnp.int32)
    cosine_base, sine_base = table_constant(grid_len, grid_len, grid_len, 1.0 / math.sqrt(grid_len))
    cosine_base = jnp.asarray(cosine_base)
    sine_base = jnp.asarray(sine_base)
    devices = grid_len // rows_per_device
    ordered_rows = jnp.transpose(
        grid_rows.reshape(grid_rows.shape[0], devices, rows_per_device), (0, 2, 1)
    ).reshape(grid_rows.shape[0], grid_len)
    picks = (positions[None, :, None] == ordered_rows[:, None, :]).astype(jnp.bfloat16)
    cosine_table = jnp.einsum(
        "jg,dgm->djm", cosine_base, picks, preferred_element_type=jnp.float32
    ).astype(jnp.bfloat16)
    sine_table = jnp.einsum(
        "jg,dgm->djm", sine_base, picks, preferred_element_type=jnp.float32
    ).astype(jnp.bfloat16)
    real_rows = jnp.concatenate([cosine_table, sine_table], axis=2)
    imag_rows = jnp.concatenate([-sine_table, cosine_table], axis=2)
    return jnp.concatenate([real_rows, imag_rows], axis=1)


def channelize_kernel(first_pair, pairs, v_ref, w_ref, t1_ref, tw_ref, t2_ref, g_ref, o_ref):
    cos_tw = tw_ref[0]
    sin_tw = tw_ref[1]
    t1 = t1_ref[...]
    t2_real = t2_ref[0]
    t2_imag = t2_ref[1]
    g_real = g_ref[0, 0]
    g_imag = g_ref[0, 1]
    half = t2_real.shape[0] // 2

    def one_frame(frame):
        acc = None
        for tap in range(TAPS):
            start = pl.multiple_of((frame - 2 * first_pair + tap) * CHA, CHA)
            piece = v_ref[0, :, pl.ds(start, CHA), :].astype(jnp.float32)
            term = w_ref[tap][None] * piece
            acc = term if acc is None else acc + term
        block = acc.astype(jnp.bfloat16).reshape(2 * CHA, CHB)
        section = jnp.dot(t1, block, preferred_element_type=jnp.float32)
        sec_real = section[:CHA]
        sec_imag = section[CHA:]
        turned_real = sec_real * cos_tw - sec_imag * sin_tw
        turned_imag = sec_real * sin_tw + sec_imag * cos_tw
        return turned_real.astype(jnp.bfloat16), turned_imag.astype(jnp.bfloat16)

    def pair(step, carry):
        first_real, first_imag = one_frame(2 * step)
        second_real, second_imag = one_frame(2 * step + 1)
        both_real = jnp.concatenate([first_real, second_real], axis=0)
        both_imag = jnp.concatenate([first_imag, second_imag], axis=0)
        dims = (((1,), (1,)), ((), ()))
        spectrum = lax.dot_general(
            t2_real, both_real, dims, preferred_element_type=jnp.float32
        ) + lax.dot_general(t2_imag, both_imag, dims, preferred_element_type=jnp.float32)
        spec_real = spectrum[:half]
        spec_imag = spectrum[half:]
        out_real = spec_real * g_real - spec_imag * g_imag
        out_imag = spec_real * g_imag + spec_imag * g_real
        lanes = pl.ds(pl.multiple_of((step - first_pair) * 2 * CHA, 2 * CHA), 2 * CHA)
        o_ref[0, 0, :, lanes] = out_real.astype(o_ref.dtype)
        o_ref[1, 0, :, lanes] = out_imag.astype(o_ref.dtype)
        return carry

    lax.fori_loop(first_pair, first_pair + pairs, pair, 0)


def beam_kernel(dish_count, carry_in, finish, *refs):
    if carry_in:
        x_ref, t_ref, c_ref, s_ref, init_ref, o_ref, acc_ref = refs
    else:
        x_ref, t_ref, c_ref, s_ref, o_ref, acc_ref = refs
    step = pl.program_id(0)
    rows = x_ref.shape[1]
    devices = x_ref.shape[2] // dish_count
    grid_len = t_ref.shape[1] // 2
    lanes = x_ref.shape[3]

    @pl.when(step == 0)
    def _():
        if carry_in:
            acc_ref[...] = init_ref[...]
        else:
            acc_ref[...] = jnp.zeros_like(acc_ref)

    parts = []
    for d in range(dish_count):
        block = x_ref[:, :, pl.ds(d * devices, devices), :].reshape(2 * rows * devices, lanes)
        sums = jnp.dot(t_ref[d], block, preferred_element_type=jnp.float32)
        sum_real = sums[:grid_len]
        sum_imag = sums[grid_len:]
        cos_d = c_ref[d]
        sin_d = s_ref[d]
        part_real = sum_real * cos_d - sum_imag * sin_d
        part_imag = sum_real * sin_d + sum_imag * cos_d
        parts.append(
            (
                part_real.astype(jnp.bfloat16).astype(jnp.float32),
                part_imag.astype(jnp.bfloat16).astype(jnp.float32),
            )
        )
    (a_re, a_im), (b_re, b_im), (c_re, c_im), (d_re, d_im) = parts
    beams = [
        (a_re + b_re + c_re + d_re, a_im + b_im + c_im + d_im),
        (a_re + b_im - c_re - d_im, a_im - b_re - c_im + d_re),
        (a_re - b_re + c_re - d_re, a_im - b_im + c_im - d_im),
        (a_re - b_im - c_re + d_im, a_im + b_re - c_im - d_re),
    ]
    for q in range(dish_count):
        beam_real, beam_imag = beams[q]
        acc_ref[q] += beam_real * beam_real + beam_imag * beam_imag

    @pl.when(step == pl.num_programs(0) - 1)
    def _():
        if not finish:
            o_ref[...] = acc_ref[...]
            return
        reversal = [
            int(format(s, "0%db" % (dish_count.bit_length() - 1))[::-1], 2)
            for s in range(dish_count)
        ]
        width = o_ref.shape[1]
        for s in range(dish_count):
            total = acc_ref[reversal[s]]
            total = total + pltpu.roll(total, width, 1)
            flipped = jnp.transpose(total, (1, 0))
            o_ref[s] = flipped[:width] * (0.25 / FRAMES)


def body(voltages, feed_gains, block_assign, grid_rows):
    dish_rows = voltages.shape[0]
    block_count = lax.axis_size("freq")
    dish_count = lax.axis_size("dish")
    block_width = NCHAN // block_count
    quarter = block_width // dish_count
    dests = block_count * dish_count
    grid_len = dish_rows * block_count
    total_dishes = grid_len * dish_count
    samples = voltages.shape[-1]

    dest = jnp.arange(dests, dtype=jnp.int32)
    dest_quarter = dest // block_count
    dest_block = jnp.take(block_assign, dest % block_count)
    dest_e = dest_block * dish_count + dest_quarter

    window = jnp.asarray(window_constant().reshape(TAPS, CHA, CHB))
    first_cos, first_sin = table_constant(CHA, CHA, CHA, 1.0 / math.sqrt(CHA))
    first_table = np.block([[first_cos, first_sin], [-first_sin, first_cos]])
    first_table = jnp.asarray(first_table)
    twiddle = jnp.asarray(np.stack(rotation_constant(CHA, CHB, NCHAN), axis=0))
    second_cos, second_sin = table_constant(CHB, CHB, CHB, 1.0 / math.sqrt(CHB))
    second_table = np.stack(
        [np.stack([second_cos, -second_sin], axis=0), np.stack([second_sin, second_cos], axis=0)],
        axis=0,
    )
    second_table = jnp.take(jnp.asarray(second_table), dest_e, axis=2).reshape(2, 2 * dests, CHB)
    gains = feed_gains[:, 0].reshape(dish_rows, 2, CHB, CHA).astype(jnp.float32)
    gains = jnp.take(gains, dest_e, axis=2)
    gains = jnp.concatenate([gains, gains], axis=3)

    chunks = 2
    pairs = FRAMES // 2 // chunks
    chunk_lanes = pairs * 2 * quarter
    tables = beam_tables(grid_rows, grid_len, dish_rows)
    feed_index = jnp.arange(dish_count, dtype=jnp.int32)
    positions = jnp.arange(grid_len, dtype=jnp.int32)
    twist_cos, twist_sin = rotation_constant(dish_count, grid_len, total_dishes)
    twist_cos = jnp.asarray(twist_cos[:, :, None])
    twist_sin = jnp.asarray(twist_sin[:, :, None])
    lane_block = 2 * quarter

    span = (2 * pairs + TAPS - 1) * CHA

    def channelize_chunk(chunk):
        first = chunk * 2 * pairs * NCHAN
        volts = voltages[:, 0, :, first : first + span * CHB].reshape(dish_rows, 2, span, CHB)
        return pl.pallas_call(
            functools.partial(channelize_kernel, chunk * pairs, pairs),
            grid=(dish_rows,),
            in_specs=[
                pl.BlockSpec((1, 2, span, CHB), lambda r: (r, 0, 0, 0)),
                pl.BlockSpec((TAPS, CHA, CHB), lambda r: (0, 0, 0)),
                pl.BlockSpec((2 * CHA, 2 * CHA), lambda r: (0, 0)),
                pl.BlockSpec((2, CHA, CHB), lambda r: (0, 0, 0)),
                pl.BlockSpec((2, 2 * dests, CHB), lambda r: (0, 0, 0)),
                pl.BlockSpec((1, 2, dests, 2 * CHA), lambda r: (r, 0, 0, 0)),
            ],
            out_specs=pl.BlockSpec((2, 1, dests, chunk_lanes), lambda r: (0, r, 0, 0)),
            out_shape=jax.ShapeDtypeStruct((2, dish_rows, dests, chunk_lanes), jnp.bfloat16),
            cost_estimate=pl.CostEstimate(
                flops=int(dish_rows * pairs * 2 * 2 * 128 * 128 * 128 * 3),
                bytes_accessed=int(voltages.size * 2 + 2 * dish_rows * dests * chunk_lanes * 2),
                transcendentals=0,
            ),
        )(volts, window, first_table, twiddle, second_table, gains)

    def beamform_chunk(received, carried, finish):
        carry_in = carried is not None
        in_specs = [
            pl.BlockSpec((2, dish_rows, dests, lane_block), lambda f: (0, 0, 0, f)),
            pl.BlockSpec((dish_count, 2 * grid_len, 2 * grid_len), lambda f: (0, 0, 0)),
            pl.BlockSpec((dish_count, grid_len, 1), lambda f: (0, 0, 0)),
            pl.BlockSpec((dish_count, grid_len, 1), lambda f: (0, 0, 0)),
        ]
        operands = [received, tables, twist_cos, twist_sin]
        if carry_in:
            in_specs.append(pl.BlockSpec((dish_count, grid_len, lane_block), lambda f: (0, 0, 0)))
            operands.append(carried)
        if finish:
            out_shape = (dish_count, quarter, grid_len)
        else:
            out_shape = (dish_count, grid_len, lane_block)
        return pl.pallas_call(
            functools.partial(beam_kernel, dish_count, carry_in, finish),
            grid=(chunk_lanes // lane_block,),
            in_specs=in_specs,
            out_specs=pl.BlockSpec(out_shape, lambda f: (0, 0, 0)),
            out_shape=jax.ShapeDtypeStruct(out_shape, jnp.float32),
            scratch_shapes=[pltpu.VMEM((dish_count, grid_len, lane_block), jnp.float32)],
            cost_estimate=pl.CostEstimate(
                flops=int(dish_count * 2 * 512 * 512 * chunk_lanes),
                bytes_accessed=int(received.size * 2 + tables.size * 2),
                transcendentals=0,
            ),
        )(*operands)

    sent = [channelize_chunk(c) for c in range(chunks)]
    arrived = [lax.all_to_all(s, ("dish", "freq"), 2, 2, tiled=True) for s in sent]
    carried = None
    for c in range(chunks):
        carried = beamform_chunk(arrived[c], carried, c == chunks - 1)
    powers = carried

    me = lax.axis_index("dish")
    pieces = [lax.dynamic_index_in_dim(powers, me, 0, keepdims=False)]
    for shift in range(1, dish_count):
        outgoing = lax.dynamic_index_in_dim(powers, me ^ shift, 0, keepdims=False)
        pairs_list = [(i, i ^ shift) for i in range(dish_count)]
        pieces.append(lax.ppermute(outgoing, "dish", pairs_list))
    stacked = jnp.stack(pieces, axis=0)
    order = jnp.arange(dish_count, dtype=jnp.int32) ^ me
    received = jnp.take(stacked, order, axis=0)
    return received.reshape(block_width, grid_len)


def solution(mesh):
    placed = (P("freq", "dish", None, None), P("freq", "dish", None, None), P(), P())
    return jax.shard_map(
        body, mesh=mesh, in_specs=placed, out_specs=P("freq", "dish"), check_vma=False
    )
```

```python
import functools
import math

import jax
import jax.numpy as jnp
import ml_dtypes
import numpy as np
from jax import lax
from jax.experimental import pallas as pl
from jax.experimental.pallas import tpu as pltpu
from jax.sharding import PartitionSpec as P

NCHAN = 8192
CHA = 64
CHB = 128
TAPS = 4
FRAMES = 16


full_turn = 2.0 * math.pi


def table_constant(row_count, col_count, modulus, scaling):
    rows = np.arange(row_count, dtype=np.int64)[:, None]
    cols = np.arange(col_count, dtype=np.int64)[None, :]
    angles = np.float32(full_turn / modulus) * (rows * cols % modulus).astype(np.float32)
    cosine = (np.cos(angles.astype(np.float64)) * scaling).astype(ml_dtypes.bfloat16)
    sine = (np.sin(angles.astype(np.float64)) * scaling).astype(ml_dtypes.bfloat16)
    return cosine, sine


def window_constant():
    sample_index = np.arange(TAPS * NCHAN, dtype=np.float64)
    centred = (sample_index - TAPS * NCHAN / 2 + 0.5) / NCHAN
    taper_curve = 0.5 - 0.5 * np.cos(full_turn * (sample_index + 0.5) / (TAPS * NCHAN))
    shaped_window = (np.sinc(centred) * taper_curve).reshape(TAPS, NCHAN)
    energy = np.mean(np.sum(shaped_window * shaped_window, axis=0))
    return (shaped_window / np.sqrt(energy)).astype(np.float32)


def rotation_constant(row_count, col_count, modulus):
    rows = np.arange(row_count, dtype=np.int64)[:, None]
    cols = np.arange(col_count, dtype=np.int64)[None, :]
    angles = np.float32(-(full_turn / modulus)) * (rows * cols % modulus).astype(np.float32)
    angles = angles.astype(np.float64)
    return np.cos(angles).astype(np.float32), np.sin(angles).astype(np.float32)


def fourier_table(row_index, col_index, modulus, scaling):
    phases = row_index[:, None] * col_index[None, :] % modulus
    angles = full_turn / modulus * phases.astype(jnp.float32)
    cosine_table = (jnp.cos(angles) * scaling).astype(jnp.bfloat16)
    sine_table = (jnp.sin(angles) * scaling).astype(jnp.bfloat16)
    upper_rows = jnp.stack([cosine_table, -sine_table], axis=1)
    lower_rows = jnp.stack([sine_table, cosine_table], axis=1)
    return jnp.stack([upper_rows, lower_rows], axis=0)


def filter_window():
    sample_index = jnp.arange(TAPS * NCHAN, dtype=jnp.float32)
    centred = (sample_index - TAPS * NCHAN / 2 + 0.5) / NCHAN
    taper_curve = 0.5 - 0.5 * jnp.cos(full_turn * (sample_index + 0.5) / (TAPS * NCHAN))
    shaped_window = (jnp.sinc(centred) * taper_curve).reshape(TAPS, NCHAN)
    energy = jnp.mean(jnp.sum(shaped_window * shaped_window, axis=0))
    return shaped_window / jnp.sqrt(energy)


def beam_tables(grid_rows, grid_len, rows_per_device):
    positions = jnp.arange(grid_len, dtype=jnp.int32)
    cosine_base, sine_base = table_constant(grid_len, grid_len, grid_len, 1.0 / math.sqrt(grid_len))
    cosine_base = jnp.asarray(cosine_base)
    sine_base = jnp.asarray(sine_base)
    devices = grid_len // rows_per_device
    ordered_rows = jnp.transpose(
        grid_rows.reshape(grid_rows.shape[0], devices, rows_per_device), (0, 2, 1)
    ).reshape(grid_rows.shape[0], grid_len)
    picks = (positions[None, :, None] == ordered_rows[:, None, :]).astype(jnp.bfloat16)
    cosine_table = jnp.einsum(
        "jg,dgm->djm", cosine_base, picks, preferred_element_type=jnp.float32
    ).astype(jnp.bfloat16)
    sine_table = jnp.einsum(
        "jg,dgm->djm", sine_base, picks, preferred_element_type=jnp.float32
    ).astype(jnp.bfloat16)
    real_rows = jnp.concatenate([cosine_table, sine_table], axis=2)
    imag_rows = jnp.concatenate([-sine_table, cosine_table], axis=2)
    return jnp.concatenate([real_rows, imag_rows], axis=1)


def channelize_kernel(first_pair, pairs, v_ref, w_ref, t1_ref, tw_ref, t2_ref, g_ref, o_ref):
    cos_tw = tw_ref[0]
    sin_tw = tw_ref[1]
    t1 = t1_ref[...]
    t2_real = t2_ref[0]
    t2_imag = t2_ref[1]
    g_real = g_ref[0, 0]
    g_imag = g_ref[0, 1]
    half = t2_real.shape[0] // 2

    def one_frame(frame):
        acc = None
        for tap in range(TAPS):
            start = pl.multiple_of((frame + tap) * CHA, CHA)
            piece = v_ref[0, :, pl.ds(start, CHA), :].astype(jnp.float32)
            term = w_ref[tap][None] * piece
            acc = term if acc is None else acc + term
        block = acc.astype(jnp.bfloat16).reshape(2 * CHA, CHB)
        section = jnp.dot(t1, block, preferred_element_type=jnp.float32)
        sec_real = section[:CHA]
        sec_imag = section[CHA:]
        turned_real = sec_real * cos_tw - sec_imag * sin_tw
        turned_imag = sec_real * sin_tw + sec_imag * cos_tw
        return turned_real.astype(jnp.bfloat16), turned_imag.astype(jnp.bfloat16)

    def pair(step, carry):
        first_real, first_imag = one_frame(2 * step)
        second_real, second_imag = one_frame(2 * step + 1)
        both_real = jnp.concatenate([first_real, second_real], axis=0)
        both_imag = jnp.concatenate([first_imag, second_imag], axis=0)
        dims = (((1,), (1,)), ((), ()))
        spectrum = lax.dot_general(
            t2_real, both_real, dims, preferred_element_type=jnp.float32
        ) + lax.dot_general(t2_imag, both_imag, dims, preferred_element_type=jnp.float32)
        spec_real = spectrum[:half]
        spec_imag = spectrum[half:]
        out_real = spec_real * g_real - spec_imag * g_imag
        out_imag = spec_real * g_imag + spec_imag * g_real
        lanes = pl.ds(pl.multiple_of((step - first_pair) * 2 * CHA, 2 * CHA), 2 * CHA)
        o_ref[0, 0, :, lanes] = out_real.astype(o_ref.dtype)
        o_ref[1, 0, :, lanes] = out_imag.astype(o_ref.dtype)
        return carry

    lax.fori_loop(first_pair, first_pair + pairs, pair, 0)


def beam_kernel(dish_count, carry_in, finish, *refs):
    if carry_in:
        x_ref, t_ref, c_ref, s_ref, init_ref, o_ref, acc_ref = refs
    else:
        x_ref, t_ref, c_ref, s_ref, o_ref, acc_ref = refs
    step = pl.program_id(0)
    rows = x_ref.shape[1]
    devices = x_ref.shape[2] // dish_count
    grid_len = t_ref.shape[1] // 2
    lanes = x_ref.shape[3]

    @pl.when(step == 0)
    def _():
        if carry_in:
            acc_ref[...] = init_ref[...]
        else:
            acc_ref[...] = jnp.zeros_like(acc_ref)

    parts = []
    for d in range(dish_count):
        block = x_ref[:, :, pl.ds(d * devices, devices), :].reshape(2 * rows * devices, lanes)
        sums = jnp.dot(t_ref[d], block, preferred_element_type=jnp.float32)
        sum_real = sums[:grid_len]
        sum_imag = sums[grid_len:]
        cos_d = c_ref[d]
        sin_d = s_ref[d]
        part_real = sum_real * cos_d - sum_imag * sin_d
        part_imag = sum_real * sin_d + sum_imag * cos_d
        parts.append(
            (
                part_real.astype(jnp.bfloat16).astype(jnp.float32),
                part_imag.astype(jnp.bfloat16).astype(jnp.float32),
            )
        )
    (a_re, a_im), (b_re, b_im), (c_re, c_im), (d_re, d_im) = parts
    beams = [
        (a_re + b_re + c_re + d_re, a_im + b_im + c_im + d_im),
        (a_re + b_im - c_re - d_im, a_im - b_re - c_im + d_re),
        (a_re - b_re + c_re - d_re, a_im - b_im + c_im - d_im),
        (a_re - b_im - c_re + d_im, a_im + b_re - c_im - d_re),
    ]
    for q in range(dish_count):
        beam_real, beam_imag = beams[q]
        acc_ref[q] += beam_real * beam_real + beam_imag * beam_imag

    @pl.when(step == pl.num_programs(0) - 1)
    def _():
        if not finish:
            o_ref[...] = acc_ref[...]
            return
        reversal = [
            int(format(s, "0%db" % (dish_count.bit_length() - 1))[::-1], 2)
            for s in range(dish_count)
        ]
        width = o_ref.shape[1]
        for s in range(dish_count):
            total = acc_ref[reversal[s]]
            total = total + pltpu.roll(total, width, 1)
            flipped = jnp.transpose(total, (1, 0))
            o_ref[s] = flipped[:width] * (0.25 / FRAMES)


def body(voltages, feed_gains, block_assign, grid_rows):
    dish_rows = voltages.shape[0]
    block_count = lax.axis_size("freq")
    dish_count = lax.axis_size("dish")
    block_width = NCHAN // block_count
    quarter = block_width // dish_count
    dests = block_count * dish_count
    grid_len = dish_rows * block_count
    total_dishes = grid_len * dish_count
    samples = voltages.shape[-1]

    dest = jnp.arange(dests, dtype=jnp.int32)
    dest_quarter = dest // block_count
    dest_block = jnp.take(block_assign, dest % block_count)
    dest_e = dest_block * dish_count + dest_quarter

    window = jnp.asarray(window_constant().reshape(TAPS, CHA, CHB))
    first_cos, first_sin = table_constant(CHA, CHA, CHA, 1.0 / math.sqrt(CHA))
    first_table = np.block([[first_cos, first_sin], [-first_sin, first_cos]])
    first_table = jnp.asarray(first_table)
    twiddle = jnp.asarray(np.stack(rotation_constant(CHA, CHB, NCHAN), axis=0))
    second_cos, second_sin = table_constant(CHB, CHB, CHB, 1.0 / math.sqrt(CHB))
    second_table = np.stack(
        [np.stack([second_cos, -second_sin], axis=0), np.stack([second_sin, second_cos], axis=0)],
        axis=0,
    )
    second_table = jnp.take(jnp.asarray(second_table), dest_e, axis=2).reshape(2, 2 * dests, CHB)
    gains = feed_gains[:, 0].reshape(dish_rows, 2, CHB, CHA).astype(jnp.float32)
    gains = jnp.take(gains, dest_e, axis=2)
    gains = jnp.concatenate([gains, gains], axis=3)

    chunks = 2
    pairs = FRAMES // 2 // chunks
    chunk_lanes = pairs * 2 * quarter
    tables = beam_tables(grid_rows, grid_len, dish_rows)
    feed_index = jnp.arange(dish_count, dtype=jnp.int32)
    positions = jnp.arange(grid_len, dtype=jnp.int32)
    twist_cos, twist_sin = rotation_constant(dish_count, grid_len, total_dishes)
    twist_cos = jnp.asarray(twist_cos[:, :, None])
    twist_sin = jnp.asarray(twist_sin[:, :, None])
    lane_block = 2 * quarter

    volts = voltages[:, 0].reshape(dish_rows, 2, samples // CHB, CHB)

    def channelize_chunk(chunk):
        return pl.pallas_call(
            functools.partial(channelize_kernel, chunk * pairs, pairs),
            grid=(dish_rows,),
            in_specs=[
                pl.BlockSpec((1, 2, samples // CHB, CHB), lambda r: (r, 0, 0, 0)),
                pl.BlockSpec((TAPS, CHA, CHB), lambda r: (0, 0, 0)),
                pl.BlockSpec((2 * CHA, 2 * CHA), lambda r: (0, 0)),
                pl.BlockSpec((2, CHA, CHB), lambda r: (0, 0, 0)),
                pl.BlockSpec((2, 2 * dests, CHB), lambda r: (0, 0, 0)),
                pl.BlockSpec((1, 2, dests, 2 * CHA), lambda r: (r, 0, 0, 0)),
            ],
            out_specs=pl.BlockSpec((2, 1, dests, chunk_lanes), lambda r: (0, r, 0, 0)),
            out_shape=jax.ShapeDtypeStruct((2, dish_rows, dests, chunk_lanes), jnp.bfloat16),
            cost_estimate=pl.CostEstimate(
                flops=int(dish_rows * pairs * 2 * 2 * 128 * 128 * 128 * 3),
                bytes_accessed=int(voltages.size * 2 + 2 * dish_rows * dests * chunk_lanes * 2),
                transcendentals=0,
            ),
        )(volts, window, first_table, twiddle, second_table, gains)

    def beamform_chunk(received, carried, finish):
        carry_in = carried is not None
        in_specs = [
            pl.BlockSpec((2, dish_rows, dests, lane_block), lambda f: (0, 0, 0, f)),
            pl.BlockSpec((dish_count, 2 * grid_len, 2 * grid_len), lambda f: (0, 0, 0)),
            pl.BlockSpec((dish_count, grid_len, 1), lambda f: (0, 0, 0)),
            pl.BlockSpec((dish_count, grid_len, 1), lambda f: (0, 0, 0)),
        ]
        operands = [received, tables, twist_cos, twist_sin]
        if carry_in:
            in_specs.append(pl.BlockSpec((dish_count, grid_len, lane_block), lambda f: (0, 0, 0)))
            operands.append(carried)
        if finish:
            out_shape = (dish_count, quarter, grid_len)
        else:
            out_shape = (dish_count, grid_len, lane_block)
        return pl.pallas_call(
            functools.partial(beam_kernel, dish_count, carry_in, finish),
            grid=(chunk_lanes // lane_block,),
            in_specs=in_specs,
            out_specs=pl.BlockSpec(out_shape, lambda f: (0, 0, 0)),
            out_shape=jax.ShapeDtypeStruct(out_shape, jnp.float32),
            scratch_shapes=[pltpu.VMEM((dish_count, grid_len, lane_block), jnp.float32)],
            cost_estimate=pl.CostEstimate(
                flops=int(dish_count * 2 * 512 * 512 * chunk_lanes),
                bytes_accessed=int(received.size * 2 + tables.size * 2),
                transcendentals=0,
            ),
        )(*operands)

    sent = [channelize_chunk(c) for c in range(chunks)]
    arrived = [lax.all_to_all(s, ("dish", "freq"), 2, 2, tiled=True) for s in sent]
    carried = None
    for c in range(chunks):
        carried = beamform_chunk(arrived[c], carried, c == chunks - 1)
    powers = carried

    me = lax.axis_index("dish")
    pieces = [lax.dynamic_index_in_dim(powers, me, 0, keepdims=False)]
    for shift in range(1, dish_count):
        outgoing = lax.dynamic_index_in_dim(powers, me ^ shift, 0, keepdims=False)
        pairs_list = [(i, i ^ shift) for i in range(dish_count)]
        pieces.append(lax.ppermute(outgoing, "dish", pairs_list))
    stacked = jnp.stack(pieces, axis=0)
    order = jnp.arange(dish_count, dtype=jnp.int32) ^ me
    received = jnp.take(stacked, order, axis=0)
    return received.reshape(block_width, grid_len)


def solution(mesh):
    placed = (P("freq", "dish", None, None), P("freq", "dish", None, None), P(), P())
    return jax.shard_map(
        body, mesh=mesh, in_specs=placed, out_specs=P("freq", "dish"), check_vma=False
    )
```

```python
import functools
import math

import jax
import jax.numpy as jnp
import ml_dtypes
import numpy as np
from jax import lax
from jax.experimental import pallas as pl
from jax.experimental.pallas import tpu as pltpu
from jax.sharding import PartitionSpec as P

NCHAN = 8192
CHA = 64
CHB = 128
TAPS = 4
FRAMES = 16


full_turn = 2.0 * math.pi


def table_constant(row_count, col_count, modulus, scaling):
    rows = np.arange(row_count, dtype=np.int64)[:, None]
    cols = np.arange(col_count, dtype=np.int64)[None, :]
    angles = np.float32(full_turn / modulus) * (rows * cols % modulus).astype(np.float32)
    cosine = (np.cos(angles.astype(np.float64)) * scaling).astype(ml_dtypes.bfloat16)
    sine = (np.sin(angles.astype(np.float64)) * scaling).astype(ml_dtypes.bfloat16)
    return cosine, sine


def window_constant():
    sample_index = np.arange(TAPS * NCHAN, dtype=np.float64)
    centred = (sample_index - TAPS * NCHAN / 2 + 0.5) / NCHAN
    taper_curve = 0.5 - 0.5 * np.cos(full_turn * (sample_index + 0.5) / (TAPS * NCHAN))
    shaped_window = (np.sinc(centred) * taper_curve).reshape(TAPS, NCHAN)
    energy = np.mean(np.sum(shaped_window * shaped_window, axis=0))
    return (shaped_window / np.sqrt(energy)).astype(np.float32)


def rotation_constant(row_count, col_count, modulus):
    rows = np.arange(row_count, dtype=np.int64)[:, None]
    cols = np.arange(col_count, dtype=np.int64)[None, :]
    angles = np.float32(-(full_turn / modulus)) * (rows * cols % modulus).astype(np.float32)
    angles = angles.astype(np.float64)
    return np.cos(angles).astype(np.float32), np.sin(angles).astype(np.float32)


def fourier_table(row_index, col_index, modulus, scaling):
    phases = row_index[:, None] * col_index[None, :] % modulus
    angles = full_turn / modulus * phases.astype(jnp.float32)
    cosine_table = (jnp.cos(angles) * scaling).astype(jnp.bfloat16)
    sine_table = (jnp.sin(angles) * scaling).astype(jnp.bfloat16)
    upper_rows = jnp.stack([cosine_table, -sine_table], axis=1)
    lower_rows = jnp.stack([sine_table, cosine_table], axis=1)
    return jnp.stack([upper_rows, lower_rows], axis=0)


def filter_window():
    sample_index = jnp.arange(TAPS * NCHAN, dtype=jnp.float32)
    centred = (sample_index - TAPS * NCHAN / 2 + 0.5) / NCHAN
    taper_curve = 0.5 - 0.5 * jnp.cos(full_turn * (sample_index + 0.5) / (TAPS * NCHAN))
    shaped_window = (jnp.sinc(centred) * taper_curve).reshape(TAPS, NCHAN)
    energy = jnp.mean(jnp.sum(shaped_window * shaped_window, axis=0))
    return shaped_window / jnp.sqrt(energy)


def beam_tables(grid_rows, grid_len, rows_per_device):
    positions = jnp.arange(grid_len, dtype=jnp.int32)
    cosine_base, sine_base = table_constant(grid_len, grid_len, grid_len, 1.0 / math.sqrt(grid_len))
    cosine_base = jnp.asarray(cosine_base)
    sine_base = jnp.asarray(sine_base)
    devices = grid_len // rows_per_device
    ordered_rows = jnp.transpose(
        grid_rows.reshape(grid_rows.shape[0], devices, rows_per_device), (0, 2, 1)
    ).reshape(grid_rows.shape[0], grid_len)
    picks = (positions[None, :, None] == ordered_rows[:, None, :]).astype(jnp.bfloat16)
    cosine_table = jnp.einsum(
        "jg,dgm->djm", cosine_base, picks, preferred_element_type=jnp.float32
    ).astype(jnp.bfloat16)
    sine_table = jnp.einsum(
        "jg,dgm->djm", sine_base, picks, preferred_element_type=jnp.float32
    ).astype(jnp.bfloat16)
    real_rows = jnp.concatenate([cosine_table, sine_table], axis=2)
    imag_rows = jnp.concatenate([-sine_table, cosine_table], axis=2)
    return jnp.concatenate([real_rows, imag_rows], axis=1)


def channelize_kernel(first_pair, pairs, v_ref, w_ref, t1_ref, tw_ref, t2_ref, g_ref, o_ref):
    cos_tw = tw_ref[0]
    sin_tw = tw_ref[1]
    t1 = t1_ref[...]
    t2_real = t2_ref[0]
    t2_imag = t2_ref[1]
    g_real = g_ref[0, 0]
    g_imag = g_ref[0, 1]
    half = t2_real.shape[0] // 2

    def one_frame(frame):
        acc = None
        for tap in range(TAPS):
            start = pl.multiple_of((frame + tap) * CHA, CHA)
            piece = v_ref[0, :, pl.ds(start, CHA), :].astype(jnp.float32)
            term = w_ref[tap][None] * piece
            acc = term if acc is None else acc + term
        block = acc.astype(jnp.bfloat16).reshape(2 * CHA, CHB)
        section = jnp.dot(t1, block, preferred_element_type=jnp.float32)
        sec_real = section[:CHA]
        sec_imag = section[CHA:]
        turned_real = sec_real * cos_tw - sec_imag * sin_tw
        turned_imag = sec_real * sin_tw + sec_imag * cos_tw
        return turned_real.astype(jnp.bfloat16), turned_imag.astype(jnp.bfloat16)

    def pair(step, carry):
        first_real, first_imag = one_frame(2 * step)
        second_real, second_imag = one_frame(2 * step + 1)
        both_real = jnp.concatenate([first_real, second_real], axis=0)
        both_imag = jnp.concatenate([first_imag, second_imag], axis=0)
        dims = (((1,), (1,)), ((), ()))
        spectrum = lax.dot_general(
            t2_real, both_real, dims, preferred_element_type=jnp.float32
        ) + lax.dot_general(t2_imag, both_imag, dims, preferred_element_type=jnp.float32)
        spec_real = spectrum[:half]
        spec_imag = spectrum[half:]
        out_real = spec_real * g_real - spec_imag * g_imag
        out_imag = spec_real * g_imag + spec_imag * g_real
        lanes = pl.ds(pl.multiple_of((step - first_pair) * 2 * CHA, 2 * CHA), 2 * CHA)
        o_ref[0, 0, :, lanes] = out_real.astype(o_ref.dtype)
        o_ref[1, 0, :, lanes] = out_imag.astype(o_ref.dtype)
        return carry

    lax.fori_loop(first_pair, first_pair + pairs, pair, 0)


def beam_kernel(dish_count, carry_in, finish, *refs):
    if carry_in:
        x_ref, t_ref, c_ref, s_ref, init_ref, o_ref, acc_ref = refs
    else:
        x_ref, t_ref, c_ref, s_ref, o_ref, acc_ref = refs
    step = pl.program_id(0)
    rows = x_ref.shape[1]
    devices = x_ref.shape[2] // dish_count
    grid_len = t_ref.shape[1] // 2
    lanes = x_ref.shape[3]

    @pl.when(step == 0)
    def _():
        if carry_in:
            acc_ref[...] = init_ref[...]
        else:
            acc_ref[...] = jnp.zeros_like(acc_ref)

    parts = []
    for d in range(dish_count):
        block = x_ref[:, :, pl.ds(d * devices, devices), :].reshape(2 * rows * devices, lanes)
        sums = jnp.dot(t_ref[d], block, preferred_element_type=jnp.float32)
        sum_real = sums[:grid_len]
        sum_imag = sums[grid_len:]
        cos_d = c_ref[d]
        sin_d = s_ref[d]
        part_real = sum_real * cos_d - sum_imag * sin_d
        part_imag = sum_real * sin_d + sum_imag * cos_d
        parts.append(
            (
                part_real.astype(jnp.bfloat16).astype(jnp.float32),
                part_imag.astype(jnp.bfloat16).astype(jnp.float32),
            )
        )
    (a_re, a_im), (b_re, b_im), (c_re, c_im), (d_re, d_im) = parts
    beams = [
        (a_re + b_re + c_re + d_re, a_im + b_im + c_im + d_im),
        (a_re + b_im - c_re - d_im, a_im - b_re - c_im + d_re),
        (a_re - b_re + c_re - d_re, a_im - b_im + c_im - d_im),
        (a_re - b_im - c_re + d_im, a_im + b_re - c_im - d_re),
    ]
    for q in range(dish_count):
        beam_real, beam_imag = beams[q]
        acc_ref[q] += beam_real * beam_real + beam_imag * beam_imag

    @pl.when(step == pl.num_programs(0) - 1)
    def _():
        if not finish:
            o_ref[...] = acc_ref[...]
            return
        reversal = [
            int(format(s, "0%db" % (dish_count.bit_length() - 1))[::-1], 2)
            for s in range(dish_count)
        ]
        width = o_ref.shape[1]
        for s in range(dish_count):
            total = acc_ref[reversal[s]]
            total = total + pltpu.roll(total, width, 1)
            flipped = jnp.transpose(total, (1, 0))
            o_ref[s] = flipped[:width] * (0.25 / FRAMES)


def body(voltages, feed_gains, block_assign, grid_rows):
    dish_rows = voltages.shape[0]
    block_count = lax.axis_size("freq")
    dish_count = lax.axis_size("dish")
    block_width = NCHAN // block_count
    quarter = block_width // dish_count
    dests = block_count * dish_count
    grid_len = dish_rows * block_count
    total_dishes = grid_len * dish_count
    samples = voltages.shape[-1]

    dest = jnp.arange(dests, dtype=jnp.int32)
    dest_quarter = dest // block_count
    dest_block = jnp.take(block_assign, dest % block_count)
    dest_e = dest_block * dish_count + dest_quarter

    window = jnp.asarray(window_constant().reshape(TAPS, CHA, CHB))
    first_cos, first_sin = table_constant(CHA, CHA, CHA, 1.0 / math.sqrt(CHA))
    first_table = np.block([[first_cos, first_sin], [-first_sin, first_cos]])
    first_table = jnp.asarray(first_table)
    twiddle = jnp.asarray(np.stack(rotation_constant(CHA, CHB, NCHAN), axis=0))
    second_cos, second_sin = table_constant(CHB, CHB, CHB, 1.0 / math.sqrt(CHB))
    second_table = np.stack(
        [np.stack([second_cos, -second_sin], axis=0), np.stack([second_sin, second_cos], axis=0)],
        axis=0,
    )
    second_table = jnp.take(jnp.asarray(second_table), dest_e, axis=2).reshape(2, 2 * dests, CHB)
    gains = feed_gains[:, 0].reshape(dish_rows, 2, CHB, CHA).astype(jnp.float32)
    gains = jnp.take(gains, dest_e, axis=2)
    gains = jnp.concatenate([gains, gains], axis=3)

    chunk_pairs = [2, 3, 3]
    chunk_starts = [sum(chunk_pairs[:c]) for c in range(len(chunk_pairs))]
    tables = beam_tables(grid_rows, grid_len, dish_rows)
    feed_index = jnp.arange(dish_count, dtype=jnp.int32)
    positions = jnp.arange(grid_len, dtype=jnp.int32)
    twist_cos, twist_sin = rotation_constant(dish_count, grid_len, total_dishes)
    twist_cos = jnp.asarray(twist_cos[:, :, None])
    twist_sin = jnp.asarray(twist_sin[:, :, None])
    lane_block = 2 * quarter

    volts = voltages[:, 0].reshape(dish_rows, 2, samples // CHB, CHB)

    def channelize_chunk(chunk):
        pairs = chunk_pairs[chunk]
        chunk_lanes = pairs * 2 * quarter
        return pl.pallas_call(
            functools.partial(channelize_kernel, chunk_starts[chunk], pairs),
            grid=(dish_rows,),
            in_specs=[
                pl.BlockSpec((1, 2, samples // CHB, CHB), lambda r: (r, 0, 0, 0)),
                pl.BlockSpec((TAPS, CHA, CHB), lambda r: (0, 0, 0)),
                pl.BlockSpec((2 * CHA, 2 * CHA), lambda r: (0, 0)),
                pl.BlockSpec((2, CHA, CHB), lambda r: (0, 0, 0)),
                pl.BlockSpec((2, 2 * dests, CHB), lambda r: (0, 0, 0)),
                pl.BlockSpec((1, 2, dests, 2 * CHA), lambda r: (r, 0, 0, 0)),
            ],
            out_specs=pl.BlockSpec((2, 1, dests, chunk_lanes), lambda r: (0, r, 0, 0)),
            out_shape=jax.ShapeDtypeStruct((2, dish_rows, dests, chunk_lanes), jnp.bfloat16),
            cost_estimate=pl.CostEstimate(
                flops=int(dish_rows * pairs * 2 * 2 * 128 * 128 * 128 * 3),
                bytes_accessed=int(voltages.size * 2 + 2 * dish_rows * dests * chunk_lanes * 2),
                transcendentals=0,
            ),
        )(volts, window, first_table, twiddle, second_table, gains)

    def beamform_chunk(received, carried, finish):
        carry_in = carried is not None
        chunk_lanes = received.shape[3]
        in_specs = [
            pl.BlockSpec((2, dish_rows, dests, lane_block), lambda f: (0, 0, 0, f)),
            pl.BlockSpec((dish_count, 2 * grid_len, 2 * grid_len), lambda f: (0, 0, 0)),
            pl.BlockSpec((dish_count, grid_len, 1), lambda f: (0, 0, 0)),
            pl.BlockSpec((dish_count, grid_len, 1), lambda f: (0, 0, 0)),
        ]
        operands = [received, tables, twist_cos, twist_sin]
        if carry_in:
            in_specs.append(pl.BlockSpec((dish_count, grid_len, lane_block), lambda f: (0, 0, 0)))
            operands.append(carried)
        if finish:
            out_shape = (dish_count, quarter, grid_len)
        else:
            out_shape = (dish_count, grid_len, lane_block)
        return pl.pallas_call(
            functools.partial(beam_kernel, dish_count, carry_in, finish),
            grid=(chunk_lanes // lane_block,),
            in_specs=in_specs,
            out_specs=pl.BlockSpec(out_shape, lambda f: (0, 0, 0)),
            out_shape=jax.ShapeDtypeStruct(out_shape, jnp.float32),
            scratch_shapes=[pltpu.VMEM((dish_count, grid_len, lane_block), jnp.float32)],
            cost_estimate=pl.CostEstimate(
                flops=int(dish_count * 2 * 512 * 512 * chunk_lanes),
                bytes_accessed=int(received.size * 2 + tables.size * 2),
                transcendentals=0,
            ),
        )(*operands)

    chunks = len(chunk_pairs)
    sent = [channelize_chunk(c) for c in range(chunks)]
    arrived = [lax.all_to_all(s, ("dish", "freq"), 2, 2, tiled=True) for s in sent]
    carried = None
    for c in range(chunks):
        carried = beamform_chunk(arrived[c], carried, c == chunks - 1)
    powers = carried

    me = lax.axis_index("dish")
    pieces = [lax.dynamic_index_in_dim(powers, me, 0, keepdims=False)]
    for shift in range(1, dish_count):
        outgoing = lax.dynamic_index_in_dim(powers, me ^ shift, 0, keepdims=False)
        pairs_list = [(i, i ^ shift) for i in range(dish_count)]
        pieces.append(lax.ppermute(outgoing, "dish", pairs_list))
    stacked = jnp.stack(pieces, axis=0)
    order = jnp.arange(dish_count, dtype=jnp.int32) ^ me
    received = jnp.take(stacked, order, axis=0)
    return received.reshape(block_width, grid_len)


def solution(mesh):
    placed = (P("freq", "dish", None, None), P("freq", "dish", None, None), P(), P())
    return jax.shard_map(
        body, mesh=mesh, in_specs=placed, out_specs=P("freq", "dish"), check_vma=False
    )
```

```python
import functools
import math

import jax
import jax.numpy as jnp
import ml_dtypes
import numpy as np
from jax import lax
from jax.experimental import pallas as pl
from jax.experimental.pallas import tpu as pltpu
from jax.sharding import PartitionSpec as P

NCHAN = 8192
CHA = 64
CHB = 128
TAPS = 4
FRAMES = 16


full_turn = 2.0 * math.pi


def table_constant(row_count, col_count, modulus, scaling):
    rows = np.arange(row_count, dtype=np.int64)[:, None]
    cols = np.arange(col_count, dtype=np.int64)[None, :]
    angles = np.float32(full_turn / modulus) * (rows * cols % modulus).astype(np.float32)
    cosine = (np.cos(angles.astype(np.float64)) * scaling).astype(ml_dtypes.bfloat16)
    sine = (np.sin(angles.astype(np.float64)) * scaling).astype(ml_dtypes.bfloat16)
    return cosine, sine


def window_constant():
    sample_index = np.arange(TAPS * NCHAN, dtype=np.float64)
    centred = (sample_index - TAPS * NCHAN / 2 + 0.5) / NCHAN
    taper_curve = 0.5 - 0.5 * np.cos(full_turn * (sample_index + 0.5) / (TAPS * NCHAN))
    shaped_window = (np.sinc(centred) * taper_curve).reshape(TAPS, NCHAN)
    energy = np.mean(np.sum(shaped_window * shaped_window, axis=0))
    return (shaped_window / np.sqrt(energy)).astype(np.float32)


def rotation_constant(row_count, col_count, modulus):
    rows = np.arange(row_count, dtype=np.int64)[:, None]
    cols = np.arange(col_count, dtype=np.int64)[None, :]
    angles = np.float32(-(full_turn / modulus)) * (rows * cols % modulus).astype(np.float32)
    angles = angles.astype(np.float64)
    return np.cos(angles).astype(np.float32), np.sin(angles).astype(np.float32)


def fourier_table(row_index, col_index, modulus, scaling):
    phases = row_index[:, None] * col_index[None, :] % modulus
    angles = full_turn / modulus * phases.astype(jnp.float32)
    cosine_table = (jnp.cos(angles) * scaling).astype(jnp.bfloat16)
    sine_table = (jnp.sin(angles) * scaling).astype(jnp.bfloat16)
    upper_rows = jnp.stack([cosine_table, -sine_table], axis=1)
    lower_rows = jnp.stack([sine_table, cosine_table], axis=1)
    return jnp.stack([upper_rows, lower_rows], axis=0)


def filter_window():
    sample_index = jnp.arange(TAPS * NCHAN, dtype=jnp.float32)
    centred = (sample_index - TAPS * NCHAN / 2 + 0.5) / NCHAN
    taper_curve = 0.5 - 0.5 * jnp.cos(full_turn * (sample_index + 0.5) / (TAPS * NCHAN))
    shaped_window = (jnp.sinc(centred) * taper_curve).reshape(TAPS, NCHAN)
    energy = jnp.mean(jnp.sum(shaped_window * shaped_window, axis=0))
    return shaped_window / jnp.sqrt(energy)


def beam_tables(grid_rows, grid_len, rows_per_device):
    positions = jnp.arange(grid_len, dtype=jnp.int32)
    cosine_base, sine_base = table_constant(grid_len, grid_len, grid_len, 1.0 / math.sqrt(grid_len))
    cosine_base = jnp.asarray(cosine_base)
    sine_base = jnp.asarray(sine_base)
    devices = grid_len // rows_per_device
    ordered_rows = jnp.transpose(
        grid_rows.reshape(grid_rows.shape[0], devices, rows_per_device), (0, 2, 1)
    ).reshape(grid_rows.shape[0], grid_len)
    picks = (positions[None, :, None] == ordered_rows[:, None, :]).astype(jnp.bfloat16)
    cosine_table = jnp.einsum(
        "jg,dgm->djm", cosine_base, picks, preferred_element_type=jnp.float32
    ).astype(jnp.bfloat16)
    sine_table = jnp.einsum(
        "jg,dgm->djm", sine_base, picks, preferred_element_type=jnp.float32
    ).astype(jnp.bfloat16)
    real_rows = jnp.concatenate([cosine_table, sine_table], axis=2)
    imag_rows = jnp.concatenate([-sine_table, cosine_table], axis=2)
    return jnp.concatenate([real_rows, imag_rows], axis=1)


def channelize_kernel(first_pair, pairs, v_ref, w_ref, t1_ref, tw_ref, t2_ref, g_ref, o_ref):
    cos_tw = tw_ref[0]
    sin_tw = tw_ref[1]
    t1 = t1_ref[...]
    t2_real = t2_ref[0]
    t2_imag = t2_ref[1]
    g_real = g_ref[0, 0]
    g_imag = g_ref[0, 1]
    half = t2_real.shape[0] // 2

    def one_frame(frame):
        acc = None
        for tap in range(TAPS):
            start = pl.multiple_of((frame - 2 * first_pair + tap) * CHA, CHA)
            piece = v_ref[0, :, pl.ds(start, CHA), :].astype(jnp.float32)
            term = w_ref[tap][None] * piece
            acc = term if acc is None else acc + term
        block = acc.astype(jnp.bfloat16).reshape(2 * CHA, CHB)
        section = jnp.dot(t1, block, preferred_element_type=jnp.float32)
        sec_real = section[:CHA]
        sec_imag = section[CHA:]
        turned_real = sec_real * cos_tw - sec_imag * sin_tw
        turned_imag = sec_real * sin_tw + sec_imag * cos_tw
        return turned_real.astype(jnp.bfloat16), turned_imag.astype(jnp.bfloat16)

    def pair(step, carry):
        first_real, first_imag = one_frame(2 * step)
        second_real, second_imag = one_frame(2 * step + 1)
        both_real = jnp.concatenate([first_real, second_real], axis=0)
        both_imag = jnp.concatenate([first_imag, second_imag], axis=0)
        dims = (((1,), (1,)), ((), ()))
        spectrum = lax.dot_general(
            t2_real, both_real, dims, preferred_element_type=jnp.float32
        ) + lax.dot_general(t2_imag, both_imag, dims, preferred_element_type=jnp.float32)
        spec_real = spectrum[:half]
        spec_imag = spectrum[half:]
        out_real = spec_real * g_real - spec_imag * g_imag
        out_imag = spec_real * g_imag + spec_imag * g_real
        lanes = pl.ds(pl.multiple_of((step - first_pair) * 2 * CHA, 2 * CHA), 2 * CHA)
        o_ref[0, 0, :, lanes] = out_real.astype(o_ref.dtype)
        o_ref[1, 0, :, lanes] = out_imag.astype(o_ref.dtype)
        return carry

    lax.fori_loop(first_pair, first_pair + pairs, pair, 0)


def beam_kernel(dish_count, carry_in, finish, *refs):
    if carry_in:
        x_ref, t_ref, c_ref, s_ref, init_ref, o_ref, acc_ref = refs
    else:
        x_ref, t_ref, c_ref, s_ref, o_ref, acc_ref = refs
    step = pl.program_id(0)
    rows = x_ref.shape[1]
    devices = x_ref.shape[2] // dish_count
    grid_len = t_ref.shape[1] // 2
    lanes = x_ref.shape[3]

    @pl.when(step == 0)
    def _():
        if carry_in:
            acc_ref[...] = init_ref[...]
        else:
            acc_ref[...] = jnp.zeros_like(acc_ref)

    parts = []
    for d in range(dish_count):
        block = x_ref[:, :, pl.ds(d * devices, devices), :].reshape(2 * rows * devices, lanes)
        sums = jnp.dot(t_ref[d], block, preferred_element_type=jnp.float32)
        sum_real = sums[:grid_len]
        sum_imag = sums[grid_len:]
        cos_d = c_ref[d]
        sin_d = s_ref[d]
        part_real = sum_real * cos_d - sum_imag * sin_d
        part_imag = sum_real * sin_d + sum_imag * cos_d
        parts.append(
            (
                part_real.astype(jnp.bfloat16).astype(jnp.float32),
                part_imag.astype(jnp.bfloat16).astype(jnp.float32),
            )
        )
    (a_re, a_im), (b_re, b_im), (c_re, c_im), (d_re, d_im) = parts
    beams = [
        (a_re + b_re + c_re + d_re, a_im + b_im + c_im + d_im),
        (a_re + b_im - c_re - d_im, a_im - b_re - c_im + d_re),
        (a_re - b_re + c_re - d_re, a_im - b_im + c_im - d_im),
        (a_re - b_im - c_re + d_im, a_im + b_re - c_im - d_re),
    ]
    for q in range(dish_count):
        beam_real, beam_imag = beams[q]
        acc_ref[q] += beam_real * beam_real + beam_imag * beam_imag

    @pl.when(step == pl.num_programs(0) - 1)
    def _():
        if not finish:
            o_ref[...] = acc_ref[...]
            return
        reversal = [
            int(format(s, "0%db" % (dish_count.bit_length() - 1))[::-1], 2)
            for s in range(dish_count)
        ]
        width = o_ref.shape[1]
        for s in range(dish_count):
            total = acc_ref[reversal[s]]
            total = total + pltpu.roll(total, width, 1)
            flipped = jnp.transpose(total, (1, 0))
            o_ref[s] = flipped[:width] * (0.25 / FRAMES)


def body(voltages, feed_gains, block_assign, grid_rows):
    dish_rows = voltages.shape[0]
    block_count = lax.axis_size("freq")
    dish_count = lax.axis_size("dish")
    block_width = NCHAN // block_count
    quarter = block_width // dish_count
    dests = block_count * dish_count
    grid_len = dish_rows * block_count
    total_dishes = grid_len * dish_count
    samples = voltages.shape[-1]

    dest = jnp.arange(dests, dtype=jnp.int32)
    dest_quarter = dest // block_count
    dest_block = jnp.tile(block_assign, dish_count)
    dest_e = dest_block * dish_count + dest_quarter
    picks_e = (dest_e[:, None] == jnp.arange(dests, dtype=jnp.int32)[None, :]).astype(jnp.bfloat16)

    window = jnp.asarray(window_constant().reshape(TAPS, CHA, CHB))
    first_cos, first_sin = table_constant(CHA, CHA, CHA, 1.0 / math.sqrt(CHA))
    first_table = np.block([[first_cos, first_sin], [-first_sin, first_cos]])
    first_table = jnp.asarray(first_table)
    twiddle = jnp.asarray(np.stack(rotation_constant(CHA, CHB, NCHAN), axis=0))
    second_cos, second_sin = table_constant(CHB, CHB, CHB, 1.0 / math.sqrt(CHB))
    second_table = np.stack(
        [np.stack([second_cos, -second_sin], axis=0), np.stack([second_sin, second_cos], axis=0)],
        axis=0,
    )
    second_table = jnp.einsum(
        "je,qseb->qsjb", picks_e, jnp.asarray(second_table), preferred_element_type=jnp.float32
    ).astype(jnp.bfloat16).reshape(2, 2 * dests, CHB)
    gains = feed_gains[:, 0].reshape(dish_rows, 2, CHB, CHA)
    gains = jnp.einsum("je,rpec->rpjc", picks_e, gains, preferred_element_type=jnp.float32)
    gains = jnp.concatenate([gains, gains], axis=3)

    chunks = 2
    pairs = FRAMES // 2 // chunks
    chunk_lanes = pairs * 2 * quarter
    tables = beam_tables(grid_rows, grid_len, dish_rows)
    feed_index = jnp.arange(dish_count, dtype=jnp.int32)
    positions = jnp.arange(grid_len, dtype=jnp.int32)
    twist_cos, twist_sin = rotation_constant(dish_count, grid_len, total_dishes)
    twist_cos = jnp.asarray(twist_cos[:, :, None])
    twist_sin = jnp.asarray(twist_sin[:, :, None])
    lane_block = 2 * quarter

    volts = voltages[:, 0].reshape(dish_rows, 2, samples // CHB, CHB)

    span = (2 * pairs + TAPS - 1) * CHA

    def channelize_chunk(chunk):
        first_row = 2 * chunk * pairs * CHA
        return pl.pallas_call(
            functools.partial(channelize_kernel, chunk * pairs, pairs),
            grid=(dish_rows,),
            in_specs=[
                pl.BlockSpec(
                    (pl.Element(1), pl.Element(2), pl.Element(span), pl.Element(CHB)),
                    lambda r: (r, 0, first_row, 0),
                ),
                pl.BlockSpec((TAPS, CHA, CHB), lambda r: (0, 0, 0)),
                pl.BlockSpec((2 * CHA, 2 * CHA), lambda r: (0, 0)),
                pl.BlockSpec((2, CHA, CHB), lambda r: (0, 0, 0)),
                pl.BlockSpec((2, 2 * dests, CHB), lambda r: (0, 0, 0)),
                pl.BlockSpec((1, 2, dests, 2 * CHA), lambda r: (r, 0, 0, 0)),
            ],
            out_specs=pl.BlockSpec((2, 1, dests, chunk_lanes), lambda r: (0, r, 0, 0)),
            out_shape=jax.ShapeDtypeStruct((2, dish_rows, dests, chunk_lanes), jnp.bfloat16),
            cost_estimate=pl.CostEstimate(
                flops=int(dish_rows * pairs * 2 * 2 * 128 * 128 * 128 * 3),
                bytes_accessed=int(voltages.size * 2 + 2 * dish_rows * dests * chunk_lanes * 2),
                transcendentals=0,
            ),
        )(volts, window, first_table, twiddle, second_table, gains)

    def beamform_chunk(received, carried, finish):
        carry_in = carried is not None
        in_specs = [
            pl.BlockSpec((2, dish_rows, dests, lane_block), lambda f: (0, 0, 0, f)),
            pl.BlockSpec((dish_count, 2 * grid_len, 2 * grid_len), lambda f: (0, 0, 0)),
            pl.BlockSpec((dish_count, grid_len, 1), lambda f: (0, 0, 0)),
            pl.BlockSpec((dish_count, grid_len, 1), lambda f: (0, 0, 0)),
        ]
        operands = [received, tables, twist_cos, twist_sin]
        if carry_in:
            in_specs.append(pl.BlockSpec((dish_count, grid_len, lane_block), lambda f: (0, 0, 0)))
            operands.append(carried)
        if finish:
            out_shape = (dish_count, quarter, grid_len)
        else:
            out_shape = (dish_count, grid_len, lane_block)
        return pl.pallas_call(
            functools.partial(beam_kernel, dish_count, carry_in, finish),
            grid=(chunk_lanes // lane_block,),
            in_specs=in_specs,
            out_specs=pl.BlockSpec(out_shape, lambda f: (0, 0, 0)),
            out_shape=jax.ShapeDtypeStruct(out_shape, jnp.float32),
            scratch_shapes=[pltpu.VMEM((dish_count, grid_len, lane_block), jnp.float32)],
            cost_estimate=pl.CostEstimate(
                flops=int(dish_count * 2 * 512 * 512 * chunk_lanes),
                bytes_accessed=int(received.size * 2 + tables.size * 2),
                transcendentals=0,
            ),
        )(*operands)

    sent = [channelize_chunk(c) for c in range(chunks)]
    arrived = [lax.all_to_all(s, ("dish", "freq"), 2, 2, tiled=True) for s in sent]
    carried = None
    for c in range(chunks):
        carried = beamform_chunk(arrived[c], carried, c == chunks - 1)
    powers = carried

    me = lax.axis_index("dish")
    pieces = [lax.dynamic_index_in_dim(powers, me, 0, keepdims=False)]
    for shift in range(1, dish_count):
        outgoing = lax.dynamic_index_in_dim(powers, me ^ shift, 0, keepdims=False)
        pairs_list = [(i, i ^ shift) for i in range(dish_count)]
        pieces.append(lax.ppermute(outgoing, "dish", pairs_list))
    stacked = jnp.stack(pieces, axis=0)
    order = jnp.arange(dish_count, dtype=jnp.int32) ^ me
    received = jnp.take(stacked, order, axis=0)
    return received.reshape(block_width, grid_len)


def solution(mesh):
    placed = (P("freq", "dish", None, None), P("freq", "dish", None, None), P(), P())
    return jax.shard_map(
        body, mesh=mesh, in_specs=placed, out_specs=P("freq", "dish"), check_vma=False
    )
```

```python
import functools
import math

import jax
import jax.numpy as jnp
import ml_dtypes
import numpy as np
from jax import lax
from jax.experimental import pallas as pl
from jax.experimental.pallas import tpu as pltpu
from jax.sharding import PartitionSpec as P

NCHAN = 8192
CHA = 64
CHB = 128
TAPS = 4
FRAMES = 16


full_turn = 2.0 * math.pi


def table_constant(row_count, col_count, modulus, scaling):
    rows = np.arange(row_count, dtype=np.int64)[:, None]
    cols = np.arange(col_count, dtype=np.int64)[None, :]
    angles = np.float32(full_turn / modulus) * (rows * cols % modulus).astype(np.float32)
    cosine = (np.cos(angles.astype(np.float64)) * scaling).astype(ml_dtypes.bfloat16)
    sine = (np.sin(angles.astype(np.float64)) * scaling).astype(ml_dtypes.bfloat16)
    return cosine, sine


def window_constant():
    sample_index = np.arange(TAPS * NCHAN, dtype=np.float64)
    centred = (sample_index - TAPS * NCHAN / 2 + 0.5) / NCHAN
    taper_curve = 0.5 - 0.5 * np.cos(full_turn * (sample_index + 0.5) / (TAPS * NCHAN))
    shaped_window = (np.sinc(centred) * taper_curve).reshape(TAPS, NCHAN)
    energy = np.mean(np.sum(shaped_window * shaped_window, axis=0))
    return (shaped_window / np.sqrt(energy)).astype(np.float32)


def rotation_constant(row_count, col_count, modulus):
    rows = np.arange(row_count, dtype=np.int64)[:, None]
    cols = np.arange(col_count, dtype=np.int64)[None, :]
    angles = np.float32(-(full_turn / modulus)) * (rows * cols % modulus).astype(np.float32)
    angles = angles.astype(np.float64)
    return np.cos(angles).astype(np.float32), np.sin(angles).astype(np.float32)


def fourier_table(row_index, col_index, modulus, scaling):
    phases = row_index[:, None] * col_index[None, :] % modulus
    angles = full_turn / modulus * phases.astype(jnp.float32)
    cosine_table = (jnp.cos(angles) * scaling).astype(jnp.bfloat16)
    sine_table = (jnp.sin(angles) * scaling).astype(jnp.bfloat16)
    upper_rows = jnp.stack([cosine_table, -sine_table], axis=1)
    lower_rows = jnp.stack([sine_table, cosine_table], axis=1)
    return jnp.stack([upper_rows, lower_rows], axis=0)


def filter_window():
    sample_index = jnp.arange(TAPS * NCHAN, dtype=jnp.float32)
    centred = (sample_index - TAPS * NCHAN / 2 + 0.5) / NCHAN
    taper_curve = 0.5 - 0.5 * jnp.cos(full_turn * (sample_index + 0.5) / (TAPS * NCHAN))
    shaped_window = (jnp.sinc(centred) * taper_curve).reshape(TAPS, NCHAN)
    energy = jnp.mean(jnp.sum(shaped_window * shaped_window, axis=0))
    return shaped_window / jnp.sqrt(energy)


def beam_tables(grid_rows, grid_len, rows_per_device):
    positions = jnp.arange(grid_len, dtype=jnp.int32)
    cosine_base, sine_base = table_constant(grid_len, grid_len, grid_len, 1.0 / math.sqrt(grid_len))
    cosine_base = jnp.asarray(cosine_base)
    sine_base = jnp.asarray(sine_base)
    devices = grid_len // rows_per_device
    picks = (positions[None, :, None] == grid_rows[:, None, :]).astype(jnp.bfloat16)
    cosine_table = jnp.einsum(
        "jg,dgm->djm", cosine_base, picks, preferred_element_type=jnp.float32
    ).astype(jnp.bfloat16)
    sine_table = jnp.einsum(
        "jg,dgm->djm", sine_base, picks, preferred_element_type=jnp.float32
    ).astype(jnp.bfloat16)
    shape = (grid_rows.shape[0], grid_len, devices, 1, rows_per_device)
    cosine_table = cosine_table.reshape(shape)
    sine_table = sine_table.reshape(shape)
    real_rows = jnp.concatenate([cosine_table, sine_table], axis=3)
    imag_rows = jnp.concatenate([-sine_table, cosine_table], axis=3)
    rows = jnp.concatenate([real_rows, imag_rows], axis=1)
    return rows.reshape(grid_rows.shape[0], 2 * grid_len, 2 * grid_len)


def channelize_kernel(first_pair, pairs, v_ref, w_ref, t1_ref, tw_ref, t2_ref, g_ref, o_ref):
    cos_tw = tw_ref[0]
    sin_tw = tw_ref[1]
    t1 = t1_ref[...]
    t2_real = t2_ref[0]
    t2_imag = t2_ref[1]
    g_real = g_ref[0, 0]
    g_imag = g_ref[0, 1]
    half = t2_real.shape[0] // 2

    def one_frame(frame):
        acc = None
        for tap in range(TAPS):
            start = pl.multiple_of((frame - 2 * first_pair + tap) * CHA, CHA)
            piece = v_ref[0, :, pl.ds(start, CHA), :].astype(jnp.float32)
            term = w_ref[tap][None] * piece
            acc = term if acc is None else acc + term
        block = acc.astype(jnp.bfloat16).reshape(2 * CHA, CHB)
        section = jnp.dot(t1, block, preferred_element_type=jnp.float32)
        sec_real = section[:CHA]
        sec_imag = section[CHA:]
        turned_real = sec_real * cos_tw - sec_imag * sin_tw
        turned_imag = sec_real * sin_tw + sec_imag * cos_tw
        return turned_real.astype(jnp.bfloat16), turned_imag.astype(jnp.bfloat16)

    def pair(step, carry):
        first_real, first_imag = one_frame(2 * step)
        second_real, second_imag = one_frame(2 * step + 1)
        both_real = jnp.concatenate([first_real, second_real], axis=0)
        both_imag = jnp.concatenate([first_imag, second_imag], axis=0)
        dims = (((1,), (1,)), ((), ()))
        spectrum = lax.dot_general(
            t2_real, both_real, dims, preferred_element_type=jnp.float32
        ) + lax.dot_general(t2_imag, both_imag, dims, preferred_element_type=jnp.float32)
        spec_real = spectrum[:half]
        spec_imag = spectrum[half:]
        out_real = spec_real * g_real - spec_imag * g_imag
        out_imag = spec_real * g_imag + spec_imag * g_real
        lanes = pl.ds(pl.multiple_of((step - first_pair) * 2 * CHA, 2 * CHA), 2 * CHA)
        o_ref[0, 0, :, lanes] = out_real.astype(o_ref.dtype)
        o_ref[1, 0, :, lanes] = out_imag.astype(o_ref.dtype)
        return carry

    lax.fori_loop(first_pair, first_pair + pairs, pair, 0)


def beam_kernel(dish_count, carry_in, finish, *refs):
    if carry_in:
        x_ref, t_ref, c_ref, s_ref, init_ref, o_ref, acc_ref = refs
    else:
        x_ref, t_ref, c_ref, s_ref, o_ref, acc_ref = refs
    step = pl.program_id(0)
    devices = x_ref.shape[0] // dish_count
    rows = x_ref.shape[2]
    grid_len = t_ref.shape[1] // 2
    lanes = x_ref.shape[3]

    @pl.when(step == 0)
    def _():
        if carry_in:
            acc_ref[...] = init_ref[...]
        else:
            acc_ref[...] = jnp.zeros_like(acc_ref)

    parts = []
    for d in range(dish_count):
        block = x_ref[pl.ds(d * devices, devices)].reshape(2 * rows * devices, lanes)
        sums = jnp.dot(t_ref[d], block, preferred_element_type=jnp.float32)
        sum_real = sums[:grid_len]
        sum_imag = sums[grid_len:]
        cos_d = c_ref[d]
        sin_d = s_ref[d]
        part_real = sum_real * cos_d - sum_imag * sin_d
        part_imag = sum_real * sin_d + sum_imag * cos_d
        parts.append(
            (
                part_real.astype(jnp.bfloat16).astype(jnp.float32),
                part_imag.astype(jnp.bfloat16).astype(jnp.float32),
            )
        )
    (a_re, a_im), (b_re, b_im), (c_re, c_im), (d_re, d_im) = parts
    beams = [
        (a_re + b_re + c_re + d_re, a_im + b_im + c_im + d_im),
        (a_re + b_im - c_re - d_im, a_im - b_re - c_im + d_re),
        (a_re - b_re + c_re - d_re, a_im - b_im + c_im - d_im),
        (a_re - b_im - c_re + d_im, a_im + b_re - c_im - d_re),
    ]
    for q in range(dish_count):
        beam_real, beam_imag = beams[q]
        acc_ref[q] += beam_real * beam_real + beam_imag * beam_imag

    @pl.when(step == pl.num_programs(0) - 1)
    def _():
        if not finish:
            o_ref[...] = acc_ref[...]
            return
        reversal = [
            int(format(s, "0%db" % (dish_count.bit_length() - 1))[::-1], 2)
            for s in range(dish_count)
        ]
        width = o_ref.shape[1]
        for s in range(dish_count):
            total = acc_ref[reversal[s]]
            total = total + pltpu.roll(total, width, 1)
            flipped = jnp.transpose(total, (1, 0))
            o_ref[s] = flipped[:width] * (0.25 / FRAMES)


def body(voltages, feed_gains, block_assign, grid_rows):
    dish_rows = voltages.shape[0]
    block_count = lax.axis_size("freq")
    dish_count = lax.axis_size("dish")
    block_width = NCHAN // block_count
    quarter = block_width // dish_count
    dests = block_count * dish_count
    grid_len = dish_rows * block_count
    total_dishes = grid_len * dish_count
    samples = voltages.shape[-1]

    dest = jnp.arange(dests, dtype=jnp.int32)
    dest_quarter = dest // block_count
    dest_block = jnp.tile(block_assign, dish_count)
    dest_e = dest_block * dish_count + dest_quarter
    picks_e = (dest_e[:, None] == jnp.arange(dests, dtype=jnp.int32)[None, :]).astype(jnp.bfloat16)

    window = jnp.asarray(window_constant().reshape(TAPS, CHA, CHB))
    first_cos, first_sin = table_constant(CHA, CHA, CHA, 1.0 / math.sqrt(CHA))
    first_table = np.block([[first_cos, first_sin], [-first_sin, first_cos]])
    first_table = jnp.asarray(first_table)
    twiddle = jnp.asarray(np.stack(rotation_constant(CHA, CHB, NCHAN), axis=0))
    second_cos, second_sin = table_constant(CHB, CHB, CHB, 1.0 / math.sqrt(CHB))
    second_table = np.stack(
        [np.stack([second_cos, -second_sin], axis=0), np.stack([second_sin, second_cos], axis=0)],
        axis=0,
    )
    second_table = jnp.einsum(
        "je,qseb->qsjb", picks_e, jnp.asarray(second_table), preferred_element_type=jnp.float32
    ).astype(jnp.bfloat16).reshape(2, 2 * dests, CHB)
    gains = feed_gains[:, 0].reshape(dish_rows, 2, CHB, CHA)
    gains = jnp.einsum("je,rpec->rpjc", picks_e, gains, preferred_element_type=jnp.float32)
    gains = jnp.concatenate([gains, gains], axis=3)

    chunks = 2
    pairs = FRAMES // 2 // chunks
    chunk_lanes = pairs * 2 * quarter
    tables = beam_tables(grid_rows, grid_len, dish_rows)
    feed_index = jnp.arange(dish_count, dtype=jnp.int32)
    positions = jnp.arange(grid_len, dtype=jnp.int32)
    twist_cos, twist_sin = rotation_constant(dish_count, grid_len, total_dishes)
    twist_cos = jnp.asarray(twist_cos[:, :, None])
    twist_sin = jnp.asarray(twist_sin[:, :, None])
    lane_block = 2 * quarter

    volts = voltages[:, 0].reshape(dish_rows, 2, samples // CHB, CHB)

    span = (2 * pairs + TAPS - 1) * CHA

    def channelize_chunk(chunk):
        first_row = 2 * chunk * pairs * CHA
        return pl.pallas_call(
            functools.partial(channelize_kernel, chunk * pairs, pairs),
            grid=(dish_rows,),
            in_specs=[
                pl.BlockSpec(
                    (pl.Element(1), pl.Element(2), pl.Element(span), pl.Element(CHB)),
                    lambda r: (r, 0, first_row, 0),
                ),
                pl.BlockSpec((TAPS, CHA, CHB), lambda r: (0, 0, 0)),
                pl.BlockSpec((2 * CHA, 2 * CHA), lambda r: (0, 0)),
                pl.BlockSpec((2, CHA, CHB), lambda r: (0, 0, 0)),
                pl.BlockSpec((2, 2 * dests, CHB), lambda r: (0, 0, 0)),
                pl.BlockSpec((1, 2, dests, 2 * CHA), lambda r: (r, 0, 0, 0)),
            ],
            out_specs=pl.BlockSpec((2, 1, dests, chunk_lanes), lambda r: (0, r, 0, 0)),
            out_shape=jax.ShapeDtypeStruct((2, dish_rows, dests, chunk_lanes), jnp.bfloat16),
            cost_estimate=pl.CostEstimate(
                flops=int(dish_rows * pairs * 2 * 2 * 128 * 128 * 128 * 3),
                bytes_accessed=int(voltages.size * 2 + 2 * dish_rows * dests * chunk_lanes * 2),
                transcendentals=0,
            ),
        )(volts, window, first_table, twiddle, second_table, gains)

    def beamform_chunk(received, carried, finish):
        carry_in = carried is not None
        in_specs = [
            pl.BlockSpec((dests, 2, dish_rows, lane_block), lambda f: (0, 0, 0, f)),
            pl.BlockSpec((dish_count, 2 * grid_len, 2 * grid_len), lambda f: (0, 0, 0)),
            pl.BlockSpec((dish_count, grid_len, 1), lambda f: (0, 0, 0)),
            pl.BlockSpec((dish_count, grid_len, 1), lambda f: (0, 0, 0)),
        ]
        operands = [received, tables, twist_cos, twist_sin]
        if carry_in:
            in_specs.append(pl.BlockSpec((dish_count, grid_len, lane_block), lambda f: (0, 0, 0)))
            operands.append(carried)
        if finish:
            out_shape = (dish_count, quarter, grid_len)
        else:
            out_shape = (dish_count, grid_len, lane_block)
        return pl.pallas_call(
            functools.partial(beam_kernel, dish_count, carry_in, finish),
            grid=(chunk_lanes // lane_block,),
            in_specs=in_specs,
            out_specs=pl.BlockSpec(out_shape, lambda f: (0, 0, 0)),
            out_shape=jax.ShapeDtypeStruct(out_shape, jnp.float32),
            scratch_shapes=[pltpu.VMEM((dish_count, grid_len, lane_block), jnp.float32)],
            cost_estimate=pl.CostEstimate(
                flops=int(dish_count * 2 * 512 * 512 * chunk_lanes),
                bytes_accessed=int(received.size * 2 + tables.size * 2),
                transcendentals=0,
            ),
        )(*operands)

    sent = [channelize_chunk(c) for c in range(chunks)]
    arrived = [
        jnp.transpose(lax.all_to_all(s, ("dish", "freq"), 2, 2, tiled=True), (2, 0, 1, 3))
        for s in sent
    ]
    carried = None
    for c in range(chunks):
        carried = beamform_chunk(arrived[c], carried, c == chunks - 1)
    powers = carried

    me = lax.axis_index("dish")
    pieces = [lax.dynamic_index_in_dim(powers, me, 0, keepdims=False)]
    for shift in range(1, dish_count):
        outgoing = lax.dynamic_index_in_dim(powers, me ^ shift, 0, keepdims=False)
        pairs_list = [(i, i ^ shift) for i in range(dish_count)]
        pieces.append(lax.ppermute(outgoing, "dish", pairs_list))
    stacked = jnp.stack(pieces, axis=0)
    order = jnp.arange(dish_count, dtype=jnp.int32) ^ me
    received = jnp.take(stacked, order, axis=0)
    return received.reshape(block_width, grid_len)


def solution(mesh):
    placed = (P("freq", "dish", None, None), P("freq", "dish", None, None), P(), P())
    return jax.shard_map(
        body, mesh=mesh, in_specs=placed, out_specs=P("freq", "dish"), check_vma=False
    )
```

```python
import functools
import math

import jax
import jax.numpy as jnp
import ml_dtypes
import numpy as np
from jax import lax
from jax.experimental import pallas as pl
from jax.experimental.pallas import tpu as pltpu
from jax.sharding import PartitionSpec as P

NCHAN = 8192
CHA = 64
CHB = 128
TAPS = 4
FRAMES = 16


full_turn = 2.0 * math.pi


def table_constant(row_count, col_count, modulus, scaling):
    rows = np.arange(row_count, dtype=np.int64)[:, None]
    cols = np.arange(col_count, dtype=np.int64)[None, :]
    angles = np.float32(full_turn / modulus) * (rows * cols % modulus).astype(np.float32)
    cosine = (np.cos(angles.astype(np.float64)) * scaling).astype(ml_dtypes.bfloat16)
    sine = (np.sin(angles.astype(np.float64)) * scaling).astype(ml_dtypes.bfloat16)
    return cosine, sine


def window_constant():
    sample_index = np.arange(TAPS * NCHAN, dtype=np.float64)
    centred = (sample_index - TAPS * NCHAN / 2 + 0.5) / NCHAN
    taper_curve = 0.5 - 0.5 * np.cos(full_turn * (sample_index + 0.5) / (TAPS * NCHAN))
    shaped_window = (np.sinc(centred) * taper_curve).reshape(TAPS, NCHAN)
    energy = np.mean(np.sum(shaped_window * shaped_window, axis=0))
    return (shaped_window / np.sqrt(energy)).astype(np.float32)


def rotation_constant(row_count, col_count, modulus):
    rows = np.arange(row_count, dtype=np.int64)[:, None]
    cols = np.arange(col_count, dtype=np.int64)[None, :]
    angles = np.float32(-(full_turn / modulus)) * (rows * cols % modulus).astype(np.float32)
    angles = angles.astype(np.float64)
    return np.cos(angles).astype(np.float32), np.sin(angles).astype(np.float32)


def fourier_table(row_index, col_index, modulus, scaling):
    phases = row_index[:, None] * col_index[None, :] % modulus
    angles = full_turn / modulus * phases.astype(jnp.float32)
    cosine_table = (jnp.cos(angles) * scaling).astype(jnp.bfloat16)
    sine_table = (jnp.sin(angles) * scaling).astype(jnp.bfloat16)
    upper_rows = jnp.stack([cosine_table, -sine_table], axis=1)
    lower_rows = jnp.stack([sine_table, cosine_table], axis=1)
    return jnp.stack([upper_rows, lower_rows], axis=0)


def filter_window():
    sample_index = jnp.arange(TAPS * NCHAN, dtype=jnp.float32)
    centred = (sample_index - TAPS * NCHAN / 2 + 0.5) / NCHAN
    taper_curve = 0.5 - 0.5 * jnp.cos(full_turn * (sample_index + 0.5) / (TAPS * NCHAN))
    shaped_window = (jnp.sinc(centred) * taper_curve).reshape(TAPS, NCHAN)
    energy = jnp.mean(jnp.sum(shaped_window * shaped_window, axis=0))
    return shaped_window / jnp.sqrt(energy)


def beam_tables(grid_rows, grid_len, rows_per_device):
    positions = jnp.arange(grid_len, dtype=jnp.int32)
    cosine_base, sine_base = table_constant(grid_len, grid_len, grid_len, 1.0 / math.sqrt(grid_len))
    cosine_base = jnp.asarray(cosine_base)
    sine_base = jnp.asarray(sine_base)
    devices = grid_len // rows_per_device
    picks = (positions[None, :, None] == grid_rows[:, None, :]).astype(jnp.bfloat16)
    cosine_table = jnp.einsum(
        "jg,dgm->djm", cosine_base, picks, preferred_element_type=jnp.float32
    ).astype(jnp.bfloat16)
    sine_table = jnp.einsum(
        "jg,dgm->djm", sine_base, picks, preferred_element_type=jnp.float32
    ).astype(jnp.bfloat16)
    shape = (grid_rows.shape[0], grid_len, devices, 1, rows_per_device)
    cosine_table = cosine_table.reshape(shape)
    sine_table = sine_table.reshape(shape)
    real_rows = jnp.concatenate([cosine_table, sine_table], axis=3)
    imag_rows = jnp.concatenate([-sine_table, cosine_table], axis=3)
    rows = jnp.concatenate([real_rows, imag_rows], axis=1)
    return rows.reshape(grid_rows.shape[0], 2 * grid_len, 2 * grid_len)


def channelize_kernel(first_pair, pairs, v_ref, w_ref, t1_ref, tw_ref, t2_ref, g_ref, o_ref):
    cos_tw = tw_ref[0]
    sin_tw = tw_ref[1]
    t1 = t1_ref[...]
    t2_real = t2_ref[0]
    t2_imag = t2_ref[1]
    g_real = g_ref[0, 0]
    g_imag = g_ref[0, 1]
    half = t2_real.shape[0] // 2

    def one_frame(pieces):
        acc = None
        for tap in range(TAPS):
            term = w_ref[tap][None] * pieces[tap]
            acc = term if acc is None else acc + term
        block = acc.astype(jnp.bfloat16).reshape(2 * CHA, CHB)
        section = jnp.dot(t1, block, preferred_element_type=jnp.float32)
        sec_real = section[:CHA]
        sec_imag = section[CHA:]
        turned_real = sec_real * cos_tw - sec_imag * sin_tw
        turned_imag = sec_real * sin_tw + sec_imag * cos_tw
        return turned_real.astype(jnp.bfloat16), turned_imag.astype(jnp.bfloat16)

    def pair(step, carry):
        pieces = []
        for offset in range(TAPS + 1):
            start = pl.multiple_of((2 * (step - first_pair) + offset) * CHA, CHA)
            pieces.append(v_ref[0, :, pl.ds(start, CHA), :].astype(jnp.float32))
        first_real, first_imag = one_frame(pieces[:TAPS])
        second_real, second_imag = one_frame(pieces[1:])
        both_real = jnp.concatenate([first_real, second_real], axis=0)
        both_imag = jnp.concatenate([first_imag, second_imag], axis=0)
        dims = (((1,), (1,)), ((), ()))
        spectrum = lax.dot_general(
            t2_real, both_real, dims, preferred_element_type=jnp.float32
        ) + lax.dot_general(t2_imag, both_imag, dims, preferred_element_type=jnp.float32)
        spec_real = spectrum[:half]
        spec_imag = spectrum[half:]
        out_real = spec_real * g_real - spec_imag * g_imag
        out_imag = spec_real * g_imag + spec_imag * g_real
        lanes = pl.ds(pl.multiple_of((step - first_pair) * 2 * CHA, 2 * CHA), 2 * CHA)
        o_ref[0, 0, :, lanes] = out_real.astype(o_ref.dtype)
        o_ref[1, 0, :, lanes] = out_imag.astype(o_ref.dtype)
        return carry

    lax.fori_loop(first_pair, first_pair + pairs, pair, 0, unroll=True)


def beam_kernel(dish_count, carry_in, finish, *refs):
    if carry_in:
        x_ref, t_ref, c_ref, s_ref, init_ref, o_ref, acc_ref = refs
    else:
        x_ref, t_ref, c_ref, s_ref, o_ref, acc_ref = refs
    step = pl.program_id(0)
    devices = x_ref.shape[0] // dish_count
    rows = x_ref.shape[2]
    grid_len = t_ref.shape[1] // 2
    lanes = x_ref.shape[3]

    @pl.when(step == 0)
    def _():
        if carry_in:
            acc_ref[...] = init_ref[...]
        else:
            acc_ref[...] = jnp.zeros_like(acc_ref)

    parts = []
    for d in range(dish_count):
        block = x_ref[pl.ds(d * devices, devices)].reshape(2 * rows * devices, lanes)
        sums = jnp.dot(t_ref[d], block, preferred_element_type=jnp.float32)
        sum_real = sums[:grid_len]
        sum_imag = sums[grid_len:]
        cos_d = c_ref[d]
        sin_d = s_ref[d]
        part_real = sum_real * cos_d - sum_imag * sin_d
        part_imag = sum_real * sin_d + sum_imag * cos_d
        parts.append(
            (
                part_real.astype(jnp.bfloat16).astype(jnp.float32),
                part_imag.astype(jnp.bfloat16).astype(jnp.float32),
            )
        )
    (a_re, a_im), (b_re, b_im), (c_re, c_im), (d_re, d_im) = parts
    beams = [
        (a_re + b_re + c_re + d_re, a_im + b_im + c_im + d_im),
        (a_re + b_im - c_re - d_im, a_im - b_re - c_im + d_re),
        (a_re - b_re + c_re - d_re, a_im - b_im + c_im - d_im),
        (a_re - b_im - c_re + d_im, a_im + b_re - c_im - d_re),
    ]
    for q in range(dish_count):
        beam_real, beam_imag = beams[q]
        acc_ref[q] += beam_real * beam_real + beam_imag * beam_imag

    @pl.when(step == pl.num_programs(0) - 1)
    def _():
        if not finish:
            o_ref[...] = acc_ref[...]
            return
        reversal = [
            int(format(s, "0%db" % (dish_count.bit_length() - 1))[::-1], 2)
            for s in range(dish_count)
        ]
        width = o_ref.shape[1]
        for s in range(dish_count):
            total = acc_ref[reversal[s]]
            total = total + pltpu.roll(total, width, 1)
            flipped = jnp.transpose(total, (1, 0))
            o_ref[s] = flipped[:width] * (0.25 / FRAMES)


def body(voltages, feed_gains, block_assign, grid_rows):
    dish_rows = voltages.shape[0]
    block_count = lax.axis_size("freq")
    dish_count = lax.axis_size("dish")
    block_width = NCHAN // block_count
    quarter = block_width // dish_count
    dests = block_count * dish_count
    grid_len = dish_rows * block_count
    total_dishes = grid_len * dish_count
    samples = voltages.shape[-1]

    dest = jnp.arange(dests, dtype=jnp.int32)
    dest_quarter = dest // block_count
    dest_block = jnp.tile(block_assign, dish_count)
    dest_e = dest_block * dish_count + dest_quarter
    picks_e = (dest_e[:, None] == jnp.arange(dests, dtype=jnp.int32)[None, :]).astype(jnp.bfloat16)

    window = jnp.asarray(window_constant().reshape(TAPS, CHA, CHB))
    first_cos, first_sin = table_constant(CHA, CHA, CHA, 1.0 / math.sqrt(CHA))
    first_table = np.block([[first_cos, first_sin], [-first_sin, first_cos]])
    first_table = jnp.asarray(first_table)
    twiddle = jnp.asarray(np.stack(rotation_constant(CHA, CHB, NCHAN), axis=0))
    second_cos, second_sin = table_constant(CHB, CHB, CHB, 1.0 / math.sqrt(CHB))
    second_table = np.stack(
        [np.stack([second_cos, -second_sin], axis=0), np.stack([second_sin, second_cos], axis=0)],
        axis=0,
    )
    second_table = jnp.einsum(
        "je,qseb->qsjb", picks_e, jnp.asarray(second_table), preferred_element_type=jnp.float32
    ).astype(jnp.bfloat16).reshape(2, 2 * dests, CHB)
    gains = feed_gains[:, 0].reshape(dish_rows, 2, CHB, CHA)
    gains = jnp.einsum("je,rpec->rpjc", picks_e, gains, preferred_element_type=jnp.float32)
    gains = jnp.concatenate([gains, gains], axis=3)

    chunks = 2
    pairs = FRAMES // 2 // chunks
    chunk_lanes = pairs * 2 * quarter
    tables = beam_tables(grid_rows, grid_len, dish_rows)
    feed_index = jnp.arange(dish_count, dtype=jnp.int32)
    positions = jnp.arange(grid_len, dtype=jnp.int32)
    twist_cos, twist_sin = rotation_constant(dish_count, grid_len, total_dishes)
    twist_cos = jnp.asarray(twist_cos[:, :, None])
    twist_sin = jnp.asarray(twist_sin[:, :, None])
    lane_block = 2 * quarter

    volts = voltages[:, 0].reshape(dish_rows, 2, samples // CHB, CHB)

    span = (2 * pairs + TAPS - 1) * CHA

    def channelize_chunk(chunk):
        first_row = 2 * chunk * pairs * CHA
        return pl.pallas_call(
            functools.partial(channelize_kernel, chunk * pairs, pairs),
            grid=(dish_rows,),
            in_specs=[
                pl.BlockSpec(
                    (pl.Element(1), pl.Element(2), pl.Element(span), pl.Element(CHB)),
                    lambda r: (r, 0, first_row, 0),
                ),
                pl.BlockSpec((TAPS, CHA, CHB), lambda r: (0, 0, 0)),
                pl.BlockSpec((2 * CHA, 2 * CHA), lambda r: (0, 0)),
                pl.BlockSpec((2, CHA, CHB), lambda r: (0, 0, 0)),
                pl.BlockSpec((2, 2 * dests, CHB), lambda r: (0, 0, 0)),
                pl.BlockSpec((1, 2, dests, 2 * CHA), lambda r: (r, 0, 0, 0)),
            ],
            out_specs=pl.BlockSpec((2, 1, dests, chunk_lanes), lambda r: (0, r, 0, 0)),
            out_shape=jax.ShapeDtypeStruct((2, dish_rows, dests, chunk_lanes), jnp.bfloat16),
            cost_estimate=pl.CostEstimate(
                flops=int(dish_rows * pairs * 2 * 2 * 128 * 128 * 128 * 3),
                bytes_accessed=int(voltages.size * 2 + 2 * dish_rows * dests * chunk_lanes * 2),
                transcendentals=0,
            ),
        )(volts, window, first_table, twiddle, second_table, gains)

    def beamform_chunk(received, carried, finish):
        carry_in = carried is not None
        in_specs = [
            pl.BlockSpec((dests, 2, dish_rows, lane_block), lambda f: (0, 0, 0, f)),
            pl.BlockSpec((dish_count, 2 * grid_len, 2 * grid_len), lambda f: (0, 0, 0)),
            pl.BlockSpec((dish_count, grid_len, 1), lambda f: (0, 0, 0)),
            pl.BlockSpec((dish_count, grid_len, 1), lambda f: (0, 0, 0)),
        ]
        operands = [received, tables, twist_cos, twist_sin]
        if carry_in:
            in_specs.append(pl.BlockSpec((dish_count, grid_len, lane_block), lambda f: (0, 0, 0)))
            operands.append(carried)
        if finish:
            out_shape = (dish_count, quarter, grid_len)
        else:
            out_shape = (dish_count, grid_len, lane_block)
        return pl.pallas_call(
            functools.partial(beam_kernel, dish_count, carry_in, finish),
            grid=(chunk_lanes // lane_block,),
            in_specs=in_specs,
            out_specs=pl.BlockSpec(out_shape, lambda f: (0, 0, 0)),
            out_shape=jax.ShapeDtypeStruct(out_shape, jnp.float32),
            scratch_shapes=[pltpu.VMEM((dish_count, grid_len, lane_block), jnp.float32)],
            cost_estimate=pl.CostEstimate(
                flops=int(dish_count * 2 * 512 * 512 * chunk_lanes),
                bytes_accessed=int(received.size * 2 + tables.size * 2),
                transcendentals=0,
            ),
        )(*operands)

    sent = [channelize_chunk(c) for c in range(chunks)]
    arrived = [
        jnp.transpose(lax.all_to_all(s, ("dish", "freq"), 2, 2, tiled=True), (2, 0, 1, 3))
        for s in sent
    ]
    carried = None
    for c in range(chunks):
        carried = beamform_chunk(arrived[c], carried, c == chunks - 1)
    powers = carried

    me = lax.axis_index("dish")
    pieces = [lax.dynamic_index_in_dim(powers, me, 0, keepdims=False)]
    for shift in range(1, dish_count):
        outgoing = lax.dynamic_index_in_dim(powers, me ^ shift, 0, keepdims=False)
        pairs_list = [(i, i ^ shift) for i in range(dish_count)]
        pieces.append(lax.ppermute(outgoing, "dish", pairs_list))
    stacked = jnp.stack(pieces, axis=0)
    order = jnp.arange(dish_count, dtype=jnp.int32) ^ me
    received = jnp.take(stacked, order, axis=0)
    return received.reshape(block_width, grid_len)


def solution(mesh):
    placed = (P("freq", "dish", None, None), P("freq", "dish", None, None), P(), P())
    return jax.shard_map(
        body, mesh=mesh, in_specs=placed, out_specs=P("freq", "dish"), check_vma=False
    )
```

```python
import functools
import math

import jax
import jax.numpy as jnp
import ml_dtypes
import numpy as np
from jax import lax
from jax.experimental import pallas as pl
from jax.experimental.pallas import tpu as pltpu
from jax.sharding import PartitionSpec as P

NCHAN = 8192
CHA = 64
CHB = 128
TAPS = 4
FRAMES = 16


full_turn = 2.0 * math.pi


def table_constant(row_count, col_count, modulus, scaling):
    rows = np.arange(row_count, dtype=np.int64)[:, None]
    cols = np.arange(col_count, dtype=np.int64)[None, :]
    angles = np.float32(full_turn / modulus) * (rows * cols % modulus).astype(np.float32)
    cosine = (np.cos(angles.astype(np.float64)) * scaling).astype(ml_dtypes.bfloat16)
    sine = (np.sin(angles.astype(np.float64)) * scaling).astype(ml_dtypes.bfloat16)
    return cosine, sine


def window_constant():
    sample_index = np.arange(TAPS * NCHAN, dtype=np.float64)
    centred = (sample_index - TAPS * NCHAN / 2 + 0.5) / NCHAN
    taper_curve = 0.5 - 0.5 * np.cos(full_turn * (sample_index + 0.5) / (TAPS * NCHAN))
    shaped_window = (np.sinc(centred) * taper_curve).reshape(TAPS, NCHAN)
    energy = np.mean(np.sum(shaped_window * shaped_window, axis=0))
    return (shaped_window / np.sqrt(energy)).astype(np.float32)


def rotation_constant(row_count, col_count, modulus):
    rows = np.arange(row_count, dtype=np.int64)[:, None]
    cols = np.arange(col_count, dtype=np.int64)[None, :]
    angles = np.float32(-(full_turn / modulus)) * (rows * cols % modulus).astype(np.float32)
    angles = angles.astype(np.float64)
    return np.cos(angles).astype(np.float32), np.sin(angles).astype(np.float32)


def fourier_table(row_index, col_index, modulus, scaling):
    phases = row_index[:, None] * col_index[None, :] % modulus
    angles = full_turn / modulus * phases.astype(jnp.float32)
    cosine_table = (jnp.cos(angles) * scaling).astype(jnp.bfloat16)
    sine_table = (jnp.sin(angles) * scaling).astype(jnp.bfloat16)
    upper_rows = jnp.stack([cosine_table, -sine_table], axis=1)
    lower_rows = jnp.stack([sine_table, cosine_table], axis=1)
    return jnp.stack([upper_rows, lower_rows], axis=0)


def filter_window():
    sample_index = jnp.arange(TAPS * NCHAN, dtype=jnp.float32)
    centred = (sample_index - TAPS * NCHAN / 2 + 0.5) / NCHAN
    taper_curve = 0.5 - 0.5 * jnp.cos(full_turn * (sample_index + 0.5) / (TAPS * NCHAN))
    shaped_window = (jnp.sinc(centred) * taper_curve).reshape(TAPS, NCHAN)
    energy = jnp.mean(jnp.sum(shaped_window * shaped_window, axis=0))
    return shaped_window / jnp.sqrt(energy)


def beam_tables(grid_rows, grid_len, rows_per_device):
    positions = jnp.arange(grid_len, dtype=jnp.int32)
    cosine_base, sine_base = table_constant(grid_len, grid_len, grid_len, 1.0 / math.sqrt(grid_len))
    cosine_base = jnp.asarray(cosine_base)
    sine_base = jnp.asarray(sine_base)
    devices = grid_len // rows_per_device
    picks = (positions[None, :, None] == grid_rows[:, None, :]).astype(jnp.bfloat16)
    cosine_table = jnp.einsum(
        "jg,dgm->djm", cosine_base, picks, preferred_element_type=jnp.float32
    ).astype(jnp.bfloat16)
    sine_table = jnp.einsum(
        "jg,dgm->djm", sine_base, picks, preferred_element_type=jnp.float32
    ).astype(jnp.bfloat16)
    shape = (grid_rows.shape[0], grid_len, devices, 1, rows_per_device)
    cosine_table = cosine_table.reshape(shape)
    sine_table = sine_table.reshape(shape)
    real_rows = jnp.concatenate([cosine_table, sine_table], axis=3)
    imag_rows = jnp.concatenate([-sine_table, cosine_table], axis=3)
    rows = jnp.concatenate([real_rows, imag_rows], axis=1)
    return rows.reshape(grid_rows.shape[0], 2 * grid_len, 2 * grid_len)


def channelize_kernel(first_pair, pairs, v_ref, w_ref, t1_ref, tw_ref, t2_ref, g_ref, o_ref):
    cos_tw = tw_ref[0]
    sin_tw = tw_ref[1]
    t1 = t1_ref[...]
    t2_real = t2_ref[0]
    t2_imag = t2_ref[1]
    g_real = g_ref[0, 0]
    g_imag = g_ref[0, 1]
    half = t2_real.shape[0] // 2

    def one_frame(pieces):
        acc = None
        for tap in range(TAPS):
            term = w_ref[tap][None] * pieces[tap]
            acc = term if acc is None else acc + term
        block = acc.astype(jnp.bfloat16).reshape(2 * CHA, CHB)
        section = jnp.dot(t1, block, preferred_element_type=jnp.float32)
        sec_real = section[:CHA]
        sec_imag = section[CHA:]
        turned_real = sec_real * cos_tw - sec_imag * sin_tw
        turned_imag = sec_real * sin_tw + sec_imag * cos_tw
        return turned_real.astype(jnp.bfloat16), turned_imag.astype(jnp.bfloat16)

    def pair(step, carry):
        pieces = []
        for offset in range(TAPS + 1):
            start = pl.multiple_of((2 * (step - first_pair) + offset) * CHA, CHA)
            pieces.append(v_ref[0, :, pl.ds(start, CHA), :].astype(jnp.float32))
        first_real, first_imag = one_frame(pieces[:TAPS])
        second_real, second_imag = one_frame(pieces[1:])
        both_real = jnp.concatenate([first_real, second_real], axis=0)
        both_imag = jnp.concatenate([first_imag, second_imag], axis=0)
        dims = (((1,), (1,)), ((), ()))
        spectrum = lax.dot_general(
            t2_real, both_real, dims, preferred_element_type=jnp.float32
        ) + lax.dot_general(t2_imag, both_imag, dims, preferred_element_type=jnp.float32)
        spec_real = spectrum[:half]
        spec_imag = spectrum[half:]
        out_real = spec_real * g_real - spec_imag * g_imag
        out_imag = spec_real * g_imag + spec_imag * g_real
        lanes = pl.ds(pl.multiple_of((step - first_pair) * 2 * CHA, 2 * CHA), 2 * CHA)
        o_ref[0, 0, :, lanes] = out_real.astype(o_ref.dtype)
        o_ref[1, 0, :, lanes] = out_imag.astype(o_ref.dtype)
        return carry

    lax.fori_loop(first_pair, first_pair + pairs, pair, 0, unroll=True)


def beam_kernel(dish_count, carry_in, finish, *refs):
    if carry_in:
        x_ref, t_ref, c_ref, s_ref, init_ref, o_ref, acc_ref = refs
    else:
        x_ref, t_ref, c_ref, s_ref, o_ref, acc_ref = refs
    step = pl.program_id(0)
    devices = x_ref.shape[0] // dish_count
    rows = x_ref.shape[2]
    grid_len = t_ref.shape[1] // 2
    lanes = x_ref.shape[3]

    @pl.when(step == 0)
    def _():
        if carry_in:
            acc_ref[...] = init_ref[...]
        else:
            acc_ref[...] = jnp.zeros_like(acc_ref)

    parts = []
    for d in range(dish_count):
        block = x_ref[pl.ds(d * devices, devices)].reshape(2 * rows * devices, lanes)
        sums = jnp.dot(t_ref[d], block, preferred_element_type=jnp.float32)
        sum_real = sums[:grid_len]
        sum_imag = sums[grid_len:]
        cos_d = c_ref[d]
        sin_d = s_ref[d]
        part_real = sum_real * cos_d - sum_imag * sin_d
        part_imag = sum_real * sin_d + sum_imag * cos_d
        parts.append(
            (
                part_real.astype(jnp.bfloat16).astype(jnp.float32),
                part_imag.astype(jnp.bfloat16).astype(jnp.float32),
            )
        )
    (a_re, a_im), (b_re, b_im), (c_re, c_im), (d_re, d_im) = parts
    beams = [
        (a_re + b_re + c_re + d_re, a_im + b_im + c_im + d_im),
        (a_re + b_im - c_re - d_im, a_im - b_re - c_im + d_re),
        (a_re - b_re + c_re - d_re, a_im - b_im + c_im - d_im),
        (a_re - b_im - c_re + d_im, a_im + b_re - c_im - d_re),
    ]
    for q in range(dish_count):
        beam_real, beam_imag = beams[q]
        acc_ref[q] += beam_real * beam_real + beam_imag * beam_imag

    @pl.when(step == pl.num_programs(0) - 1)
    def _():
        if not finish:
            o_ref[...] = acc_ref[...]
            return
        me = lax.axis_index("dish")
        width = o_ref.shape[1]
        for shift in range(dish_count):
            target = jnp.bitwise_xor(me, shift)
            beam_index = jnp.bitwise_or(
                jnp.left_shift(jnp.bitwise_and(target, 1), 1), jnp.right_shift(target, 1)
            )
            total = acc_ref[beam_index]
            folded = total[:, :CHB]
            for k in range(1, lanes // CHB):
                folded = folded + total[:, k * CHB : (k + 1) * CHB]
            folded = folded + pltpu.roll(folded, width, 1)
            flipped = jnp.transpose(folded, (1, 0))
            o_ref[shift] = flipped[:width] * (0.25 / FRAMES)


def body(voltages, feed_gains, block_assign, grid_rows):
    dish_rows = voltages.shape[0]
    block_count = lax.axis_size("freq")
    dish_count = lax.axis_size("dish")
    block_width = NCHAN // block_count
    quarter = block_width // dish_count
    dests = block_count * dish_count
    grid_len = dish_rows * block_count
    total_dishes = grid_len * dish_count
    samples = voltages.shape[-1]

    dest = jnp.arange(dests, dtype=jnp.int32)
    dest_quarter = dest // block_count
    dest_block = jnp.tile(block_assign, dish_count)
    dest_e = dest_block * dish_count + dest_quarter
    picks_e = (dest_e[:, None] == jnp.arange(dests, dtype=jnp.int32)[None, :]).astype(jnp.bfloat16)

    window = jnp.asarray(window_constant().reshape(TAPS, CHA, CHB))
    first_cos, first_sin = table_constant(CHA, CHA, CHA, 1.0 / math.sqrt(CHA))
    first_table = np.block([[first_cos, first_sin], [-first_sin, first_cos]])
    first_table = jnp.asarray(first_table)
    twiddle = jnp.asarray(np.stack(rotation_constant(CHA, CHB, NCHAN), axis=0))
    second_cos, second_sin = table_constant(CHB, CHB, CHB, 1.0 / math.sqrt(CHB))
    second_table = np.stack(
        [np.stack([second_cos, -second_sin], axis=0), np.stack([second_sin, second_cos], axis=0)],
        axis=0,
    )
    second_table = jnp.einsum(
        "je,qseb->qsjb", picks_e, jnp.asarray(second_table), preferred_element_type=jnp.float32
    ).astype(jnp.bfloat16).reshape(2, 2 * dests, CHB)
    gains = feed_gains[:, 0].reshape(dish_rows, 2, CHB, CHA)
    gains = jnp.einsum("je,rpec->rpjc", picks_e, gains, preferred_element_type=jnp.float32)
    gains = jnp.concatenate([gains, gains], axis=3)

    chunks = 2
    pairs = FRAMES // 2 // chunks
    chunk_lanes = pairs * 2 * quarter
    tables = beam_tables(grid_rows, grid_len, dish_rows)
    feed_index = jnp.arange(dish_count, dtype=jnp.int32)
    positions = jnp.arange(grid_len, dtype=jnp.int32)
    twist_cos, twist_sin = rotation_constant(dish_count, grid_len, total_dishes)
    twist_cos = jnp.asarray(twist_cos[:, :, None])
    twist_sin = jnp.asarray(twist_sin[:, :, None])
    lane_block = 4 * quarter

    volts = voltages[:, 0].reshape(dish_rows, 2, samples // CHB, CHB)

    span = (2 * pairs + TAPS - 1) * CHA

    def channelize_chunk(chunk):
        first_row = 2 * chunk * pairs * CHA
        return pl.pallas_call(
            functools.partial(channelize_kernel, chunk * pairs, pairs),
            grid=(dish_rows,),
            in_specs=[
                pl.BlockSpec(
                    (pl.Element(1), pl.Element(2), pl.Element(span), pl.Element(CHB)),
                    lambda r: (r, 0, first_row, 0),
                ),
                pl.BlockSpec((TAPS, CHA, CHB), lambda r: (0, 0, 0)),
                pl.BlockSpec((2 * CHA, 2 * CHA), lambda r: (0, 0)),
                pl.BlockSpec((2, CHA, CHB), lambda r: (0, 0, 0)),
                pl.BlockSpec((2, 2 * dests, CHB), lambda r: (0, 0, 0)),
                pl.BlockSpec((1, 2, dests, 2 * CHA), lambda r: (r, 0, 0, 0)),
            ],
            out_specs=pl.BlockSpec((2, 1, dests, chunk_lanes), lambda r: (0, r, 0, 0)),
            out_shape=jax.ShapeDtypeStruct((2, dish_rows, dests, chunk_lanes), jnp.bfloat16),
            cost_estimate=pl.CostEstimate(
                flops=int(dish_rows * pairs * 2 * 2 * 128 * 128 * 128 * 3),
                bytes_accessed=int(voltages.size * 2 + 2 * dish_rows * dests * chunk_lanes * 2),
                transcendentals=0,
            ),
        )(volts, window, first_table, twiddle, second_table, gains)

    def beamform_chunk(received, carried, finish):
        carry_in = carried is not None
        in_specs = [
            pl.BlockSpec((dests, 2, dish_rows, lane_block), lambda f: (0, 0, 0, f)),
            pl.BlockSpec((dish_count, 2 * grid_len, 2 * grid_len), lambda f: (0, 0, 0)),
            pl.BlockSpec((dish_count, grid_len, 1), lambda f: (0, 0, 0)),
            pl.BlockSpec((dish_count, grid_len, 1), lambda f: (0, 0, 0)),
        ]
        operands = [received, tables, twist_cos, twist_sin]
        if carry_in:
            in_specs.append(pl.BlockSpec((dish_count, grid_len, lane_block), lambda f: (0, 0, 0)))
            operands.append(carried)
        if finish:
            out_shape = (dish_count, quarter, grid_len)
        else:
            out_shape = (dish_count, grid_len, lane_block)
        return pl.pallas_call(
            functools.partial(beam_kernel, dish_count, carry_in, finish),
            grid=(chunk_lanes // lane_block,),
            in_specs=in_specs,
            out_specs=pl.BlockSpec(out_shape, lambda f: (0, 0, 0)),
            out_shape=jax.ShapeDtypeStruct(out_shape, jnp.float32),
            scratch_shapes=[pltpu.VMEM((dish_count, grid_len, lane_block), jnp.float32)],
            cost_estimate=pl.CostEstimate(
                flops=int(dish_count * 2 * 512 * 512 * chunk_lanes),
                bytes_accessed=int(received.size * 2 + tables.size * 2),
                transcendentals=0,
            ),
        )(*operands)

    sent = [channelize_chunk(c) for c in range(chunks)]
    arrived = [
        jnp.transpose(lax.all_to_all(s, ("dish", "freq"), 2, 2, tiled=True), (2, 0, 1, 3))
        for s in sent
    ]
    carried = None
    for c in range(chunks):
        carried = beamform_chunk(arrived[c], carried, c == chunks - 1)
    powers = carried

    me = lax.axis_index("dish")
    pieces = [powers[0]]
    for shift in range(1, dish_count):
        outgoing = powers[shift]
        pairs_list = [(i, i ^ shift) for i in range(dish_count)]
        pieces.append(lax.ppermute(outgoing, "dish", pairs_list))
    stacked = jnp.stack(pieces, axis=0)
    order = jnp.arange(dish_count, dtype=jnp.int32) ^ me
    received = jnp.take(stacked, order, axis=0)
    return received.reshape(block_width, grid_len)


def solution(mesh):
    placed = (P("freq", "dish", None, None), P("freq", "dish", None, None), P(), P())
    return jax.shard_map(
        body, mesh=mesh, in_specs=placed, out_specs=P("freq", "dish"), check_vma=False
    )
```

```python
import functools
import math

import jax
import jax.numpy as jnp
import ml_dtypes
import numpy as np
from jax import lax
from jax.experimental import pallas as pl
from jax.experimental.pallas import tpu as pltpu
from jax.sharding import PartitionSpec as P

NCHAN = 8192
CHA = 64
CHB = 128
TAPS = 4
FRAMES = 16


full_turn = 2.0 * math.pi


def table_constant(row_count, col_count, modulus, scaling):
    rows = np.arange(row_count, dtype=np.int64)[:, None]
    cols = np.arange(col_count, dtype=np.int64)[None, :]
    angles = np.float32(full_turn / modulus) * (rows * cols % modulus).astype(np.float32)
    cosine = (np.cos(angles.astype(np.float64)) * scaling).astype(ml_dtypes.bfloat16)
    sine = (np.sin(angles.astype(np.float64)) * scaling).astype(ml_dtypes.bfloat16)
    return cosine, sine


def window_constant():
    sample_index = np.arange(TAPS * NCHAN, dtype=np.float64)
    centred = (sample_index - TAPS * NCHAN / 2 + 0.5) / NCHAN
    taper_curve = 0.5 - 0.5 * np.cos(full_turn * (sample_index + 0.5) / (TAPS * NCHAN))
    shaped_window = (np.sinc(centred) * taper_curve).reshape(TAPS, NCHAN)
    energy = np.mean(np.sum(shaped_window * shaped_window, axis=0))
    return (shaped_window / np.sqrt(energy)).astype(np.float32)


def rotation_constant(row_count, col_count, modulus):
    rows = np.arange(row_count, dtype=np.int64)[:, None]
    cols = np.arange(col_count, dtype=np.int64)[None, :]
    angles = np.float32(-(full_turn / modulus)) * (rows * cols % modulus).astype(np.float32)
    angles = angles.astype(np.float64)
    return np.cos(angles).astype(np.float32), np.sin(angles).astype(np.float32)


def fourier_table(row_index, col_index, modulus, scaling):
    phases = row_index[:, None] * col_index[None, :] % modulus
    angles = full_turn / modulus * phases.astype(jnp.float32)
    cosine_table = (jnp.cos(angles) * scaling).astype(jnp.bfloat16)
    sine_table = (jnp.sin(angles) * scaling).astype(jnp.bfloat16)
    upper_rows = jnp.stack([cosine_table, -sine_table], axis=1)
    lower_rows = jnp.stack([sine_table, cosine_table], axis=1)
    return jnp.stack([upper_rows, lower_rows], axis=0)


def filter_window():
    sample_index = jnp.arange(TAPS * NCHAN, dtype=jnp.float32)
    centred = (sample_index - TAPS * NCHAN / 2 + 0.5) / NCHAN
    taper_curve = 0.5 - 0.5 * jnp.cos(full_turn * (sample_index + 0.5) / (TAPS * NCHAN))
    shaped_window = (jnp.sinc(centred) * taper_curve).reshape(TAPS, NCHAN)
    energy = jnp.mean(jnp.sum(shaped_window * shaped_window, axis=0))
    return shaped_window / jnp.sqrt(energy)


def beam_tables(grid_rows, grid_len, rows_per_device):
    positions = jnp.arange(grid_len, dtype=jnp.int32)
    cosine_base, sine_base = table_constant(grid_len, grid_len, grid_len, 1.0 / math.sqrt(grid_len))
    cosine_base = jnp.asarray(cosine_base)
    sine_base = jnp.asarray(sine_base)
    devices = grid_len // rows_per_device
    picks = (positions[None, :, None] == grid_rows[:, None, :]).astype(jnp.bfloat16)
    cosine_table = jnp.einsum(
        "jg,dgm->djm", cosine_base, picks, preferred_element_type=jnp.float32
    ).astype(jnp.bfloat16)
    sine_table = jnp.einsum(
        "jg,dgm->djm", sine_base, picks, preferred_element_type=jnp.float32
    ).astype(jnp.bfloat16)
    shape = (grid_rows.shape[0], grid_len, devices, 1, rows_per_device)
    cosine_table = cosine_table.reshape(shape)
    sine_table = sine_table.reshape(shape)
    real_rows = jnp.concatenate([cosine_table, sine_table], axis=3)
    imag_rows = jnp.concatenate([-sine_table, cosine_table], axis=3)
    rows = jnp.concatenate([real_rows, imag_rows], axis=1)
    return rows.reshape(grid_rows.shape[0], 2 * grid_len, 2 * grid_len)


def channelize_kernel(first_pair, pairs, v_ref, w_ref, t1_ref, tw_ref, t2_ref, g_ref, o_ref):
    cos_tw = tw_ref[0]
    sin_tw = tw_ref[1]
    t1 = t1_ref[...]
    t2_real = t2_ref[0]
    t2_imag = t2_ref[1]
    g_real = g_ref[0, 0]
    g_imag = g_ref[0, 1]
    half = t2_real.shape[0] // 2

    def one_frame(pieces):
        acc = None
        for tap in range(TAPS):
            term = w_ref[tap][None] * pieces[tap]
            acc = term if acc is None else acc + term
        block = acc.astype(jnp.bfloat16).reshape(2 * CHA, CHB)
        section = jnp.dot(t1, block, preferred_element_type=jnp.float32)
        sec_real = section[:CHA]
        sec_imag = section[CHA:]
        turned_real = sec_real * cos_tw - sec_imag * sin_tw
        turned_imag = sec_real * sin_tw + sec_imag * cos_tw
        return turned_real.astype(jnp.bfloat16), turned_imag.astype(jnp.bfloat16)

    def pair(step, carry):
        pieces = []
        for offset in range(TAPS + 1):
            start = pl.multiple_of((2 * (step - first_pair) + offset) * CHA, CHA)
            pieces.append(v_ref[0, :, pl.ds(start, CHA), :].astype(jnp.float32))
        first_real, first_imag = one_frame(pieces[:TAPS])
        second_real, second_imag = one_frame(pieces[1:])
        both_real = jnp.concatenate([first_real, second_real], axis=0)
        both_imag = jnp.concatenate([first_imag, second_imag], axis=0)
        dims = (((1,), (1,)), ((), ()))
        spectrum = lax.dot_general(
            t2_real, both_real, dims, preferred_element_type=jnp.float32
        ) + lax.dot_general(t2_imag, both_imag, dims, preferred_element_type=jnp.float32)
        spec_real = spectrum[:half]
        spec_imag = spectrum[half:]
        out_real = spec_real * g_real - spec_imag * g_imag
        out_imag = spec_real * g_imag + spec_imag * g_real
        lanes = pl.ds(pl.multiple_of((step - first_pair) * 2 * CHA, 2 * CHA), 2 * CHA)
        o_ref[0, 0, :, lanes] = out_real.astype(o_ref.dtype)
        o_ref[1, 0, :, lanes] = out_imag.astype(o_ref.dtype)
        return carry

    lax.fori_loop(first_pair, first_pair + pairs, pair, 0, unroll=True)


def beam_kernel(dish_count, carry_in, finish, *refs):
    if carry_in:
        x_ref, t_ref, c_ref, s_ref, init_ref, o_ref, acc_ref = refs
    else:
        x_ref, t_ref, c_ref, s_ref, o_ref, acc_ref = refs
    step = pl.program_id(0)
    devices = x_ref.shape[0] // dish_count
    rows = x_ref.shape[2]
    grid_len = t_ref.shape[1] // 2
    lanes = x_ref.shape[3]

    @pl.when(step == 0)
    def _():
        if carry_in:
            acc_ref[...] = init_ref[...]
        else:
            acc_ref[...] = jnp.zeros_like(acc_ref)

    parts = []
    for d in range(dish_count):
        block = x_ref[pl.ds(d * devices, devices)].reshape(2 * rows * devices, lanes)
        sums = jnp.dot(t_ref[d], block, preferred_element_type=jnp.float32)
        sum_real = sums[:grid_len]
        sum_imag = sums[grid_len:]
        cos_d = c_ref[d]
        sin_d = s_ref[d]
        part_real = sum_real * cos_d - sum_imag * sin_d
        part_imag = sum_real * sin_d + sum_imag * cos_d
        parts.append(
            (
                part_real.astype(jnp.bfloat16).astype(jnp.float32),
                part_imag.astype(jnp.bfloat16).astype(jnp.float32),
            )
        )
    (a_re, a_im), (b_re, b_im), (c_re, c_im), (d_re, d_im) = parts
    beams = [
        (a_re + b_re + c_re + d_re, a_im + b_im + c_im + d_im),
        (a_re + b_im - c_re - d_im, a_im - b_re - c_im + d_re),
        (a_re - b_re + c_re - d_re, a_im - b_im + c_im - d_im),
        (a_re - b_im - c_re + d_im, a_im + b_re - c_im - d_re),
    ]
    for q in range(dish_count):
        beam_real, beam_imag = beams[q]
        acc_ref[q] += beam_real * beam_real + beam_imag * beam_imag

    @pl.when(step == pl.num_programs(0) - 1)
    def _():
        if not finish:
            o_ref[...] = acc_ref[...]
            return
        me = lax.axis_index("dish")
        width = o_ref.shape[1]
        for shift in range(dish_count):
            target = jnp.bitwise_xor(me, shift)
            beam_index = jnp.bitwise_or(
                jnp.left_shift(jnp.bitwise_and(target, 1), 1), jnp.right_shift(target, 1)
            )
            total = acc_ref[beam_index]
            folded = total[:, :CHB]
            for k in range(1, lanes // CHB):
                folded = folded + total[:, k * CHB : (k + 1) * CHB]
            folded = folded + pltpu.roll(folded, width, 1)
            flipped = jnp.transpose(folded, (1, 0))
            o_ref[shift] = flipped[:width] * (0.25 / FRAMES)


def body(voltages, feed_gains, block_assign, grid_rows):
    dish_rows = voltages.shape[0]
    block_count = lax.axis_size("freq")
    dish_count = lax.axis_size("dish")
    block_width = NCHAN // block_count
    quarter = block_width // dish_count
    dests = block_count * dish_count
    grid_len = dish_rows * block_count
    total_dishes = grid_len * dish_count
    samples = voltages.shape[-1]

    dest = jnp.arange(dests, dtype=jnp.int32)
    dest_quarter = dest // block_count
    dest_block = jnp.tile(block_assign, dish_count)
    dest_e = dest_block * dish_count + dest_quarter
    picks_e = (dest_e[:, None] == jnp.arange(dests, dtype=jnp.int32)[None, :]).astype(jnp.bfloat16)

    window = jnp.asarray(window_constant().reshape(TAPS, CHA, CHB))
    first_cos, first_sin = table_constant(CHA, CHA, CHA, 1.0 / math.sqrt(CHA))
    first_table = np.block([[first_cos, first_sin], [-first_sin, first_cos]])
    first_table = jnp.asarray(first_table)
    twiddle = jnp.asarray(np.stack(rotation_constant(CHA, CHB, NCHAN), axis=0))
    second_cos, second_sin = table_constant(CHB, CHB, CHB, 1.0 / math.sqrt(CHB))
    second_table = np.stack(
        [np.stack([second_cos, -second_sin], axis=0), np.stack([second_sin, second_cos], axis=0)],
        axis=0,
    )
    second_table = jnp.einsum(
        "je,qseb->qsjb", picks_e, jnp.asarray(second_table), preferred_element_type=jnp.float32
    ).astype(jnp.bfloat16).reshape(2, 2 * dests, CHB)
    gains = feed_gains[:, 0].reshape(dish_rows, 2, CHB, CHA)
    gains = jnp.einsum("je,rpec->rpjc", picks_e, gains, preferred_element_type=jnp.float32)
    gains = jnp.concatenate([gains, gains], axis=3)

    chunk_pairs = [2, 6]
    chunks = len(chunk_pairs)
    tables = beam_tables(grid_rows, grid_len, dish_rows)
    feed_index = jnp.arange(dish_count, dtype=jnp.int32)
    positions = jnp.arange(grid_len, dtype=jnp.int32)
    twist_cos, twist_sin = rotation_constant(dish_count, grid_len, total_dishes)
    twist_cos = jnp.asarray(twist_cos[:, :, None])
    twist_sin = jnp.asarray(twist_sin[:, :, None])
    lane_block = 4 * quarter

    volts = voltages[:, 0].reshape(dish_rows, 2, samples // CHB, CHB)

    def channelize_chunk(chunk):
        pairs = chunk_pairs[chunk]
        first_pair = sum(chunk_pairs[:chunk])
        chunk_lanes = pairs * 2 * quarter
        span = (2 * pairs + TAPS - 1) * CHA
        first_row = 2 * first_pair * CHA
        return pl.pallas_call(
            functools.partial(channelize_kernel, first_pair, pairs),
            grid=(dish_rows,),
            in_specs=[
                pl.BlockSpec(
                    (pl.Element(1), pl.Element(2), pl.Element(span), pl.Element(CHB)),
                    lambda r: (r, 0, first_row, 0),
                ),
                pl.BlockSpec((TAPS, CHA, CHB), lambda r: (0, 0, 0)),
                pl.BlockSpec((2 * CHA, 2 * CHA), lambda r: (0, 0)),
                pl.BlockSpec((2, CHA, CHB), lambda r: (0, 0, 0)),
                pl.BlockSpec((2, 2 * dests, CHB), lambda r: (0, 0, 0)),
                pl.BlockSpec((1, 2, dests, 2 * CHA), lambda r: (r, 0, 0, 0)),
            ],
            out_specs=pl.BlockSpec((2, 1, dests, chunk_lanes), lambda r: (0, r, 0, 0)),
            out_shape=jax.ShapeDtypeStruct((2, dish_rows, dests, chunk_lanes), jnp.bfloat16),
            cost_estimate=pl.CostEstimate(
                flops=int(dish_rows * pairs * 2 * 2 * 128 * 128 * 128 * 3),
                bytes_accessed=int(voltages.size * 2 + 2 * dish_rows * dests * chunk_lanes * 2),
                transcendentals=0,
            ),
        )(volts, window, first_table, twiddle, second_table, gains)

    def beamform_chunk(received, carried, finish):
        carry_in = carried is not None
        chunk_lanes = received.shape[3]
        in_specs = [
            pl.BlockSpec((dests, 2, dish_rows, lane_block), lambda f: (0, 0, 0, f)),
            pl.BlockSpec((dish_count, 2 * grid_len, 2 * grid_len), lambda f: (0, 0, 0)),
            pl.BlockSpec((dish_count, grid_len, 1), lambda f: (0, 0, 0)),
            pl.BlockSpec((dish_count, grid_len, 1), lambda f: (0, 0, 0)),
        ]
        operands = [received, tables, twist_cos, twist_sin]
        if carry_in:
            in_specs.append(pl.BlockSpec((dish_count, grid_len, lane_block), lambda f: (0, 0, 0)))
            operands.append(carried)
        if finish:
            out_shape = (dish_count, quarter, grid_len)
        else:
            out_shape = (dish_count, grid_len, lane_block)
        return pl.pallas_call(
            functools.partial(beam_kernel, dish_count, carry_in, finish),
            grid=(chunk_lanes // lane_block,),
            in_specs=in_specs,
            out_specs=pl.BlockSpec(out_shape, lambda f: (0, 0, 0)),
            out_shape=jax.ShapeDtypeStruct(out_shape, jnp.float32),
            scratch_shapes=[pltpu.VMEM((dish_count, grid_len, lane_block), jnp.float32)],
            cost_estimate=pl.CostEstimate(
                flops=int(dish_count * 2 * 512 * 512 * chunk_lanes),
                bytes_accessed=int(received.size * 2 + tables.size * 2),
                transcendentals=0,
            ),
        )(*operands)

    sent = [channelize_chunk(c) for c in range(chunks)]
    arrived = [
        jnp.transpose(lax.all_to_all(s, ("dish", "freq"), 2, 2, tiled=True), (2, 0, 1, 3))
        for s in sent
    ]
    carried = None
    for c in range(chunks):
        carried = beamform_chunk(arrived[c], carried, c == chunks - 1)
    powers = carried

    me = lax.axis_index("dish")
    pieces = [powers[0]]
    for shift in range(1, dish_count):
        outgoing = powers[shift]
        pairs_list = [(i, i ^ shift) for i in range(dish_count)]
        pieces.append(lax.ppermute(outgoing, "dish", pairs_list))
    stacked = jnp.stack(pieces, axis=0)
    order = jnp.arange(dish_count, dtype=jnp.int32) ^ me
    received = jnp.take(stacked, order, axis=0)
    return received.reshape(block_width, grid_len)


def solution(mesh):
    placed = (P("freq", "dish", None, None), P("freq", "dish", None, None), P(), P())
    return jax.shard_map(
        body, mesh=mesh, in_specs=placed, out_specs=P("freq", "dish"), check_vma=False
    )
```

```python
import functools
import math

import jax
import jax.numpy as jnp
import ml_dtypes
import numpy as np
from jax import lax
from jax.experimental import pallas as pl
from jax.experimental.pallas import tpu as pltpu
from jax.sharding import PartitionSpec as P

NCHAN = 8192
CHA = 64
CHB = 128
TAPS = 4
FRAMES = 16
FEEDS_PER_STEP = 2


full_turn = 2.0 * math.pi


def table_constant(row_count, col_count, modulus, scaling):
    rows = np.arange(row_count, dtype=np.int64)[:, None]
    cols = np.arange(col_count, dtype=np.int64)[None, :]
    angles = np.float32(full_turn / modulus) * (rows * cols % modulus).astype(np.float32)
    cosine = (np.cos(angles.astype(np.float64)) * scaling).astype(ml_dtypes.bfloat16)
    sine = (np.sin(angles.astype(np.float64)) * scaling).astype(ml_dtypes.bfloat16)
    return cosine, sine


def window_constant():
    sample_index = np.arange(TAPS * NCHAN, dtype=np.float64)
    centred = (sample_index - TAPS * NCHAN / 2 + 0.5) / NCHAN
    taper_curve = 0.5 - 0.5 * np.cos(full_turn * (sample_index + 0.5) / (TAPS * NCHAN))
    shaped_window = (np.sinc(centred) * taper_curve).reshape(TAPS, NCHAN)
    energy = np.mean(np.sum(shaped_window * shaped_window, axis=0))
    return (shaped_window / np.sqrt(energy)).astype(np.float32)


def rotation_constant(row_count, col_count, modulus):
    rows = np.arange(row_count, dtype=np.int64)[:, None]
    cols = np.arange(col_count, dtype=np.int64)[None, :]
    angles = np.float32(-(full_turn / modulus)) * (rows * cols % modulus).astype(np.float32)
    angles = angles.astype(np.float64)
    return np.cos(angles).astype(np.float32), np.sin(angles).astype(np.float32)


def fourier_table(row_index, col_index, modulus, scaling):
    phases = row_index[:, None] * col_index[None, :] % modulus
    angles = full_turn / modulus * phases.astype(jnp.float32)
    cosine_table = (jnp.cos(angles) * scaling).astype(jnp.bfloat16)
    sine_table = (jnp.sin(angles) * scaling).astype(jnp.bfloat16)
    upper_rows = jnp.stack([cosine_table, -sine_table], axis=1)
    lower_rows = jnp.stack([sine_table, cosine_table], axis=1)
    return jnp.stack([upper_rows, lower_rows], axis=0)


def filter_window():
    sample_index = jnp.arange(TAPS * NCHAN, dtype=jnp.float32)
    centred = (sample_index - TAPS * NCHAN / 2 + 0.5) / NCHAN
    taper_curve = 0.5 - 0.5 * jnp.cos(full_turn * (sample_index + 0.5) / (TAPS * NCHAN))
    shaped_window = (jnp.sinc(centred) * taper_curve).reshape(TAPS, NCHAN)
    energy = jnp.mean(jnp.sum(shaped_window * shaped_window, axis=0))
    return shaped_window / jnp.sqrt(energy)


def beam_tables(grid_rows, grid_len, rows_per_device):
    positions = jnp.arange(grid_len, dtype=jnp.int32)
    cosine_base, sine_base = table_constant(grid_len, grid_len, grid_len, 1.0 / math.sqrt(grid_len))
    cosine_base = jnp.asarray(cosine_base)
    sine_base = jnp.asarray(sine_base)
    devices = grid_len // rows_per_device
    picks = (positions[None, :, None] == grid_rows[:, None, :]).astype(jnp.bfloat16)
    cosine_table = jnp.einsum(
        "jg,dgm->djm", cosine_base, picks, preferred_element_type=jnp.float32
    ).astype(jnp.bfloat16)
    sine_table = jnp.einsum(
        "jg,dgm->djm", sine_base, picks, preferred_element_type=jnp.float32
    ).astype(jnp.bfloat16)
    shape = (grid_rows.shape[0], grid_len, devices, 1, rows_per_device)
    cosine_table = cosine_table.reshape(shape)
    sine_table = sine_table.reshape(shape)
    real_rows = jnp.concatenate([cosine_table, sine_table], axis=3)
    imag_rows = jnp.concatenate([-sine_table, cosine_table], axis=3)
    rows = jnp.concatenate([real_rows, imag_rows], axis=1)
    return rows.reshape(grid_rows.shape[0], 2 * grid_len, 2 * grid_len)


def channelize_kernel(first_pair, pairs, v_ref, w_ref, t1_ref, tw_ref, t2_ref, g_ref, o_ref):
    cos_tw = tw_ref[0]
    sin_tw = tw_ref[1]
    t1 = t1_ref[...]
    t2_real = t2_ref[0]
    t2_imag = t2_ref[1]
    half = t2_real.shape[0] // 2
    feeds = v_ref.shape[0]

    def one_frame(pieces):
        acc = None
        for tap in range(TAPS):
            term = w_ref[tap][None] * pieces[tap]
            acc = term if acc is None else acc + term
        block = acc.astype(jnp.bfloat16).reshape(2 * CHA, CHB)
        section = jnp.dot(t1, block, preferred_element_type=jnp.float32)
        sec_real = section[:CHA]
        sec_imag = section[CHA:]
        turned_real = sec_real * cos_tw - sec_imag * sin_tw
        turned_imag = sec_real * sin_tw + sec_imag * cos_tw
        return turned_real.astype(jnp.bfloat16), turned_imag.astype(jnp.bfloat16)

    def pair(feed, step):
        g_real = g_ref[feed, 0].astype(jnp.float32)
        g_imag = g_ref[feed, 1].astype(jnp.float32)
        pieces = []
        for offset in range(TAPS + 1):
            start = pl.multiple_of((2 * (step - first_pair) + offset) * CHA, CHA)
            pieces.append(v_ref[feed, :, pl.ds(start, CHA), :].astype(jnp.float32))
        first_real, first_imag = one_frame(pieces[:TAPS])
        second_real, second_imag = one_frame(pieces[1:])
        both_real = jnp.concatenate([first_real, second_real], axis=0)
        both_imag = jnp.concatenate([first_imag, second_imag], axis=0)
        dims = (((1,), (1,)), ((), ()))
        spectrum = lax.dot_general(
            t2_real, both_real, dims, preferred_element_type=jnp.float32
        ) + lax.dot_general(t2_imag, both_imag, dims, preferred_element_type=jnp.float32)
        spec_real = spectrum[:half]
        spec_imag = spectrum[half:]
        out_real = spec_real * g_real - spec_imag * g_imag
        out_imag = spec_real * g_imag + spec_imag * g_real
        lanes = pl.ds(pl.multiple_of((step - first_pair) * 2 * CHA, 2 * CHA), 2 * CHA)
        o_ref[0, feed, :, lanes] = out_real.astype(o_ref.dtype)
        o_ref[1, feed, :, lanes] = out_imag.astype(o_ref.dtype)

    for feed in range(feeds):
        for step in range(first_pair, first_pair + pairs):
            pair(feed, step)


def beam_kernel(dish_count, carry_in, finish, *refs):
    if carry_in:
        x_ref, t_ref, c_ref, s_ref, init_ref, o_ref, acc_ref = refs
    else:
        x_ref, t_ref, c_ref, s_ref, o_ref, acc_ref = refs
    step = pl.program_id(0)
    devices = x_ref.shape[0] // dish_count
    rows = x_ref.shape[2]
    grid_len = t_ref.shape[1] // 2
    lanes = x_ref.shape[3]

    @pl.when(step == 0)
    def _():
        if carry_in:
            acc_ref[...] = init_ref[...]
        else:
            acc_ref[...] = jnp.zeros_like(acc_ref)

    parts = []
    for d in range(dish_count):
        block = x_ref[pl.ds(d * devices, devices)].reshape(2 * rows * devices, lanes)
        sums = jnp.dot(t_ref[d], block, preferred_element_type=jnp.float32)
        sum_real = sums[:grid_len]
        sum_imag = sums[grid_len:]
        cos_d = c_ref[d]
        sin_d = s_ref[d]
        part_real = sum_real * cos_d - sum_imag * sin_d
        part_imag = sum_real * sin_d + sum_imag * cos_d
        parts.append(
            (
                part_real.astype(jnp.bfloat16).astype(jnp.float32),
                part_imag.astype(jnp.bfloat16).astype(jnp.float32),
            )
        )
    (a_re, a_im), (b_re, b_im), (c_re, c_im), (d_re, d_im) = parts
    beams = [
        (a_re + b_re + c_re + d_re, a_im + b_im + c_im + d_im),
        (a_re + b_im - c_re - d_im, a_im - b_re - c_im + d_re),
        (a_re - b_re + c_re - d_re, a_im - b_im + c_im - d_im),
        (a_re - b_im - c_re + d_im, a_im + b_re - c_im - d_re),
    ]
    for q in range(dish_count):
        beam_real, beam_imag = beams[q]
        acc_ref[q] += beam_real * beam_real + beam_imag * beam_imag

    @pl.when(step == pl.num_programs(0) - 1)
    def _():
        if not finish:
            o_ref[...] = acc_ref[...]
            return
        me = lax.axis_index("dish")
        width = o_ref.shape[1]
        for shift in range(dish_count):
            target = jnp.bitwise_xor(me, shift)
            beam_index = jnp.bitwise_or(
                jnp.left_shift(jnp.bitwise_and(target, 1), 1), jnp.right_shift(target, 1)
            )
            total = acc_ref[beam_index]
            folded = total[:, :CHB]
            for k in range(1, lanes // CHB):
                folded = folded + total[:, k * CHB : (k + 1) * CHB]
            folded = folded + pltpu.roll(folded, width, 1)
            flipped = jnp.transpose(folded, (1, 0))
            o_ref[shift] = flipped[:width] * (0.25 / FRAMES)


def body(voltages, feed_gains, block_assign, grid_rows):
    dish_rows = voltages.shape[0]
    block_count = lax.axis_size("freq")
    dish_count = lax.axis_size("dish")
    block_width = NCHAN // block_count
    quarter = block_width // dish_count
    dests = block_count * dish_count
    grid_len = dish_rows * block_count
    total_dishes = grid_len * dish_count
    samples = voltages.shape[-1]

    dest = jnp.arange(dests, dtype=jnp.int32)
    dest_quarter = dest // block_count
    dest_block = jnp.tile(block_assign, dish_count)
    dest_e = dest_block * dish_count + dest_quarter
    picks_e = (dest_e[:, None] == jnp.arange(dests, dtype=jnp.int32)[None, :]).astype(jnp.bfloat16)

    window = jnp.asarray(window_constant().reshape(TAPS, CHA, CHB))
    first_cos, first_sin = table_constant(CHA, CHA, CHA, 1.0 / math.sqrt(CHA))
    first_table = np.block([[first_cos, first_sin], [-first_sin, first_cos]])
    first_table = jnp.asarray(first_table)
    twiddle = jnp.asarray(np.stack(rotation_constant(CHA, CHB, NCHAN), axis=0))
    second_cos, second_sin = table_constant(CHB, CHB, CHB, 1.0 / math.sqrt(CHB))
    second_table = np.stack(
        [np.stack([second_cos, -second_sin], axis=0), np.stack([second_sin, second_cos], axis=0)],
        axis=0,
    )
    second_table = jnp.einsum(
        "je,qseb->qsjb", picks_e, jnp.asarray(second_table), preferred_element_type=jnp.float32
    ).astype(jnp.bfloat16).reshape(2, 2 * dests, CHB)
    gains = feed_gains[:, 0].reshape(dish_rows, 2, CHB, CHA)
    gains = jnp.einsum("je,rpec->rpjc", picks_e, gains, preferred_element_type=jnp.float32)
    gains = jnp.concatenate([gains, gains], axis=3).astype(jnp.bfloat16)

    chunk_pairs = [4, 4]
    chunks = len(chunk_pairs)
    tables = beam_tables(grid_rows, grid_len, dish_rows)
    feed_index = jnp.arange(dish_count, dtype=jnp.int32)
    positions = jnp.arange(grid_len, dtype=jnp.int32)
    twist_cos, twist_sin = rotation_constant(dish_count, grid_len, total_dishes)
    twist_cos = jnp.asarray(twist_cos[:, :, None])
    twist_sin = jnp.asarray(twist_sin[:, :, None])
    lane_block = 4 * quarter

    volts = voltages[:, 0].reshape(dish_rows, 2, samples // CHB, CHB)

    def channelize_chunk(chunk):
        pairs = chunk_pairs[chunk]
        first_pair = sum(chunk_pairs[:chunk])
        chunk_lanes = pairs * 2 * quarter
        span = (2 * pairs + TAPS - 1) * CHA
        first_row = 2 * first_pair * CHA
        return pl.pallas_call(
            functools.partial(channelize_kernel, first_pair, pairs),
            grid=(dish_rows // FEEDS_PER_STEP,),
            in_specs=[
                pl.BlockSpec(
                    (pl.Element(FEEDS_PER_STEP), pl.Element(2), pl.Element(span), pl.Element(CHB)),
                    lambda r: (r * FEEDS_PER_STEP, 0, first_row, 0),
                ),
                pl.BlockSpec((TAPS, CHA, CHB), lambda r: (0, 0, 0)),
                pl.BlockSpec((2 * CHA, 2 * CHA), lambda r: (0, 0)),
                pl.BlockSpec((2, CHA, CHB), lambda r: (0, 0, 0)),
                pl.BlockSpec((2, 2 * dests, CHB), lambda r: (0, 0, 0)),
                pl.BlockSpec((FEEDS_PER_STEP, 2, dests, 2 * CHA), lambda r: (r, 0, 0, 0)),
            ],
            out_specs=pl.BlockSpec((2, FEEDS_PER_STEP, dests, chunk_lanes), lambda r: (0, r, 0, 0)),
            out_shape=jax.ShapeDtypeStruct((2, dish_rows, dests, chunk_lanes), jnp.bfloat16),
            cost_estimate=pl.CostEstimate(
                flops=int(dish_rows * pairs * 2 * 2 * 128 * 128 * 128 * 3),
                bytes_accessed=int(voltages.size * 2 + 2 * dish_rows * dests * chunk_lanes * 2),
                transcendentals=0,
            ),
        )(volts, window, first_table, twiddle, second_table, gains)

    def beamform_chunk(received, carried, finish):
        carry_in = carried is not None
        chunk_lanes = received.shape[3]
        in_specs = [
            pl.BlockSpec((dests, 2, dish_rows, lane_block), lambda f: (0, 0, 0, f)),
            pl.BlockSpec((dish_count, 2 * grid_len, 2 * grid_len), lambda f: (0, 0, 0)),
            pl.BlockSpec((dish_count, grid_len, 1), lambda f: (0, 0, 0)),
            pl.BlockSpec((dish_count, grid_len, 1), lambda f: (0, 0, 0)),
        ]
        operands = [received, tables, twist_cos, twist_sin]
        if carry_in:
            in_specs.append(pl.BlockSpec((dish_count, grid_len, lane_block), lambda f: (0, 0, 0)))
            operands.append(carried)
        if finish:
            out_shape = (dish_count, quarter, grid_len)
        else:
            out_shape = (dish_count, grid_len, lane_block)
        return pl.pallas_call(
            functools.partial(beam_kernel, dish_count, carry_in, finish),
            grid=(chunk_lanes // lane_block,),
            in_specs=in_specs,
            out_specs=pl.BlockSpec(out_shape, lambda f: (0, 0, 0)),
            out_shape=jax.ShapeDtypeStruct(out_shape, jnp.float32),
            scratch_shapes=[pltpu.VMEM((dish_count, grid_len, lane_block), jnp.float32)],
            cost_estimate=pl.CostEstimate(
                flops=int(dish_count * 2 * 512 * 512 * chunk_lanes),
                bytes_accessed=int(received.size * 2 + tables.size * 2),
                transcendentals=0,
            ),
        )(*operands)

    sent = [channelize_chunk(c) for c in range(chunks)]
    arrived = [
        jnp.transpose(lax.all_to_all(s, ("dish", "freq"), 2, 2, tiled=True), (2, 0, 1, 3))
        for s in sent
    ]
    carried = None
    for c in range(chunks):
        carried = beamform_chunk(arrived[c], carried, c == chunks - 1)
    powers = carried

    me = lax.axis_index("dish")
    pieces = [powers[0]]
    for shift in range(1, dish_count):
        outgoing = powers[shift]
        pairs_list = [(i, i ^ shift) for i in range(dish_count)]
        pieces.append(lax.ppermute(outgoing, "dish", pairs_list))
    stacked = jnp.stack(pieces, axis=0)
    order = jnp.arange(dish_count, dtype=jnp.int32) ^ me
    received = jnp.take(stacked, order, axis=0)
    return received.reshape(block_width, grid_len)


def solution(mesh):
    placed = (P("freq", "dish", None, None), P("freq", "dish", None, None), P(), P())
    return jax.shard_map(
        body, mesh=mesh, in_specs=placed, out_specs=P("freq", "dish"), check_vma=False
    )
```

```python
import functools
import math

import jax
import jax.numpy as jnp
import ml_dtypes
import numpy as np
from jax import lax
from jax.experimental import pallas as pl
from jax.experimental.pallas import tpu as pltpu
from jax.sharding import PartitionSpec as P

NCHAN = 8192
CHA = 64
CHB = 128
TAPS = 4
FRAMES = 16
FEEDS_PER_STEP = 4


full_turn = 2.0 * math.pi


def table_constant(row_count, col_count, modulus, scaling):
    rows = np.arange(row_count, dtype=np.int64)[:, None]
    cols = np.arange(col_count, dtype=np.int64)[None, :]
    angles = np.float32(full_turn / modulus) * (rows * cols % modulus).astype(np.float32)
    cosine = (np.cos(angles.astype(np.float64)) * scaling).astype(ml_dtypes.bfloat16)
    sine = (np.sin(angles.astype(np.float64)) * scaling).astype(ml_dtypes.bfloat16)
    return cosine, sine


def window_constant():
    sample_index = np.arange(TAPS * NCHAN, dtype=np.float64)
    centred = (sample_index - TAPS * NCHAN / 2 + 0.5) / NCHAN
    taper_curve = 0.5 - 0.5 * np.cos(full_turn * (sample_index + 0.5) / (TAPS * NCHAN))
    shaped_window = (np.sinc(centred) * taper_curve).reshape(TAPS, NCHAN)
    energy = np.mean(np.sum(shaped_window * shaped_window, axis=0))
    return (shaped_window / np.sqrt(energy)).astype(np.float32)


def rotation_constant(row_count, col_count, modulus):
    rows = np.arange(row_count, dtype=np.int64)[:, None]
    cols = np.arange(col_count, dtype=np.int64)[None, :]
    angles = np.float32(-(full_turn / modulus)) * (rows * cols % modulus).astype(np.float32)
    angles = angles.astype(np.float64)
    return np.cos(angles).astype(np.float32), np.sin(angles).astype(np.float32)


def fourier_table(row_index, col_index, modulus, scaling):
    phases = row_index[:, None] * col_index[None, :] % modulus
    angles = full_turn / modulus * phases.astype(jnp.float32)
    cosine_table = (jnp.cos(angles) * scaling).astype(jnp.bfloat16)
    sine_table = (jnp.sin(angles) * scaling).astype(jnp.bfloat16)
    upper_rows = jnp.stack([cosine_table, -sine_table], axis=1)
    lower_rows = jnp.stack([sine_table, cosine_table], axis=1)
    return jnp.stack([upper_rows, lower_rows], axis=0)


def filter_window():
    sample_index = jnp.arange(TAPS * NCHAN, dtype=jnp.float32)
    centred = (sample_index - TAPS * NCHAN / 2 + 0.5) / NCHAN
    taper_curve = 0.5 - 0.5 * jnp.cos(full_turn * (sample_index + 0.5) / (TAPS * NCHAN))
    shaped_window = (jnp.sinc(centred) * taper_curve).reshape(TAPS, NCHAN)
    energy = jnp.mean(jnp.sum(shaped_window * shaped_window, axis=0))
    return shaped_window / jnp.sqrt(energy)


def beam_tables(grid_rows, grid_len, rows_per_device):
    positions = jnp.arange(grid_len, dtype=jnp.int32)
    cosine_base, sine_base = table_constant(grid_len, grid_len, grid_len, 1.0 / math.sqrt(grid_len))
    cosine_base = jnp.asarray(cosine_base)
    sine_base = jnp.asarray(sine_base)
    devices = grid_len // rows_per_device
    picks = (positions[None, :, None] == grid_rows[:, None, :]).astype(jnp.bfloat16)
    cosine_table = jnp.einsum(
        "jg,dgm->djm", cosine_base, picks, preferred_element_type=jnp.float32
    ).astype(jnp.bfloat16)
    sine_table = jnp.einsum(
        "jg,dgm->djm", sine_base, picks, preferred_element_type=jnp.float32
    ).astype(jnp.bfloat16)
    shape = (grid_rows.shape[0], grid_len, devices, 1, rows_per_device)
    cosine_table = cosine_table.reshape(shape)
    sine_table = sine_table.reshape(shape)
    real_rows = jnp.concatenate([cosine_table, sine_table], axis=3)
    imag_rows = jnp.concatenate([-sine_table, cosine_table], axis=3)
    rows = jnp.concatenate([real_rows, imag_rows], axis=1)
    return rows.reshape(grid_rows.shape[0], 2 * grid_len, 2 * grid_len)


def channelize_kernel(first_pair, pairs, v_ref, w_ref, t1_ref, tw_ref, t2_ref, g_ref, o_ref):
    cos_tw = tw_ref[0]
    sin_tw = tw_ref[1]
    t1 = t1_ref[...]
    t2_real = t2_ref[0]
    t2_imag = t2_ref[1]
    half = t2_real.shape[0] // 2
    feeds = v_ref.shape[0]

    def one_frame(pieces):
        acc = None
        for tap in range(TAPS):
            term = w_ref[tap][None] * pieces[tap]
            acc = term if acc is None else acc + term
        block = acc.astype(jnp.bfloat16).reshape(2 * CHA, CHB)
        section = jnp.dot(t1, block, preferred_element_type=jnp.float32)
        sec_real = section[:CHA]
        sec_imag = section[CHA:]
        turned_real = sec_real * cos_tw - sec_imag * sin_tw
        turned_imag = sec_real * sin_tw + sec_imag * cos_tw
        return turned_real.astype(jnp.bfloat16), turned_imag.astype(jnp.bfloat16)

    def pair(feed, step):
        g_real = g_ref[feed, 0].astype(jnp.float32)
        g_imag = g_ref[feed, 1].astype(jnp.float32)
        pieces = []
        for offset in range(TAPS + 1):
            start = pl.multiple_of((2 * (step - first_pair) + offset) * CHA, CHA)
            pieces.append(v_ref[feed, :, pl.ds(start, CHA), :].astype(jnp.float32))
        first_real, first_imag = one_frame(pieces[:TAPS])
        second_real, second_imag = one_frame(pieces[1:])
        both_real = jnp.concatenate([first_real, second_real], axis=0)
        both_imag = jnp.concatenate([first_imag, second_imag], axis=0)
        dims = (((1,), (1,)), ((), ()))
        spectrum = lax.dot_general(
            t2_real, both_real, dims, preferred_element_type=jnp.float32
        ) + lax.dot_general(t2_imag, both_imag, dims, preferred_element_type=jnp.float32)
        spec_real = spectrum[:half]
        spec_imag = spectrum[half:]
        out_real = spec_real * g_real - spec_imag * g_imag
        out_imag = spec_real * g_imag + spec_imag * g_real
        lanes = pl.ds(pl.multiple_of((step - first_pair) * 2 * CHA, 2 * CHA), 2 * CHA)
        o_ref[0, feed, :, lanes] = out_real.astype(o_ref.dtype)
        o_ref[1, feed, :, lanes] = out_imag.astype(o_ref.dtype)

    for feed in range(feeds):
        for step in range(first_pair, first_pair + pairs):
            pair(feed, step)


def beam_kernel(dish_count, carry_in, finish, *refs):
    if carry_in:
        x_ref, t_ref, c_ref, s_ref, init_ref, o_ref, acc_ref = refs
    else:
        x_ref, t_ref, c_ref, s_ref, o_ref, acc_ref = refs
    step = pl.program_id(0)
    devices = x_ref.shape[0] // dish_count
    rows = x_ref.shape[2]
    grid_len = t_ref.shape[1] // 2
    lanes = x_ref.shape[3]

    @pl.when(step == 0)
    def _():
        if carry_in:
            acc_ref[...] = init_ref[...]
        else:
            acc_ref[...] = jnp.zeros_like(acc_ref)

    parts = []
    for d in range(dish_count):
        block = x_ref[pl.ds(d * devices, devices)].reshape(2 * rows * devices, lanes)
        sums = jnp.dot(t_ref[d], block, preferred_element_type=jnp.float32)
        sum_real = sums[:grid_len]
        sum_imag = sums[grid_len:]
        cos_d = c_ref[d]
        sin_d = s_ref[d]
        part_real = sum_real * cos_d - sum_imag * sin_d
        part_imag = sum_real * sin_d + sum_imag * cos_d
        parts.append(
            (
                part_real.astype(jnp.bfloat16).astype(jnp.float32),
                part_imag.astype(jnp.bfloat16).astype(jnp.float32),
            )
        )
    (a_re, a_im), (b_re, b_im), (c_re, c_im), (d_re, d_im) = parts
    beams = [
        (a_re + b_re + c_re + d_re, a_im + b_im + c_im + d_im),
        (a_re + b_im - c_re - d_im, a_im - b_re - c_im + d_re),
        (a_re - b_re + c_re - d_re, a_im - b_im + c_im - d_im),
        (a_re - b_im - c_re + d_im, a_im + b_re - c_im - d_re),
    ]
    for q in range(dish_count):
        beam_real, beam_imag = beams[q]
        acc_ref[q] += beam_real * beam_real + beam_imag * beam_imag

    @pl.when(step == pl.num_programs(0) - 1)
    def _():
        if not finish:
            o_ref[...] = acc_ref[...]
            return
        me = lax.axis_index("dish")
        width = o_ref.shape[1]
        for shift in range(dish_count):
            target = jnp.bitwise_xor(me, shift)
            beam_index = jnp.bitwise_or(
                jnp.left_shift(jnp.bitwise_and(target, 1), 1), jnp.right_shift(target, 1)
            )
            total = acc_ref[beam_index]
            folded = total[:, :CHB]
            for k in range(1, lanes // CHB):
                folded = folded + total[:, k * CHB : (k + 1) * CHB]
            folded = folded + pltpu.roll(folded, width, 1)
            flipped = jnp.transpose(folded, (1, 0))
            o_ref[shift] = flipped[:width] * (0.25 / FRAMES)


def body(voltages, feed_gains, block_assign, grid_rows):
    dish_rows = voltages.shape[0]
    block_count = lax.axis_size("freq")
    dish_count = lax.axis_size("dish")
    block_width = NCHAN // block_count
    quarter = block_width // dish_count
    dests = block_count * dish_count
    grid_len = dish_rows * block_count
    total_dishes = grid_len * dish_count
    samples = voltages.shape[-1]

    dest = jnp.arange(dests, dtype=jnp.int32)
    dest_quarter = dest // block_count
    dest_block = jnp.tile(block_assign, dish_count)
    dest_e = dest_block * dish_count + dest_quarter
    picks_e = (dest_e[:, None] == jnp.arange(dests, dtype=jnp.int32)[None, :]).astype(jnp.bfloat16)

    window = jnp.asarray(window_constant().reshape(TAPS, CHA, CHB))
    first_cos, first_sin = table_constant(CHA, CHA, CHA, 1.0 / math.sqrt(CHA))
    first_table = np.block([[first_cos, first_sin], [-first_sin, first_cos]])
    first_table = jnp.asarray(first_table)
    twiddle = jnp.asarray(np.stack(rotation_constant(CHA, CHB, NCHAN), axis=0))
    second_cos, second_sin = table_constant(CHB, CHB, CHB, 1.0 / math.sqrt(CHB))
    second_table = np.stack(
        [np.stack([second_cos, -second_sin], axis=0), np.stack([second_sin, second_cos], axis=0)],
        axis=0,
    )
    second_table = jnp.einsum(
        "je,qseb->qsjb", picks_e, jnp.asarray(second_table), preferred_element_type=jnp.float32
    ).astype(jnp.bfloat16).reshape(2, 2 * dests, CHB)
    gains = feed_gains[:, 0].reshape(dish_rows, 2, CHB, CHA)
    gains = jnp.einsum("je,rpec->rpjc", picks_e, gains, preferred_element_type=jnp.float32)
    gains = jnp.concatenate([gains, gains], axis=3).astype(jnp.bfloat16)

    chunk_pairs = [4, 4]
    chunks = len(chunk_pairs)
    tables = beam_tables(grid_rows, grid_len, dish_rows)
    feed_index = jnp.arange(dish_count, dtype=jnp.int32)
    positions = jnp.arange(grid_len, dtype=jnp.int32)
    twist_cos, twist_sin = rotation_constant(dish_count, grid_len, total_dishes)
    twist_cos = jnp.asarray(twist_cos[:, :, None])
    twist_sin = jnp.asarray(twist_sin[:, :, None])
    lane_block = 4 * quarter

    volts = voltages[:, 0].reshape(dish_rows, 2, samples // CHB, CHB)

    def channelize_chunk(chunk):
        pairs = chunk_pairs[chunk]
        first_pair = sum(chunk_pairs[:chunk])
        chunk_lanes = pairs * 2 * quarter
        span = (2 * pairs + TAPS - 1) * CHA
        first_row = 2 * first_pair * CHA
        return pl.pallas_call(
            functools.partial(channelize_kernel, first_pair, pairs),
            grid=(dish_rows // FEEDS_PER_STEP,),
            in_specs=[
                pl.BlockSpec(
                    (pl.Element(FEEDS_PER_STEP), pl.Element(2), pl.Element(span), pl.Element(CHB)),
                    lambda r: (r * FEEDS_PER_STEP, 0, first_row, 0),
                ),
                pl.BlockSpec((TAPS, CHA, CHB), lambda r: (0, 0, 0)),
                pl.BlockSpec((2 * CHA, 2 * CHA), lambda r: (0, 0)),
                pl.BlockSpec((2, CHA, CHB), lambda r: (0, 0, 0)),
                pl.BlockSpec((2, 2 * dests, CHB), lambda r: (0, 0, 0)),
                pl.BlockSpec((FEEDS_PER_STEP, 2, dests, 2 * CHA), lambda r: (r, 0, 0, 0)),
            ],
            out_specs=pl.BlockSpec((2, FEEDS_PER_STEP, dests, chunk_lanes), lambda r: (0, r, 0, 0)),
            out_shape=jax.ShapeDtypeStruct((2, dish_rows, dests, chunk_lanes), jnp.bfloat16),
            cost_estimate=pl.CostEstimate(
                flops=int(dish_rows * pairs * 2 * 2 * 128 * 128 * 128 * 3),
                bytes_accessed=int(voltages.size * 2 + 2 * dish_rows * dests * chunk_lanes * 2),
                transcendentals=0,
            ),
        )(volts, window, first_table, twiddle, second_table, gains)

    def beamform_chunk(received, carried, finish):
        carry_in = carried is not None
        chunk_lanes = received.shape[3]
        in_specs = [
            pl.BlockSpec((dests, 2, dish_rows, lane_block), lambda f: (0, 0, 0, f)),
            pl.BlockSpec((dish_count, 2 * grid_len, 2 * grid_len), lambda f: (0, 0, 0)),
            pl.BlockSpec((dish_count, grid_len, 1), lambda f: (0, 0, 0)),
            pl.BlockSpec((dish_count, grid_len, 1), lambda f: (0, 0, 0)),
        ]
        operands = [received, tables, twist_cos, twist_sin]
        if carry_in:
            in_specs.append(pl.BlockSpec((dish_count, grid_len, lane_block), lambda f: (0, 0, 0)))
            operands.append(carried)
        if finish:
            out_shape = (dish_count, quarter, grid_len)
        else:
            out_shape = (dish_count, grid_len, lane_block)
        return pl.pallas_call(
            functools.partial(beam_kernel, dish_count, carry_in, finish),
            grid=(chunk_lanes // lane_block,),
            in_specs=in_specs,
            out_specs=pl.BlockSpec(out_shape, lambda f: (0, 0, 0)),
            out_shape=jax.ShapeDtypeStruct(out_shape, jnp.float32),
            scratch_shapes=[pltpu.VMEM((dish_count, grid_len, lane_block), jnp.float32)],
            cost_estimate=pl.CostEstimate(
                flops=int(dish_count * 2 * 512 * 512 * chunk_lanes),
                bytes_accessed=int(received.size * 2 + tables.size * 2),
                transcendentals=0,
            ),
        )(*operands)

    sent = [channelize_chunk(c) for c in range(chunks)]
    arrived = [
        jnp.transpose(lax.all_to_all(s, ("dish", "freq"), 2, 2, tiled=True), (2, 0, 1, 3))
        for s in sent
    ]
    carried = None
    for c in range(chunks):
        carried = beamform_chunk(arrived[c], carried, c == chunks - 1)
    powers = carried

    me = lax.axis_index("dish")
    pieces = [powers[0]]
    for shift in range(1, dish_count):
        outgoing = powers[shift]
        pairs_list = [(i, i ^ shift) for i in range(dish_count)]
        pieces.append(lax.ppermute(outgoing, "dish", pairs_list))
    stacked = jnp.stack(pieces, axis=0)
    order = jnp.arange(dish_count, dtype=jnp.int32) ^ me
    received = jnp.take(stacked, order, axis=0)
    return received.reshape(block_width, grid_len)


def solution(mesh):
    placed = (P("freq", "dish", None, None), P("freq", "dish", None, None), P(), P())
    return jax.shard_map(
        body, mesh=mesh, in_specs=placed, out_specs=P("freq", "dish"), check_vma=False
    )
```

```python
import functools
import math

import jax
import jax.numpy as jnp
import ml_dtypes
import numpy as np
from jax import lax
from jax.experimental import pallas as pl
from jax.experimental.pallas import tpu as pltpu
from jax.sharding import PartitionSpec as P

NCHAN = 8192
CHA = 64
CHB = 128
TAPS = 4
FRAMES = 16
FEEDS_PER_STEP = 4


full_turn = 2.0 * math.pi


def table_constant(row_count, col_count, modulus, scaling):
    rows = np.arange(row_count, dtype=np.int64)[:, None]
    cols = np.arange(col_count, dtype=np.int64)[None, :]
    angles = np.float32(full_turn / modulus) * (rows * cols % modulus).astype(np.float32)
    cosine = (np.cos(angles.astype(np.float64)) * scaling).astype(ml_dtypes.bfloat16)
    sine = (np.sin(angles.astype(np.float64)) * scaling).astype(ml_dtypes.bfloat16)
    return cosine, sine


def window_constant():
    sample_index = np.arange(TAPS * NCHAN, dtype=np.float64)
    centred = (sample_index - TAPS * NCHAN / 2 + 0.5) / NCHAN
    taper_curve = 0.5 - 0.5 * np.cos(full_turn * (sample_index + 0.5) / (TAPS * NCHAN))
    shaped_window = (np.sinc(centred) * taper_curve).reshape(TAPS, NCHAN)
    energy = np.mean(np.sum(shaped_window * shaped_window, axis=0))
    return (shaped_window / np.sqrt(energy)).astype(np.float32)


def rotation_constant(row_count, col_count, modulus):
    rows = np.arange(row_count, dtype=np.int64)[:, None]
    cols = np.arange(col_count, dtype=np.int64)[None, :]
    angles = np.float32(-(full_turn / modulus)) * (rows * cols % modulus).astype(np.float32)
    angles = angles.astype(np.float64)
    return np.cos(angles).astype(np.float32), np.sin(angles).astype(np.float32)


def fourier_table(row_index, col_index, modulus, scaling):
    phases = row_index[:, None] * col_index[None, :] % modulus
    angles = full_turn / modulus * phases.astype(jnp.float32)
    cosine_table = (jnp.cos(angles) * scaling).astype(jnp.bfloat16)
    sine_table = (jnp.sin(angles) * scaling).astype(jnp.bfloat16)
    upper_rows = jnp.stack([cosine_table, -sine_table], axis=1)
    lower_rows = jnp.stack([sine_table, cosine_table], axis=1)
    return jnp.stack([upper_rows, lower_rows], axis=0)


def filter_window():
    sample_index = jnp.arange(TAPS * NCHAN, dtype=jnp.float32)
    centred = (sample_index - TAPS * NCHAN / 2 + 0.5) / NCHAN
    taper_curve = 0.5 - 0.5 * jnp.cos(full_turn * (sample_index + 0.5) / (TAPS * NCHAN))
    shaped_window = (jnp.sinc(centred) * taper_curve).reshape(TAPS, NCHAN)
    energy = jnp.mean(jnp.sum(shaped_window * shaped_window, axis=0))
    return shaped_window / jnp.sqrt(energy)


def beam_tables(grid_rows, grid_len, rows_per_device):
    positions = jnp.arange(grid_len, dtype=jnp.int32)
    cosine_base, sine_base = table_constant(grid_len, grid_len, grid_len, 1.0 / math.sqrt(grid_len))
    cosine_base = jnp.asarray(cosine_base)
    sine_base = jnp.asarray(sine_base)
    devices = grid_len // rows_per_device
    picks = (positions[None, :, None] == grid_rows[:, None, :]).astype(jnp.bfloat16)
    cosine_table = jnp.einsum(
        "jg,dgm->djm", cosine_base, picks, preferred_element_type=jnp.float32
    ).astype(jnp.bfloat16)
    sine_table = jnp.einsum(
        "jg,dgm->djm", sine_base, picks, preferred_element_type=jnp.float32
    ).astype(jnp.bfloat16)
    shape = (grid_rows.shape[0], grid_len, devices, 1, rows_per_device)
    cosine_table = cosine_table.reshape(shape)
    sine_table = sine_table.reshape(shape)
    real_rows = jnp.concatenate([cosine_table, sine_table], axis=3)
    imag_rows = jnp.concatenate([-sine_table, cosine_table], axis=3)
    rows = jnp.concatenate([real_rows, imag_rows], axis=1)
    return rows.reshape(grid_rows.shape[0], 2 * grid_len, 2 * grid_len)


def channelize_kernel(first_pair, pairs, v_ref, w_ref, t1_ref, tw_ref, t2_ref, g_ref, o_ref):
    cos_tw = tw_ref[0]
    sin_tw = tw_ref[1]
    t1 = t1_ref[...]
    t2_real = t2_ref[0]
    t2_imag = t2_ref[1]
    half = t2_real.shape[0] // 2
    feeds = v_ref.shape[0]

    def one_frame(pieces):
        acc = None
        for tap in range(TAPS):
            term = w_ref[tap][None] * pieces[tap]
            acc = term if acc is None else acc + term
        block = acc.astype(jnp.bfloat16).reshape(2 * CHA, CHB)
        section = jnp.dot(t1, block, preferred_element_type=jnp.float32)
        sec_real = section[:CHA]
        sec_imag = section[CHA:]
        turned_real = sec_real * cos_tw - sec_imag * sin_tw
        turned_imag = sec_real * sin_tw + sec_imag * cos_tw
        return turned_real.astype(jnp.bfloat16), turned_imag.astype(jnp.bfloat16)

    def pair(feed, step):
        g_real = g_ref[feed, 0].astype(jnp.float32)
        g_imag = g_ref[feed, 1].astype(jnp.float32)
        pieces = []
        for offset in range(TAPS + 1):
            start = pl.multiple_of((2 * (step - first_pair) + offset) * CHA, CHA)
            pieces.append(v_ref[feed, :, pl.ds(start, CHA), :].astype(jnp.float32))
        first_real, first_imag = one_frame(pieces[:TAPS])
        second_real, second_imag = one_frame(pieces[1:])
        both_real = jnp.concatenate([first_real, second_real], axis=0)
        both_imag = jnp.concatenate([first_imag, second_imag], axis=0)
        dims = (((1,), (1,)), ((), ()))
        spectrum = lax.dot_general(
            t2_real, both_real, dims, preferred_element_type=jnp.float32
        ) + lax.dot_general(t2_imag, both_imag, dims, preferred_element_type=jnp.float32)
        spec_real = spectrum[:half]
        spec_imag = spectrum[half:]
        out_real = spec_real * g_real - spec_imag * g_imag
        out_imag = spec_real * g_imag + spec_imag * g_real
        lanes = pl.ds(pl.multiple_of((step - first_pair) * 2 * CHA, 2 * CHA), 2 * CHA)
        o_ref[0, feed, :, lanes] = out_real.astype(o_ref.dtype)
        o_ref[1, feed, :, lanes] = out_imag.astype(o_ref.dtype)

    for feed in range(feeds):
        for step in range(first_pair, first_pair + pairs):
            pair(feed, step)


def beam_kernel(dish_count, carry_in, finish, lanes, *refs):
    x_ref, t_ref, c_ref, s_ref = refs[:4]
    init_ref = refs[4] if carry_in else None
    out_refs = refs[4 + carry_in : -1]
    acc_ref = refs[-1]
    step = pl.program_id(0)
    devices = x_ref.shape[0] // dish_count
    rows = x_ref.shape[2]
    grid_len = t_ref.shape[1] // 2
    lane_window = slice(None)

    @pl.when(step == 0)
    def _():
        if carry_in:
            acc_ref[...] = init_ref[...]
        else:
            acc_ref[...] = jnp.zeros_like(acc_ref)

    parts = []
    for d in range(dish_count):
        block = x_ref[pl.ds(d * devices, devices), :, :, lane_window].reshape(
            2 * rows * devices, lanes
        )
        sums = jnp.dot(t_ref[d], block, preferred_element_type=jnp.float32)
        sum_real = sums[:grid_len]
        sum_imag = sums[grid_len:]
        cos_d = c_ref[d]
        sin_d = s_ref[d]
        part_real = sum_real * cos_d - sum_imag * sin_d
        part_imag = sum_real * sin_d + sum_imag * cos_d
        parts.append(
            (
                part_real.astype(jnp.bfloat16).astype(jnp.float32),
                part_imag.astype(jnp.bfloat16).astype(jnp.float32),
            )
        )
    (a_re, a_im), (b_re, b_im), (c_re, c_im), (d_re, d_im) = parts
    beams = [
        (a_re + b_re + c_re + d_re, a_im + b_im + c_im + d_im),
        (a_re + b_im - c_re - d_im, a_im - b_re - c_im + d_re),
        (a_re - b_re + c_re - d_re, a_im - b_im + c_im - d_im),
        (a_re - b_im - c_re + d_im, a_im + b_re - c_im - d_re),
    ]
    for q in range(dish_count):
        beam_real, beam_imag = beams[q]
        acc_ref[q] += beam_real * beam_real + beam_imag * beam_imag

    @pl.when(step == pl.num_programs(0) - 1)
    def _():
        if not finish:
            out_refs[0][...] = acc_ref[...]
            return
        me = lax.axis_index("dish")
        width = out_refs[0].shape[0]
        for shift in range(dish_count):
            target = jnp.bitwise_xor(me, shift)
            beam_index = jnp.bitwise_or(
                jnp.left_shift(jnp.bitwise_and(target, 1), 1), jnp.right_shift(target, 1)
            )
            total = acc_ref[beam_index]
            folded = total[:, :CHB]
            for k in range(1, lanes // CHB):
                folded = folded + total[:, k * CHB : (k + 1) * CHB]
            folded = folded + pltpu.roll(folded, width, 1)
            flipped = jnp.transpose(folded, (1, 0))
            out_refs[shift][...] = flipped[:width] * (0.25 / FRAMES)


def body(voltages, feed_gains, block_assign, grid_rows):
    dish_rows = voltages.shape[0]
    block_count = lax.axis_size("freq")
    dish_count = lax.axis_size("dish")
    block_width = NCHAN // block_count
    quarter = block_width // dish_count
    dests = block_count * dish_count
    grid_len = dish_rows * block_count
    total_dishes = grid_len * dish_count
    samples = voltages.shape[-1]

    dest = jnp.arange(dests, dtype=jnp.int32)
    dest_quarter = dest // block_count
    dest_block = jnp.tile(block_assign, dish_count)
    dest_e = dest_block * dish_count + dest_quarter
    picks_e = (dest_e[:, None] == jnp.arange(dests, dtype=jnp.int32)[None, :]).astype(jnp.bfloat16)

    window = jnp.asarray(window_constant().reshape(TAPS, CHA, CHB))
    first_cos, first_sin = table_constant(CHA, CHA, CHA, 1.0 / math.sqrt(CHA))
    first_table = np.block([[first_cos, first_sin], [-first_sin, first_cos]])
    first_table = jnp.asarray(first_table)
    twiddle = jnp.asarray(np.stack(rotation_constant(CHA, CHB, NCHAN), axis=0))
    second_cos, second_sin = table_constant(CHB, CHB, CHB, 1.0 / math.sqrt(CHB))
    second_table = np.stack(
        [np.stack([second_cos, -second_sin], axis=0), np.stack([second_sin, second_cos], axis=0)],
        axis=0,
    )
    second_table = jnp.einsum(
        "je,qseb->qsjb", picks_e, jnp.asarray(second_table), preferred_element_type=jnp.float32
    ).astype(jnp.bfloat16).reshape(2, 2 * dests, CHB)
    gains = feed_gains[:, 0].reshape(dish_rows, 2, CHB, CHA)
    gains = jnp.einsum("je,rpec->rpjc", picks_e, gains, preferred_element_type=jnp.float32)
    gains = jnp.concatenate([gains, gains], axis=3).astype(jnp.bfloat16)

    chunk_pairs = [4, 4]
    chunks = len(chunk_pairs)
    tables = beam_tables(grid_rows, grid_len, dish_rows)
    feed_index = jnp.arange(dish_count, dtype=jnp.int32)
    positions = jnp.arange(grid_len, dtype=jnp.int32)
    twist_cos, twist_sin = rotation_constant(dish_count, grid_len, total_dishes)
    twist_cos = jnp.asarray(twist_cos[:, :, None])
    twist_sin = jnp.asarray(twist_sin[:, :, None])
    lane_block = 4 * quarter

    volts = voltages[:, 0].reshape(dish_rows, 2, samples // CHB, CHB)

    def channelize_chunk(chunk):
        pairs = chunk_pairs[chunk]
        first_pair = sum(chunk_pairs[:chunk])
        chunk_lanes = pairs * 2 * quarter
        span = (2 * pairs + TAPS - 1) * CHA
        first_row = 2 * first_pair * CHA
        return pl.pallas_call(
            functools.partial(channelize_kernel, first_pair, pairs),
            grid=(dish_rows // FEEDS_PER_STEP,),
            in_specs=[
                pl.BlockSpec(
                    (pl.Element(FEEDS_PER_STEP), pl.Element(2), pl.Element(span), pl.Element(CHB)),
                    lambda r: (r * FEEDS_PER_STEP, 0, first_row, 0),
                ),
                pl.BlockSpec((TAPS, CHA, CHB), lambda r: (0, 0, 0)),
                pl.BlockSpec((2 * CHA, 2 * CHA), lambda r: (0, 0)),
                pl.BlockSpec((2, CHA, CHB), lambda r: (0, 0, 0)),
                pl.BlockSpec((2, 2 * dests, CHB), lambda r: (0, 0, 0)),
                pl.BlockSpec((FEEDS_PER_STEP, 2, dests, 2 * CHA), lambda r: (r, 0, 0, 0)),
            ],
            out_specs=pl.BlockSpec((2, FEEDS_PER_STEP, dests, chunk_lanes), lambda r: (0, r, 0, 0)),
            out_shape=jax.ShapeDtypeStruct((2, dish_rows, dests, chunk_lanes), jnp.bfloat16),
            cost_estimate=pl.CostEstimate(
                flops=int(dish_rows * pairs * 2 * 2 * 128 * 128 * 128 * 3),
                bytes_accessed=int(voltages.size * 2 + 2 * dish_rows * dests * chunk_lanes * 2),
                transcendentals=0,
            ),
        )(volts, window, first_table, twiddle, second_table, gains)

    def beamform_chunk(received, carried, finish):
        carry_in = carried is not None
        chunk_lanes = received.shape[3]
        in_specs = [
            pl.BlockSpec((dests, 2, dish_rows, lane_block), lambda f: (0, 0, 0, f)),
            pl.BlockSpec((dish_count, 2 * grid_len, 2 * grid_len), lambda f: (0, 0, 0)),
        ]
        in_specs += [pl.BlockSpec((dish_count, grid_len, 1), lambda f: (0, 0, 0))] * 2
        operands = [received, tables, twist_cos, twist_sin]
        if carry_in:
            in_specs.append(pl.BlockSpec((dish_count, grid_len, lane_block), lambda f: (0, 0, 0)))
            operands.append(carried)
        if finish:
            out_specs = [pl.BlockSpec((quarter, grid_len), lambda f: (0, 0))] * dish_count
            out_shape = [jax.ShapeDtypeStruct((quarter, grid_len), jnp.float32)] * dish_count
        else:
            out_specs = pl.BlockSpec((dish_count, grid_len, lane_block), lambda f: (0, 0, 0))
            out_shape = jax.ShapeDtypeStruct((dish_count, grid_len, lane_block), jnp.float32)
        return pl.pallas_call(
            functools.partial(beam_kernel, dish_count, carry_in, finish, lane_block),
            grid=(chunk_lanes // lane_block,),
            in_specs=in_specs,
            out_specs=out_specs,
            out_shape=out_shape,
            scratch_shapes=[pltpu.VMEM((dish_count, grid_len, lane_block), jnp.float32)],
            cost_estimate=pl.CostEstimate(
                flops=int(dish_count * 2 * 512 * 512 * chunk_lanes),
                bytes_accessed=int(received.size * 2 + tables.size * 2),
                transcendentals=0,
            ),
        )(*operands)

    sent = [channelize_chunk(c) for c in range(chunks)]
    arrived = [
        jnp.transpose(lax.all_to_all(s, ("dish", "freq"), 2, 2, tiled=True), (2, 0, 1, 3))
        for s in sent
    ]
    carried = None
    for c in range(chunks):
        carried = beamform_chunk(arrived[c], carried, c == chunks - 1)
    powers = carried

    me = lax.axis_index("dish")
    pieces = [powers[0]]
    for shift in range(1, dish_count):
        outgoing = powers[shift]
        pairs_list = [(i, i ^ shift) for i in range(dish_count)]
        pieces.append(lax.ppermute(outgoing, "dish", pairs_list))
    stacked = jnp.stack(pieces, axis=0)
    order = jnp.arange(dish_count, dtype=jnp.int32) ^ me
    received = jnp.take(stacked, order, axis=0)
    return received.reshape(block_width, grid_len)


def solution(mesh):
    placed = (P("freq", "dish", None, None), P("freq", "dish", None, None), P(), P())
    return jax.shard_map(
        body, mesh=mesh, in_specs=placed, out_specs=P("freq", "dish"), check_vma=False
    )
```

```python
import functools
import math

import jax
import jax.numpy as jnp
import ml_dtypes
import numpy as np
from jax import lax
from jax.experimental import pallas as pl
from jax.experimental.pallas import tpu as pltpu
from jax.sharding import PartitionSpec as P

NCHAN = 8192
CHA = 64
CHB = 128
TAPS = 4
FRAMES = 16
FEEDS_PER_STEP = 4


full_turn = 2.0 * math.pi


def table_constant(row_count, col_count, modulus, scaling):
    rows = np.arange(row_count, dtype=np.int64)[:, None]
    cols = np.arange(col_count, dtype=np.int64)[None, :]
    angles = np.float32(full_turn / modulus) * (rows * cols % modulus).astype(np.float32)
    cosine = (np.cos(angles.astype(np.float64)) * scaling).astype(ml_dtypes.bfloat16)
    sine = (np.sin(angles.astype(np.float64)) * scaling).astype(ml_dtypes.bfloat16)
    return cosine, sine


def window_constant():
    sample_index = np.arange(TAPS * NCHAN, dtype=np.float64)
    centred = (sample_index - TAPS * NCHAN / 2 + 0.5) / NCHAN
    taper_curve = 0.5 - 0.5 * np.cos(full_turn * (sample_index + 0.5) / (TAPS * NCHAN))
    shaped_window = (np.sinc(centred) * taper_curve).reshape(TAPS, NCHAN)
    energy = np.mean(np.sum(shaped_window * shaped_window, axis=0))
    return (shaped_window / np.sqrt(energy)).astype(np.float32)


def rotation_constant(row_count, col_count, modulus):
    rows = np.arange(row_count, dtype=np.int64)[:, None]
    cols = np.arange(col_count, dtype=np.int64)[None, :]
    angles = np.float32(-(full_turn / modulus)) * (rows * cols % modulus).astype(np.float32)
    angles = angles.astype(np.float64)
    return np.cos(angles).astype(np.float32), np.sin(angles).astype(np.float32)


def fourier_table(row_index, col_index, modulus, scaling):
    phases = row_index[:, None] * col_index[None, :] % modulus
    angles = full_turn / modulus * phases.astype(jnp.float32)
    cosine_table = (jnp.cos(angles) * scaling).astype(jnp.bfloat16)
    sine_table = (jnp.sin(angles) * scaling).astype(jnp.bfloat16)
    upper_rows = jnp.stack([cosine_table, -sine_table], axis=1)
    lower_rows = jnp.stack([sine_table, cosine_table], axis=1)
    return jnp.stack([upper_rows, lower_rows], axis=0)


def filter_window():
    sample_index = jnp.arange(TAPS * NCHAN, dtype=jnp.float32)
    centred = (sample_index - TAPS * NCHAN / 2 + 0.5) / NCHAN
    taper_curve = 0.5 - 0.5 * jnp.cos(full_turn * (sample_index + 0.5) / (TAPS * NCHAN))
    shaped_window = (jnp.sinc(centred) * taper_curve).reshape(TAPS, NCHAN)
    energy = jnp.mean(jnp.sum(shaped_window * shaped_window, axis=0))
    return shaped_window / jnp.sqrt(energy)


def beam_tables(grid_rows, grid_len, rows_per_device):
    positions = jnp.arange(grid_len, dtype=jnp.int32)
    cosine_base, sine_base = table_constant(grid_len, grid_len, grid_len, 1.0 / math.sqrt(grid_len))
    cosine_base = jnp.asarray(cosine_base)
    sine_base = jnp.asarray(sine_base)
    devices = grid_len // rows_per_device
    picks = (positions[None, :, None] == grid_rows[:, None, :]).astype(jnp.bfloat16)
    cosine_table = jnp.einsum(
        "jg,dgm->djm", cosine_base, picks, preferred_element_type=jnp.float32
    ).astype(jnp.bfloat16)
    sine_table = jnp.einsum(
        "jg,dgm->djm", sine_base, picks, preferred_element_type=jnp.float32
    ).astype(jnp.bfloat16)
    shape = (grid_rows.shape[0], grid_len, devices, 1, rows_per_device)
    cosine_table = cosine_table.reshape(shape)
    sine_table = sine_table.reshape(shape)
    real_rows = jnp.concatenate([cosine_table, sine_table], axis=3)
    imag_rows = jnp.concatenate([-sine_table, cosine_table], axis=3)
    rows = jnp.concatenate([real_rows, imag_rows], axis=1)
    return rows.reshape(grid_rows.shape[0], 2 * grid_len, 2 * grid_len)


def channelize_kernel(first_pair, pairs, v_ref, w_ref, t1_ref, tw_ref, t2_ref, g_ref, o_ref):
    cos_tw = tw_ref[0]
    sin_tw = tw_ref[1]
    t1 = t1_ref[...]
    t2_real = t2_ref[0]
    t2_imag = t2_ref[1]
    half = t2_real.shape[0] // 2
    feeds = v_ref.shape[0]

    def one_frame(pieces):
        acc = None
        for tap in range(TAPS):
            term = w_ref[tap][None] * pieces[tap]
            acc = term if acc is None else acc + term
        block = acc.astype(jnp.bfloat16).reshape(2 * CHA, CHB)
        section = jnp.dot(t1, block, preferred_element_type=jnp.float32)
        sec_real = section[:CHA]
        sec_imag = section[CHA:]
        turned_real = sec_real * cos_tw - sec_imag * sin_tw
        turned_imag = sec_real * sin_tw + sec_imag * cos_tw
        return turned_real.astype(jnp.bfloat16), turned_imag.astype(jnp.bfloat16)

    def pair(feed, step):
        g_real = g_ref[feed, 0].astype(jnp.float32)
        g_imag = g_ref[feed, 1].astype(jnp.float32)
        pieces = []
        for offset in range(TAPS + 1):
            start = pl.multiple_of((2 * (step - first_pair) + offset) * CHA, CHA)
            pieces.append(v_ref[feed, :, pl.ds(start, CHA), :].astype(jnp.float32))
        first_real, first_imag = one_frame(pieces[:TAPS])
        second_real, second_imag = one_frame(pieces[1:])
        both_real = jnp.concatenate([first_real, second_real], axis=0)
        both_imag = jnp.concatenate([first_imag, second_imag], axis=0)
        dims = (((1,), (1,)), ((), ()))
        spectrum = lax.dot_general(
            t2_real, both_real, dims, preferred_element_type=jnp.float32
        ) + lax.dot_general(t2_imag, both_imag, dims, preferred_element_type=jnp.float32)
        spec_real = spectrum[:half]
        spec_imag = spectrum[half:]
        out_real = spec_real * g_real - spec_imag * g_imag
        out_imag = spec_real * g_imag + spec_imag * g_real
        lanes = pl.ds(pl.multiple_of((step - first_pair) * 2 * CHA, 2 * CHA), 2 * CHA)
        o_ref[0, feed, :, lanes] = out_real.astype(o_ref.dtype)
        o_ref[1, feed, :, lanes] = out_imag.astype(o_ref.dtype)

    for feed in range(feeds):
        for step in range(first_pair, first_pair + pairs):
            pair(feed, step)


def beam_kernel(dish_count, carry_in, finish, lanes, *refs):
    x_ref, t_ref, c_ref, s_ref = refs[:4]
    init_ref = refs[4] if carry_in else None
    out_refs = refs[4 + carry_in : -1]
    acc_ref = refs[-1]
    step = pl.program_id(0)
    devices = x_ref.shape[0] // dish_count
    rows = x_ref.shape[2]
    grid_len = t_ref.shape[1] // 2
    lane_window = slice(None)

    @pl.when(step == 0)
    def _():
        if carry_in:
            acc_ref[...] = init_ref[...]
        else:
            acc_ref[...] = jnp.zeros_like(acc_ref)

    parts = []
    for d in range(dish_count):
        block = x_ref[pl.ds(d * devices, devices), :, :, lane_window].reshape(
            2 * rows * devices, lanes
        )
        sums = jnp.dot(t_ref[d], block, preferred_element_type=jnp.float32)
        sum_real = sums[:grid_len]
        sum_imag = sums[grid_len:]
        cos_d = c_ref[d]
        sin_d = s_ref[d]
        part_real = sum_real * cos_d - sum_imag * sin_d
        part_imag = sum_real * sin_d + sum_imag * cos_d
        parts.append(
            (
                part_real.astype(jnp.bfloat16).astype(jnp.float32),
                part_imag.astype(jnp.bfloat16).astype(jnp.float32),
            )
        )
    (a_re, a_im), (b_re, b_im), (c_re, c_im), (d_re, d_im) = parts
    beams = [
        (a_re + b_re + c_re + d_re, a_im + b_im + c_im + d_im),
        (a_re + b_im - c_re - d_im, a_im - b_re - c_im + d_re),
        (a_re - b_re + c_re - d_re, a_im - b_im + c_im - d_im),
        (a_re - b_im - c_re + d_im, a_im + b_re - c_im - d_re),
    ]
    for q in range(dish_count):
        beam_real, beam_imag = beams[q]
        acc_ref[q] += beam_real * beam_real + beam_imag * beam_imag

    @pl.when(step == pl.num_programs(0) - 1)
    def _():
        if not finish:
            out_refs[0][...] = acc_ref[...]
            return
        me = lax.axis_index("dish")
        width = out_refs[0].shape[0]
        for shift in range(dish_count):
            target = jnp.bitwise_xor(me, shift)
            beam_index = jnp.bitwise_or(
                jnp.left_shift(jnp.bitwise_and(target, 1), 1), jnp.right_shift(target, 1)
            )
            total = acc_ref[beam_index]
            folded = total[:, :CHB]
            for k in range(1, lanes // CHB):
                folded = folded + total[:, k * CHB : (k + 1) * CHB]
            folded = folded + pltpu.roll(folded, width, 1)
            flipped = jnp.transpose(folded, (1, 0))
            out_refs[shift][...] = flipped[:width] * (0.25 / FRAMES)


def body(voltages, feed_gains, block_assign, grid_rows):
    dish_rows = voltages.shape[0]
    block_count = lax.axis_size("freq")
    dish_count = lax.axis_size("dish")
    block_width = NCHAN // block_count
    quarter = block_width // dish_count
    dests = block_count * dish_count
    grid_len = dish_rows * block_count
    total_dishes = grid_len * dish_count
    samples = voltages.shape[-1]

    dest = jnp.arange(dests, dtype=jnp.int32)
    dest_quarter = dest // block_count
    dest_block = jnp.tile(block_assign, dish_count)
    dest_e = dest_block * dish_count + dest_quarter
    picks_e = (dest_e[:, None] == jnp.arange(dests, dtype=jnp.int32)[None, :]).astype(jnp.bfloat16)

    window = jnp.asarray(window_constant().reshape(TAPS, CHA, CHB))
    first_cos, first_sin = table_constant(CHA, CHA, CHA, 1.0 / math.sqrt(CHA))
    first_table = np.block([[first_cos, first_sin], [-first_sin, first_cos]])
    first_table = jnp.asarray(first_table)
    twiddle = jnp.asarray(np.stack(rotation_constant(CHA, CHB, NCHAN), axis=0))
    second_cos, second_sin = table_constant(CHB, CHB, CHB, 1.0 / math.sqrt(CHB))
    second_table = np.stack(
        [np.stack([second_cos, -second_sin], axis=0), np.stack([second_sin, second_cos], axis=0)],
        axis=0,
    )
    second_table = jnp.einsum(
        "je,qseb->qsjb", picks_e, jnp.asarray(second_table), preferred_element_type=jnp.float32
    ).astype(jnp.bfloat16).reshape(2, 2 * dests, CHB)
    gains = feed_gains[:, 0].reshape(dish_rows, 2, CHB, CHA)
    gains = jnp.einsum("je,rpec->rpjc", picks_e, gains, preferred_element_type=jnp.float32)
    gains = jnp.concatenate([gains, gains], axis=3).astype(jnp.bfloat16)

    chunk_pairs = [4, 4]
    chunks = len(chunk_pairs)
    tables = beam_tables(grid_rows, grid_len, dish_rows)
    feed_index = jnp.arange(dish_count, dtype=jnp.int32)
    positions = jnp.arange(grid_len, dtype=jnp.int32)
    twist_cos, twist_sin = rotation_constant(dish_count, grid_len, total_dishes)
    twist_cos = jnp.asarray(twist_cos[:, :, None])
    twist_sin = jnp.asarray(twist_sin[:, :, None])
    lane_block = 4 * quarter

    volts = voltages[:, 0].reshape(dish_rows, 2, samples // CHB, CHB)

    def channelize_chunk(chunk):
        pairs = chunk_pairs[chunk]
        first_pair = sum(chunk_pairs[:chunk])
        chunk_lanes = pairs * 2 * quarter
        span = (2 * pairs + TAPS - 1) * CHA
        first_row = 2 * first_pair * CHA
        return pl.pallas_call(
            functools.partial(channelize_kernel, first_pair, pairs),
            grid=(dish_rows // FEEDS_PER_STEP,),
            in_specs=[
                pl.BlockSpec(
                    (pl.Element(FEEDS_PER_STEP), pl.Element(2), pl.Element(span), pl.Element(CHB)),
                    lambda r: (r * FEEDS_PER_STEP, 0, first_row, 0),
                ),
                pl.BlockSpec((TAPS, CHA, CHB), lambda r: (0, 0, 0)),
                pl.BlockSpec((2 * CHA, 2 * CHA), lambda r: (0, 0)),
                pl.BlockSpec((2, CHA, CHB), lambda r: (0, 0, 0)),
                pl.BlockSpec((2, 2 * dests, CHB), lambda r: (0, 0, 0)),
                pl.BlockSpec((FEEDS_PER_STEP, 2, dests, 2 * CHA), lambda r: (r, 0, 0, 0)),
            ],
            out_specs=pl.BlockSpec((2, FEEDS_PER_STEP, dests, chunk_lanes), lambda r: (0, r, 0, 0)),
            out_shape=jax.ShapeDtypeStruct((2, dish_rows, dests, chunk_lanes), jnp.bfloat16),
            cost_estimate=pl.CostEstimate(
                flops=int(dish_rows * pairs * 2 * 2 * 128 * 128 * 128 * 3),
                bytes_accessed=int(voltages.size * 2 + 2 * dish_rows * dests * chunk_lanes * 2),
                transcendentals=0,
            ),
        )(volts, window, first_table, twiddle, second_table, gains)

    def beamform_chunk(received, carried, finish):
        carry_in = carried is not None
        chunk_lanes = received.shape[3]
        in_specs = [
            pl.BlockSpec((dests, 2, dish_rows, lane_block), lambda f: (0, 0, 0, f)),
            pl.BlockSpec((dish_count, 2 * grid_len, 2 * grid_len), lambda f: (0, 0, 0)),
        ]
        in_specs += [pl.BlockSpec((dish_count, grid_len, 1), lambda f: (0, 0, 0))] * 2
        operands = [received, tables, twist_cos, twist_sin]
        if carry_in:
            in_specs.append(pl.BlockSpec((dish_count, grid_len, lane_block), lambda f: (0, 0, 0)))
            operands.append(carried)
        if finish:
            out_specs = [pl.BlockSpec((quarter, grid_len), lambda f: (0, 0))] * dish_count
            out_shape = [jax.ShapeDtypeStruct((quarter, grid_len), jnp.float32)] * dish_count
        else:
            out_specs = pl.BlockSpec((dish_count, grid_len, lane_block), lambda f: (0, 0, 0))
            out_shape = jax.ShapeDtypeStruct((dish_count, grid_len, lane_block), jnp.float32)
        return pl.pallas_call(
            functools.partial(beam_kernel, dish_count, carry_in, finish, lane_block),
            grid=(chunk_lanes // lane_block,),
            in_specs=in_specs,
            out_specs=out_specs,
            out_shape=out_shape,
            scratch_shapes=[pltpu.VMEM((dish_count, grid_len, lane_block), jnp.float32)],
            cost_estimate=pl.CostEstimate(
                flops=int(dish_count * 2 * 512 * 512 * chunk_lanes),
                bytes_accessed=int(received.size * 2 + tables.size * 2),
                transcendentals=0,
            ),
        )(*operands)

    sent = [channelize_chunk(c) for c in range(chunks)]
    arrived = [
        jnp.transpose(lax.all_to_all(s, ("dish", "freq"), 2, 2, tiled=True), (2, 0, 1, 3))
        for s in sent
    ]
    carried = None
    for c in range(chunks):
        carried = beamform_chunk(arrived[c], carried, c == chunks - 1)
    powers = carried

    me = lax.axis_index("dish")
    pieces = [powers[0]]
    for shift in range(1, dish_count):
        outgoing = powers[shift]
        pairs_list = [(i, i ^ shift) for i in range(dish_count)]
        pieces.append(lax.ppermute(outgoing, "dish", pairs_list))
    blocks = []
    for source in range(dish_count):
        shift_of = jnp.bitwise_xor(me, source)
        chosen = pieces[dish_count - 1]
        for shift in range(dish_count - 2, -1, -1):
            chosen = jnp.where(shift_of == shift, pieces[shift], chosen)
        blocks.append(chosen)
    return jnp.concatenate(blocks, axis=0)


def solution(mesh):
    placed = (P("freq", "dish", None, None), P("freq", "dish", None, None), P(), P())
    return jax.shard_map(
        body, mesh=mesh, in_specs=placed, out_specs=P("freq", "dish"), check_vma=False
    )
```

```python
import functools
import math

import jax
import jax.numpy as jnp
import ml_dtypes
import numpy as np
from jax import lax
from jax.experimental import pallas as pl
from jax.experimental.pallas import tpu as pltpu
from jax.sharding import PartitionSpec as P

NCHAN = 8192
CHA = 64
CHB = 128
TAPS = 4
FRAMES = 16
FEEDS_PER_STEP = 4


full_turn = 2.0 * math.pi


def table_constant(row_count, col_count, modulus, scaling):
    rows = np.arange(row_count, dtype=np.int64)[:, None]
    cols = np.arange(col_count, dtype=np.int64)[None, :]
    angles = np.float32(full_turn / modulus) * (rows * cols % modulus).astype(np.float32)
    cosine = (np.cos(angles.astype(np.float64)) * scaling).astype(ml_dtypes.bfloat16)
    sine = (np.sin(angles.astype(np.float64)) * scaling).astype(ml_dtypes.bfloat16)
    return cosine, sine


def window_constant():
    sample_index = np.arange(TAPS * NCHAN, dtype=np.float64)
    centred = (sample_index - TAPS * NCHAN / 2 + 0.5) / NCHAN
    taper_curve = 0.5 - 0.5 * np.cos(full_turn * (sample_index + 0.5) / (TAPS * NCHAN))
    shaped_window = (np.sinc(centred) * taper_curve).reshape(TAPS, NCHAN)
    energy = np.mean(np.sum(shaped_window * shaped_window, axis=0))
    return (shaped_window / np.sqrt(energy)).astype(np.float32)


def rotation_constant(row_count, col_count, modulus):
    rows = np.arange(row_count, dtype=np.int64)[:, None]
    cols = np.arange(col_count, dtype=np.int64)[None, :]
    angles = np.float32(-(full_turn / modulus)) * (rows * cols % modulus).astype(np.float32)
    angles = angles.astype(np.float64)
    return np.cos(angles).astype(np.float32), np.sin(angles).astype(np.float32)


def fourier_table(row_index, col_index, modulus, scaling):
    phases = row_index[:, None] * col_index[None, :] % modulus
    angles = full_turn / modulus * phases.astype(jnp.float32)
    cosine_table = (jnp.cos(angles) * scaling).astype(jnp.bfloat16)
    sine_table = (jnp.sin(angles) * scaling).astype(jnp.bfloat16)
    upper_rows = jnp.stack([cosine_table, -sine_table], axis=1)
    lower_rows = jnp.stack([sine_table, cosine_table], axis=1)
    return jnp.stack([upper_rows, lower_rows], axis=0)


def filter_window():
    sample_index = jnp.arange(TAPS * NCHAN, dtype=jnp.float32)
    centred = (sample_index - TAPS * NCHAN / 2 + 0.5) / NCHAN
    taper_curve = 0.5 - 0.5 * jnp.cos(full_turn * (sample_index + 0.5) / (TAPS * NCHAN))
    shaped_window = (jnp.sinc(centred) * taper_curve).reshape(TAPS, NCHAN)
    energy = jnp.mean(jnp.sum(shaped_window * shaped_window, axis=0))
    return shaped_window / jnp.sqrt(energy)


def beam_tables(grid_rows, grid_len, rows_per_device):
    positions = jnp.arange(grid_len, dtype=jnp.int32)
    cosine_base, sine_base = table_constant(grid_len, grid_len, grid_len, 1.0 / math.sqrt(grid_len))
    cosine_base = jnp.asarray(cosine_base)
    sine_base = jnp.asarray(sine_base)
    devices = grid_len // rows_per_device
    picks = (positions[None, :, None] == grid_rows[:, None, :]).astype(jnp.bfloat16)
    cosine_table = jnp.einsum(
        "jg,dgm->djm", cosine_base, picks, preferred_element_type=jnp.float32
    ).astype(jnp.bfloat16)
    sine_table = jnp.einsum(
        "jg,dgm->djm", sine_base, picks, preferred_element_type=jnp.float32
    ).astype(jnp.bfloat16)
    shape = (grid_rows.shape[0], grid_len, devices, 1, rows_per_device)
    cosine_table = cosine_table.reshape(shape)
    sine_table = sine_table.reshape(shape)
    real_rows = jnp.concatenate([cosine_table, sine_table], axis=3)
    imag_rows = jnp.concatenate([-sine_table, cosine_table], axis=3)
    rows = jnp.concatenate([real_rows, imag_rows], axis=1)
    return rows.reshape(grid_rows.shape[0], 2 * grid_len, 2 * grid_len)


def channelize_kernel(first_pair, pairs, v_ref, w_ref, t1_ref, tw_ref, t2_ref, g_ref, o_ref):
    cos_tw = tw_ref[0]
    sin_tw = tw_ref[1]
    t1 = t1_ref[...]
    t2_real = t2_ref[0]
    t2_imag = t2_ref[1]
    half = t2_real.shape[0] // 2
    feeds = v_ref.shape[0]

    def one_frame(pieces):
        acc = None
        for tap in range(TAPS):
            term = w_ref[tap][None] * pieces[tap]
            acc = term if acc is None else acc + term
        block = acc.astype(jnp.bfloat16).reshape(2 * CHA, CHB)
        section = jnp.dot(t1, block, preferred_element_type=jnp.float32)
        sec_real = section[:CHA]
        sec_imag = section[CHA:]
        turned_real = sec_real * cos_tw - sec_imag * sin_tw
        turned_imag = sec_real * sin_tw + sec_imag * cos_tw
        return turned_real.astype(jnp.bfloat16), turned_imag.astype(jnp.bfloat16)

    def pair(feed, step):
        g_real = g_ref[feed, 0].astype(jnp.float32)
        g_imag = g_ref[feed, 1].astype(jnp.float32)
        pieces = []
        for offset in range(TAPS + 1):
            start = pl.multiple_of((2 * (step - first_pair) + offset) * CHA, CHA)
            pieces.append(v_ref[feed, :, pl.ds(start, CHA), :].astype(jnp.float32))
        first_real, first_imag = one_frame(pieces[:TAPS])
        second_real, second_imag = one_frame(pieces[1:])
        both_real = jnp.concatenate([first_real, second_real], axis=0)
        both_imag = jnp.concatenate([first_imag, second_imag], axis=0)
        dims = (((1,), (1,)), ((), ()))
        spectrum = lax.dot_general(
            t2_real, both_real, dims, preferred_element_type=jnp.float32
        ) + lax.dot_general(t2_imag, both_imag, dims, preferred_element_type=jnp.float32)
        spec_real = spectrum[:half]
        spec_imag = spectrum[half:]
        out_real = spec_real * g_real - spec_imag * g_imag
        out_imag = spec_real * g_imag + spec_imag * g_real
        lanes = pl.ds(pl.multiple_of((step - first_pair) * 2 * CHA, 2 * CHA), 2 * CHA)
        o_ref[0, feed, :, lanes] = out_real.astype(o_ref.dtype)
        o_ref[1, feed, :, lanes] = out_imag.astype(o_ref.dtype)

    for feed in range(feeds):
        for step in range(first_pair, first_pair + pairs):
            pair(feed, step)


def beam_kernel(dish_count, carry_in, finish, lanes, *refs):
    x_ref, t_ref, c_ref, s_ref = refs[:4]
    init_ref = refs[4] if carry_in else None
    out_refs = refs[4 + carry_in : -1]
    acc_ref = refs[-1]
    step = pl.program_id(0)
    devices = x_ref.shape[0] // dish_count
    rows = x_ref.shape[2]
    grid_len = t_ref.shape[1] // 2
    lane_window = slice(None)

    @pl.when(step == 0)
    def _():
        if carry_in:
            acc_ref[...] = init_ref[...]
        else:
            acc_ref[...] = jnp.zeros_like(acc_ref)

    parts = []
    for d in range(dish_count):
        block = x_ref[pl.ds(d * devices, devices), :, :, lane_window].reshape(
            2 * rows * devices, lanes
        )
        sums = jnp.dot(t_ref[d], block, preferred_element_type=jnp.float32)
        sum_real = sums[:grid_len]
        sum_imag = sums[grid_len:]
        cos_d = c_ref[d]
        sin_d = s_ref[d]
        part_real = sum_real * cos_d - sum_imag * sin_d
        part_imag = sum_real * sin_d + sum_imag * cos_d
        parts.append(
            (
                part_real.astype(jnp.bfloat16).astype(jnp.float32),
                part_imag.astype(jnp.bfloat16).astype(jnp.float32),
            )
        )
    (a_re, a_im), (b_re, b_im), (c_re, c_im), (d_re, d_im) = parts
    beams = [
        (a_re + b_re + c_re + d_re, a_im + b_im + c_im + d_im),
        (a_re + b_im - c_re - d_im, a_im - b_re - c_im + d_re),
        (a_re - b_re + c_re - d_re, a_im - b_im + c_im - d_im),
        (a_re - b_im - c_re + d_im, a_im + b_re - c_im - d_re),
    ]
    for q in range(dish_count):
        beam_real, beam_imag = beams[q]
        acc_ref[q] += beam_real * beam_real + beam_imag * beam_imag

    @pl.when(step == pl.num_programs(0) - 1)
    def _():
        if not finish:
            out_refs[0][...] = acc_ref[...]
            return
        me = lax.axis_index("dish")
        width = out_refs[0].shape[0]
        for shift in range(dish_count):
            target = jnp.bitwise_xor(me, shift)
            beam_index = jnp.bitwise_or(
                jnp.left_shift(jnp.bitwise_and(target, 1), 1), jnp.right_shift(target, 1)
            )
            total = acc_ref[beam_index]
            folded = total[:, :CHB]
            for k in range(1, lanes // CHB):
                folded = folded + total[:, k * CHB : (k + 1) * CHB]
            folded = folded + pltpu.roll(folded, width, 1)
            flipped = jnp.transpose(folded, (1, 0))
            out_refs[shift][...] = flipped[:width] * (0.25 / FRAMES)


def body(voltages, feed_gains, block_assign, grid_rows):
    dish_rows = voltages.shape[0]
    block_count = lax.axis_size("freq")
    dish_count = lax.axis_size("dish")
    block_width = NCHAN // block_count
    quarter = block_width // dish_count
    dests = block_count * dish_count
    grid_len = dish_rows * block_count
    total_dishes = grid_len * dish_count
    samples = voltages.shape[-1]

    dest = jnp.arange(dests, dtype=jnp.int32)
    dest_quarter = dest // block_count
    dest_block = jnp.tile(block_assign, dish_count)
    dest_e = dest_block * dish_count + dest_quarter
    picks_e = (dest_e[:, None] == jnp.arange(dests, dtype=jnp.int32)[None, :]).astype(jnp.bfloat16)

    window = jnp.asarray(window_constant().reshape(TAPS, CHA, CHB))
    first_cos, first_sin = table_constant(CHA, CHA, CHA, 1.0 / math.sqrt(CHA))
    first_table = np.block([[first_cos, first_sin], [-first_sin, first_cos]])
    first_table = jnp.asarray(first_table)
    twiddle = jnp.asarray(np.stack(rotation_constant(CHA, CHB, NCHAN), axis=0))
    second_cos, second_sin = table_constant(CHB, CHB, CHB, 1.0 / math.sqrt(CHB))
    second_table = np.stack(
        [np.stack([second_cos, -second_sin], axis=0), np.stack([second_sin, second_cos], axis=0)],
        axis=0,
    )
    second_table = jnp.einsum(
        "je,qseb->qsjb", picks_e, jnp.asarray(second_table), preferred_element_type=jnp.float32
    ).astype(jnp.bfloat16).reshape(2, 2 * dests, CHB)
    gains = feed_gains[:, 0].reshape(dish_rows, 2, CHB, CHA)
    gains = jnp.einsum("je,rpec->rpjc", picks_e, gains, preferred_element_type=jnp.float32)
    gains = jnp.concatenate([gains, gains], axis=3).astype(jnp.bfloat16)

    chunk_pairs = [4, 4]
    chunks = len(chunk_pairs)
    tables = beam_tables(grid_rows, grid_len, dish_rows)
    feed_index = jnp.arange(dish_count, dtype=jnp.int32)
    positions = jnp.arange(grid_len, dtype=jnp.int32)
    twist_cos, twist_sin = rotation_constant(dish_count, grid_len, total_dishes)
    twist_cos = jnp.asarray(twist_cos[:, :, None])
    twist_sin = jnp.asarray(twist_sin[:, :, None])
    lane_block = 4 * quarter

    volts = voltages[:, 0].astype(jnp.float32).reshape(dish_rows, 2, samples // CHB, CHB)

    def channelize_chunk(chunk):
        pairs = chunk_pairs[chunk]
        first_pair = sum(chunk_pairs[:chunk])
        chunk_lanes = pairs * 2 * quarter
        span = (2 * pairs + TAPS - 1) * CHA
        first_row = 2 * first_pair * CHA
        return pl.pallas_call(
            functools.partial(channelize_kernel, first_pair, pairs),
            grid=(dish_rows // FEEDS_PER_STEP,),
            in_specs=[
                pl.BlockSpec(
                    (pl.Element(FEEDS_PER_STEP), pl.Element(2), pl.Element(span), pl.Element(CHB)),
                    lambda r: (r * FEEDS_PER_STEP, 0, first_row, 0),
                ),
                pl.BlockSpec((TAPS, CHA, CHB), lambda r: (0, 0, 0)),
                pl.BlockSpec((2 * CHA, 2 * CHA), lambda r: (0, 0)),
                pl.BlockSpec((2, CHA, CHB), lambda r: (0, 0, 0)),
                pl.BlockSpec((2, 2 * dests, CHB), lambda r: (0, 0, 0)),
                pl.BlockSpec((FEEDS_PER_STEP, 2, dests, 2 * CHA), lambda r: (r, 0, 0, 0)),
            ],
            out_specs=pl.BlockSpec((2, FEEDS_PER_STEP, dests, chunk_lanes), lambda r: (0, r, 0, 0)),
            out_shape=jax.ShapeDtypeStruct((2, dish_rows, dests, chunk_lanes), jnp.bfloat16),
            cost_estimate=pl.CostEstimate(
                flops=int(dish_rows * pairs * 2 * 2 * 128 * 128 * 128 * 3),
                bytes_accessed=int(voltages.size * 2 + 2 * dish_rows * dests * chunk_lanes * 2),
                transcendentals=0,
            ),
        )(volts, window, first_table, twiddle, second_table, gains)

    def beamform_chunk(received, carried, finish):
        carry_in = carried is not None
        chunk_lanes = received.shape[3]
        in_specs = [
            pl.BlockSpec((dests, 2, dish_rows, lane_block), lambda f: (0, 0, 0, f)),
            pl.BlockSpec((dish_count, 2 * grid_len, 2 * grid_len), lambda f: (0, 0, 0)),
        ]
        in_specs += [pl.BlockSpec((dish_count, grid_len, 1), lambda f: (0, 0, 0))] * 2
        operands = [received, tables, twist_cos, twist_sin]
        if carry_in:
            in_specs.append(pl.BlockSpec((dish_count, grid_len, lane_block), lambda f: (0, 0, 0)))
            operands.append(carried)
        if finish:
            out_specs = [pl.BlockSpec((quarter, grid_len), lambda f: (0, 0))] * dish_count
            out_shape = [jax.ShapeDtypeStruct((quarter, grid_len), jnp.float32)] * dish_count
        else:
            out_specs = pl.BlockSpec((dish_count, grid_len, lane_block), lambda f: (0, 0, 0))
            out_shape = jax.ShapeDtypeStruct((dish_count, grid_len, lane_block), jnp.float32)
        return pl.pallas_call(
            functools.partial(beam_kernel, dish_count, carry_in, finish, lane_block),
            grid=(chunk_lanes // lane_block,),
            in_specs=in_specs,
            out_specs=out_specs,
            out_shape=out_shape,
            scratch_shapes=[pltpu.VMEM((dish_count, grid_len, lane_block), jnp.float32)],
            cost_estimate=pl.CostEstimate(
                flops=int(dish_count * 2 * 512 * 512 * chunk_lanes),
                bytes_accessed=int(received.size * 2 + tables.size * 2),
                transcendentals=0,
            ),
        )(*operands)

    sent = [channelize_chunk(c) for c in range(chunks)]
    arrived = [
        jnp.transpose(lax.all_to_all(s, ("dish", "freq"), 2, 2, tiled=True), (2, 0, 1, 3))
        for s in sent
    ]
    carried = None
    for c in range(chunks):
        carried = beamform_chunk(arrived[c], carried, c == chunks - 1)
    powers = carried

    me = lax.axis_index("dish")
    pieces = [powers[0]]
    for shift in range(1, dish_count):
        outgoing = powers[shift]
        pairs_list = [(i, i ^ shift) for i in range(dish_count)]
        pieces.append(lax.ppermute(outgoing, "dish", pairs_list))
    blocks = []
    for source in range(dish_count):
        shift_of = jnp.bitwise_xor(me, source)
        chosen = pieces[dish_count - 1]
        for shift in range(dish_count - 2, -1, -1):
            chosen = jnp.where(shift_of == shift, pieces[shift], chosen)
        blocks.append(chosen)
    return jnp.concatenate(blocks, axis=0)


def solution(mesh):
    placed = (P("freq", "dish", None, None), P("freq", "dish", None, None), P(), P())
    return jax.shard_map(
        body, mesh=mesh, in_specs=placed, out_specs=P("freq", "dish"), check_vma=False
    )
```

```python
import functools
import math

import jax
import jax.numpy as jnp
import ml_dtypes
import numpy as np
from jax import lax
from jax.experimental import pallas as pl
from jax.experimental.pallas import tpu as pltpu
from jax.sharding import PartitionSpec as P

NCHAN = 8192
CHA = 64
CHB = 128
TAPS = 4
FRAMES = 16
FEEDS_PER_STEP = 4


full_turn = 2.0 * math.pi


def table_constant(row_count, col_count, modulus, scaling):
    rows = np.arange(row_count, dtype=np.int64)[:, None]
    cols = np.arange(col_count, dtype=np.int64)[None, :]
    angles = np.float32(full_turn / modulus) * (rows * cols % modulus).astype(np.float32)
    cosine = (np.cos(angles.astype(np.float64)) * scaling).astype(ml_dtypes.bfloat16)
    sine = (np.sin(angles.astype(np.float64)) * scaling).astype(ml_dtypes.bfloat16)
    return cosine, sine


def window_constant():
    sample_index = np.arange(TAPS * NCHAN, dtype=np.float64)
    centred = (sample_index - TAPS * NCHAN / 2 + 0.5) / NCHAN
    taper_curve = 0.5 - 0.5 * np.cos(full_turn * (sample_index + 0.5) / (TAPS * NCHAN))
    shaped_window = (np.sinc(centred) * taper_curve).reshape(TAPS, NCHAN)
    energy = np.mean(np.sum(shaped_window * shaped_window, axis=0))
    return (shaped_window / np.sqrt(energy)).astype(np.float32)


def rotation_constant(row_count, col_count, modulus):
    rows = np.arange(row_count, dtype=np.int64)[:, None]
    cols = np.arange(col_count, dtype=np.int64)[None, :]
    angles = np.float32(-(full_turn / modulus)) * (rows * cols % modulus).astype(np.float32)
    angles = angles.astype(np.float64)
    return np.cos(angles).astype(np.float32), np.sin(angles).astype(np.float32)


def fourier_table(row_index, col_index, modulus, scaling):
    phases = row_index[:, None] * col_index[None, :] % modulus
    angles = full_turn / modulus * phases.astype(jnp.float32)
    cosine_table = (jnp.cos(angles) * scaling).astype(jnp.bfloat16)
    sine_table = (jnp.sin(angles) * scaling).astype(jnp.bfloat16)
    upper_rows = jnp.stack([cosine_table, -sine_table], axis=1)
    lower_rows = jnp.stack([sine_table, cosine_table], axis=1)
    return jnp.stack([upper_rows, lower_rows], axis=0)


def filter_window():
    sample_index = jnp.arange(TAPS * NCHAN, dtype=jnp.float32)
    centred = (sample_index - TAPS * NCHAN / 2 + 0.5) / NCHAN
    taper_curve = 0.5 - 0.5 * jnp.cos(full_turn * (sample_index + 0.5) / (TAPS * NCHAN))
    shaped_window = (jnp.sinc(centred) * taper_curve).reshape(TAPS, NCHAN)
    energy = jnp.mean(jnp.sum(shaped_window * shaped_window, axis=0))
    return shaped_window / jnp.sqrt(energy)


def beam_tables(grid_rows, grid_len, rows_per_device):
    positions = jnp.arange(grid_len, dtype=jnp.int32)
    cosine_base, sine_base = table_constant(grid_len, grid_len, grid_len, 1.0 / math.sqrt(grid_len))
    cosine_base = jnp.asarray(cosine_base)
    sine_base = jnp.asarray(sine_base)
    devices = grid_len // rows_per_device
    picks = (positions[None, :, None] == grid_rows[:, None, :]).astype(jnp.bfloat16)
    cosine_table = jnp.einsum(
        "jg,dgm->djm", cosine_base, picks, preferred_element_type=jnp.float32
    ).astype(jnp.bfloat16)
    sine_table = jnp.einsum(
        "jg,dgm->djm", sine_base, picks, preferred_element_type=jnp.float32
    ).astype(jnp.bfloat16)
    shape = (grid_rows.shape[0], grid_len, devices, 1, rows_per_device)
    cosine_table = cosine_table.reshape(shape)
    sine_table = sine_table.reshape(shape)
    real_rows = jnp.concatenate([cosine_table, sine_table], axis=3)
    imag_rows = jnp.concatenate([-sine_table, cosine_table], axis=3)
    rows = jnp.concatenate([real_rows, imag_rows], axis=1)
    return rows.reshape(grid_rows.shape[0], 2 * grid_len, 2 * grid_len)


def channelize_kernel(
    first_pair, pairs, v_ref, w_ref, t1_ref, tw_ref, t2_ref, g_ref, pe_ref, dup_ref, o_ref
):
    cos_tw = tw_ref[0]
    sin_tw = tw_ref[1]
    t1 = t1_ref[...]
    t2_real = t2_ref[0]
    t2_imag = t2_ref[1]
    half = t2_real.shape[0] // 2
    feeds = v_ref.shape[0]

    def one_frame(pieces):
        acc = None
        for tap in range(TAPS):
            term = w_ref[tap][None] * pieces[tap]
            acc = term if acc is None else acc + term
        block = acc.astype(jnp.bfloat16).reshape(2 * CHA, CHB)
        section = jnp.dot(t1, block, preferred_element_type=jnp.float32)
        sec_real = section[:CHA]
        sec_imag = section[CHA:]
        turned_real = sec_real * cos_tw - sec_imag * sin_tw
        turned_imag = sec_real * sin_tw + sec_imag * cos_tw
        return turned_real.astype(jnp.bfloat16), turned_imag.astype(jnp.bfloat16)

    def feed_gains(feed, part):
        picked = jnp.dot(pe_ref[...], g_ref[feed, part], preferred_element_type=jnp.float32)
        return jnp.dot(picked.astype(jnp.bfloat16), dup_ref[...], preferred_element_type=jnp.float32)

    def pair(feed, step, g_real, g_imag):
        pieces = []
        for offset in range(TAPS + 1):
            start = pl.multiple_of((2 * (step - first_pair) + offset) * CHA, CHA)
            pieces.append(v_ref[feed, :, pl.ds(start, CHA), :].astype(jnp.float32))
        first_real, first_imag = one_frame(pieces[:TAPS])
        second_real, second_imag = one_frame(pieces[1:])
        both_real = jnp.concatenate([first_real, second_real], axis=0)
        both_imag = jnp.concatenate([first_imag, second_imag], axis=0)
        dims = (((1,), (1,)), ((), ()))
        spectrum = lax.dot_general(
            t2_real, both_real, dims, preferred_element_type=jnp.float32
        ) + lax.dot_general(t2_imag, both_imag, dims, preferred_element_type=jnp.float32)
        spec_real = spectrum[:half]
        spec_imag = spectrum[half:]
        out_real = spec_real * g_real - spec_imag * g_imag
        out_imag = spec_real * g_imag + spec_imag * g_real
        lanes = pl.ds(pl.multiple_of((step - first_pair) * 2 * CHA, 2 * CHA), 2 * CHA)
        o_ref[0, feed, :, lanes] = out_real.astype(o_ref.dtype)
        o_ref[1, feed, :, lanes] = out_imag.astype(o_ref.dtype)

    for feed in range(feeds):
        g_real = feed_gains(feed, 0)
        g_imag = feed_gains(feed, 1)
        for step in range(first_pair, first_pair + pairs):
            pair(feed, step, g_real, g_imag)


def beam_kernel(dish_count, carry_in, finish, lanes, *refs):
    x_ref, t_ref, c_ref, s_ref = refs[:4]
    init_ref = refs[4] if carry_in else None
    out_refs = refs[4 + carry_in : -1]
    acc_ref = refs[-1]
    step = pl.program_id(0)
    devices = x_ref.shape[0] // dish_count
    rows = x_ref.shape[2]
    grid_len = t_ref.shape[1] // 2
    lane_window = slice(None)

    @pl.when(step == 0)
    def _():
        if carry_in:
            acc_ref[...] = init_ref[...]
        else:
            acc_ref[...] = jnp.zeros_like(acc_ref)

    parts = []
    for d in range(dish_count):
        block = x_ref[pl.ds(d * devices, devices), :, :, lane_window].reshape(
            2 * rows * devices, lanes
        )
        sums = jnp.dot(t_ref[d], block, preferred_element_type=jnp.float32)
        sum_real = sums[:grid_len]
        sum_imag = sums[grid_len:]
        cos_d = c_ref[d]
        sin_d = s_ref[d]
        part_real = sum_real * cos_d - sum_imag * sin_d
        part_imag = sum_real * sin_d + sum_imag * cos_d
        parts.append(
            (
                part_real.astype(jnp.bfloat16).astype(jnp.float32),
                part_imag.astype(jnp.bfloat16).astype(jnp.float32),
            )
        )
    (a_re, a_im), (b_re, b_im), (c_re, c_im), (d_re, d_im) = parts
    beams = [
        (a_re + b_re + c_re + d_re, a_im + b_im + c_im + d_im),
        (a_re + b_im - c_re - d_im, a_im - b_re - c_im + d_re),
        (a_re - b_re + c_re - d_re, a_im - b_im + c_im - d_im),
        (a_re - b_im - c_re + d_im, a_im + b_re - c_im - d_re),
    ]
    for q in range(dish_count):
        beam_real, beam_imag = beams[q]
        acc_ref[q] += beam_real * beam_real + beam_imag * beam_imag

    @pl.when(step == pl.num_programs(0) - 1)
    def _():
        if not finish:
            out_refs[0][...] = acc_ref[...]
            return
        me = lax.axis_index("dish")
        width = out_refs[0].shape[0]
        for shift in range(dish_count):
            target = jnp.bitwise_xor(me, shift)
            beam_index = jnp.bitwise_or(
                jnp.left_shift(jnp.bitwise_and(target, 1), 1), jnp.right_shift(target, 1)
            )
            total = acc_ref[beam_index]
            folded = total[:, :CHB]
            for k in range(1, lanes // CHB):
                folded = folded + total[:, k * CHB : (k + 1) * CHB]
            folded = folded + pltpu.roll(folded, width, 1)
            flipped = jnp.transpose(folded, (1, 0))
            out_refs[shift][...] = flipped[:width] * (0.25 / FRAMES)


def body(voltages, feed_gains, block_assign, grid_rows):
    dish_rows = voltages.shape[0]
    block_count = lax.axis_size("freq")
    dish_count = lax.axis_size("dish")
    block_width = NCHAN // block_count
    quarter = block_width // dish_count
    dests = block_count * dish_count
    grid_len = dish_rows * block_count
    total_dishes = grid_len * dish_count
    samples = voltages.shape[-1]

    dest = jnp.arange(dests, dtype=jnp.int32)
    dest_quarter = dest // block_count
    dest_block = jnp.tile(block_assign, dish_count)
    dest_e = dest_block * dish_count + dest_quarter
    picks_e = (dest_e[:, None] == jnp.arange(dests, dtype=jnp.int32)[None, :]).astype(jnp.bfloat16)

    window = jnp.asarray(window_constant().reshape(TAPS, CHA, CHB))
    first_cos, first_sin = table_constant(CHA, CHA, CHA, 1.0 / math.sqrt(CHA))
    first_table = np.block([[first_cos, first_sin], [-first_sin, first_cos]])
    first_table = jnp.asarray(first_table)
    twiddle = jnp.asarray(np.stack(rotation_constant(CHA, CHB, NCHAN), axis=0))
    second_cos, second_sin = table_constant(CHB, CHB, CHB, 1.0 / math.sqrt(CHB))
    second_table = np.stack(
        [np.stack([second_cos, -second_sin], axis=0), np.stack([second_sin, second_cos], axis=0)],
        axis=0,
    )
    second_table = jnp.einsum(
        "je,qseb->qsjb", picks_e, jnp.asarray(second_table), preferred_element_type=jnp.float32
    ).astype(jnp.bfloat16).reshape(2, 2 * dests, CHB)
    gains = feed_gains[:, 0].reshape(dish_rows, 2, CHB, CHA)
    lane_pick = np.arange(2 * CHA)[None, :] % CHA == np.arange(CHA)[:, None]
    duplicate = jnp.asarray(lane_pick.astype(ml_dtypes.bfloat16))

    chunk_pairs = [4, 4]
    chunks = len(chunk_pairs)
    tables = beam_tables(grid_rows, grid_len, dish_rows)
    feed_index = jnp.arange(dish_count, dtype=jnp.int32)
    positions = jnp.arange(grid_len, dtype=jnp.int32)
    twist_cos, twist_sin = rotation_constant(dish_count, grid_len, total_dishes)
    twist_cos = jnp.asarray(twist_cos[:, :, None])
    twist_sin = jnp.asarray(twist_sin[:, :, None])
    lane_block = 4 * quarter

    volts = voltages[:, 0].reshape(dish_rows, 2, samples // CHB, CHB)

    def channelize_chunk(chunk):
        pairs = chunk_pairs[chunk]
        first_pair = sum(chunk_pairs[:chunk])
        chunk_lanes = pairs * 2 * quarter
        span = (2 * pairs + TAPS - 1) * CHA
        first_row = 2 * first_pair * CHA
        return pl.pallas_call(
            functools.partial(channelize_kernel, first_pair, pairs),
            grid=(dish_rows // FEEDS_PER_STEP,),
            in_specs=[
                pl.BlockSpec(
                    (pl.Element(FEEDS_PER_STEP), pl.Element(2), pl.Element(span), pl.Element(CHB)),
                    lambda r: (r * FEEDS_PER_STEP, 0, first_row, 0),
                ),
                pl.BlockSpec((TAPS, CHA, CHB), lambda r: (0, 0, 0)),
                pl.BlockSpec((2 * CHA, 2 * CHA), lambda r: (0, 0)),
                pl.BlockSpec((2, CHA, CHB), lambda r: (0, 0, 0)),
                pl.BlockSpec((2, 2 * dests, CHB), lambda r: (0, 0, 0)),
                pl.BlockSpec((FEEDS_PER_STEP, 2, dests, CHA), lambda r: (r, 0, 0, 0)),
                pl.BlockSpec((dests, dests), lambda r: (0, 0)),
                pl.BlockSpec((CHA, 2 * CHA), lambda r: (0, 0)),
            ],
            out_specs=pl.BlockSpec((2, FEEDS_PER_STEP, dests, chunk_lanes), lambda r: (0, r, 0, 0)),
            out_shape=jax.ShapeDtypeStruct((2, dish_rows, dests, chunk_lanes), jnp.bfloat16),
            cost_estimate=pl.CostEstimate(
                flops=int(dish_rows * pairs * 2 * 2 * 128 * 128 * 128 * 3),
                bytes_accessed=int(voltages.size * 2 + 2 * dish_rows * dests * chunk_lanes * 2),
                transcendentals=0,
            ),
        )(volts, window, first_table, twiddle, second_table, gains, picks_e, duplicate)

    def beamform_chunk(received, carried, finish):
        carry_in = carried is not None
        chunk_lanes = received.shape[3]
        in_specs = [
            pl.BlockSpec((dests, 2, dish_rows, lane_block), lambda f: (0, 0, 0, f)),
            pl.BlockSpec((dish_count, 2 * grid_len, 2 * grid_len), lambda f: (0, 0, 0)),
        ]
        in_specs += [pl.BlockSpec((dish_count, grid_len, 1), lambda f: (0, 0, 0))] * 2
        operands = [received, tables, twist_cos, twist_sin]
        if carry_in:
            in_specs.append(pl.BlockSpec((dish_count, grid_len, lane_block), lambda f: (0, 0, 0)))
            operands.append(carried)
        if finish:
            out_specs = [pl.BlockSpec((quarter, grid_len), lambda f: (0, 0))] * dish_count
            out_shape = [jax.ShapeDtypeStruct((quarter, grid_len), jnp.float32)] * dish_count
        else:
            out_specs = pl.BlockSpec((dish_count, grid_len, lane_block), lambda f: (0, 0, 0))
            out_shape = jax.ShapeDtypeStruct((dish_count, grid_len, lane_block), jnp.float32)
        return pl.pallas_call(
            functools.partial(beam_kernel, dish_count, carry_in, finish, lane_block),
            grid=(chunk_lanes // lane_block,),
            in_specs=in_specs,
            out_specs=out_specs,
            out_shape=out_shape,
            scratch_shapes=[pltpu.VMEM((dish_count, grid_len, lane_block), jnp.float32)],
            cost_estimate=pl.CostEstimate(
                flops=int(dish_count * 2 * 512 * 512 * chunk_lanes),
                bytes_accessed=int(received.size * 2 + tables.size * 2),
                transcendentals=0,
            ),
        )(*operands)

    sent = [channelize_chunk(c) for c in range(chunks)]
    arrived = [
        jnp.transpose(lax.all_to_all(s, ("dish", "freq"), 2, 2, tiled=True), (2, 0, 1, 3))
        for s in sent
    ]
    carried = None
    for c in range(chunks):
        carried = beamform_chunk(arrived[c], carried, c == chunks - 1)
    powers = carried

    me = lax.axis_index("dish")
    pieces = [powers[0]]
    for shift in range(1, dish_count):
        outgoing = powers[shift]
        pairs_list = [(i, i ^ shift) for i in range(dish_count)]
        pieces.append(lax.ppermute(outgoing, "dish", pairs_list))
    blocks = []
    for source in range(dish_count):
        shift_of = jnp.bitwise_xor(me, source)
        chosen = pieces[dish_count - 1]
        for shift in range(dish_count - 2, -1, -1):
            chosen = jnp.where(shift_of == shift, pieces[shift], chosen)
        blocks.append(chosen)
    return jnp.concatenate(blocks, axis=0)


def solution(mesh):
    placed = (P("freq", "dish", None, None), P("freq", "dish", None, None), P(), P())
    return jax.shard_map(
        body, mesh=mesh, in_specs=placed, out_specs=P("freq", "dish"), check_vma=False
    )
```

```python
import functools
import math

import jax
import jax.numpy as jnp
import ml_dtypes
import numpy as np
from jax import lax
from jax.experimental import pallas as pl
from jax.experimental.pallas import tpu as pltpu
from jax.sharding import PartitionSpec as P

NCHAN = 8192
CHA = 64
CHB = 128
TAPS = 4
FRAMES = 16
FEEDS_PER_STEP = 4


full_turn = 2.0 * math.pi


def table_constant(row_count, col_count, modulus, scaling):
    rows = np.arange(row_count, dtype=np.int64)[:, None]
    cols = np.arange(col_count, dtype=np.int64)[None, :]
    angles = np.float32(full_turn / modulus) * (rows * cols % modulus).astype(np.float32)
    cosine = (np.cos(angles.astype(np.float64)) * scaling).astype(ml_dtypes.bfloat16)
    sine = (np.sin(angles.astype(np.float64)) * scaling).astype(ml_dtypes.bfloat16)
    return cosine, sine


def window_constant():
    sample_index = np.arange(TAPS * NCHAN, dtype=np.float64)
    centred = (sample_index - TAPS * NCHAN / 2 + 0.5) / NCHAN
    taper_curve = 0.5 - 0.5 * np.cos(full_turn * (sample_index + 0.5) / (TAPS * NCHAN))
    shaped_window = (np.sinc(centred) * taper_curve).reshape(TAPS, NCHAN)
    energy = np.mean(np.sum(shaped_window * shaped_window, axis=0))
    return (shaped_window / np.sqrt(energy)).astype(np.float32)


def rotation_constant(row_count, col_count, modulus):
    rows = np.arange(row_count, dtype=np.int64)[:, None]
    cols = np.arange(col_count, dtype=np.int64)[None, :]
    angles = np.float32(-(full_turn / modulus)) * (rows * cols % modulus).astype(np.float32)
    angles = angles.astype(np.float64)
    return np.cos(angles).astype(np.float32), np.sin(angles).astype(np.float32)


def fourier_table(row_index, col_index, modulus, scaling):
    phases = row_index[:, None] * col_index[None, :] % modulus
    angles = full_turn / modulus * phases.astype(jnp.float32)
    cosine_table = (jnp.cos(angles) * scaling).astype(jnp.bfloat16)
    sine_table = (jnp.sin(angles) * scaling).astype(jnp.bfloat16)
    upper_rows = jnp.stack([cosine_table, -sine_table], axis=1)
    lower_rows = jnp.stack([sine_table, cosine_table], axis=1)
    return jnp.stack([upper_rows, lower_rows], axis=0)


def filter_window():
    sample_index = jnp.arange(TAPS * NCHAN, dtype=jnp.float32)
    centred = (sample_index - TAPS * NCHAN / 2 + 0.5) / NCHAN
    taper_curve = 0.5 - 0.5 * jnp.cos(full_turn * (sample_index + 0.5) / (TAPS * NCHAN))
    shaped_window = (jnp.sinc(centred) * taper_curve).reshape(TAPS, NCHAN)
    energy = jnp.mean(jnp.sum(shaped_window * shaped_window, axis=0))
    return shaped_window / jnp.sqrt(energy)


def beam_tables(grid_rows, grid_len, rows_per_device):
    positions = jnp.arange(grid_len, dtype=jnp.int32)
    cosine_base, sine_base = table_constant(grid_len, grid_len, grid_len, 1.0 / math.sqrt(grid_len))
    cosine_base = jnp.asarray(cosine_base)
    sine_base = jnp.asarray(sine_base)
    devices = grid_len // rows_per_device
    picks = (positions[None, :, None] == grid_rows[:, None, :]).astype(jnp.bfloat16)
    cosine_table = jnp.einsum(
        "jg,dgm->djm", cosine_base, picks, preferred_element_type=jnp.float32
    ).astype(jnp.bfloat16)
    sine_table = jnp.einsum(
        "jg,dgm->djm", sine_base, picks, preferred_element_type=jnp.float32
    ).astype(jnp.bfloat16)
    shape = (grid_rows.shape[0], grid_len, devices, 1, rows_per_device)
    cosine_table = cosine_table.reshape(shape)
    sine_table = sine_table.reshape(shape)
    real_rows = jnp.concatenate([cosine_table, sine_table], axis=3)
    imag_rows = jnp.concatenate([-sine_table, cosine_table], axis=3)
    rows = jnp.concatenate([real_rows, imag_rows], axis=1)
    return rows.reshape(grid_rows.shape[0], 2 * grid_len, 2 * grid_len)


def channelize_kernel(first_pair, pairs, v_ref, w_ref, t1_ref, tw_ref, t2_ref, g_ref, o_ref):
    cos_tw = tw_ref[0]
    sin_tw = tw_ref[1]
    t1 = t1_ref[...]
    t2_real = t2_ref[0]
    t2_imag = t2_ref[1]
    half = t2_real.shape[0] // 2
    feeds = v_ref.shape[0]

    def one_frame(pieces):
        acc = None
        for tap in range(TAPS):
            term = w_ref[tap][None] * pieces[tap]
            acc = term if acc is None else acc + term
        block = acc.astype(jnp.bfloat16).reshape(2 * CHA, CHB)
        section = jnp.dot(t1, block, preferred_element_type=jnp.float32)
        sec_real = section[:CHA]
        sec_imag = section[CHA:]
        turned_real = sec_real * cos_tw - sec_imag * sin_tw
        turned_imag = sec_real * sin_tw + sec_imag * cos_tw
        return turned_real.astype(jnp.bfloat16), turned_imag.astype(jnp.bfloat16)

    def pair(feed, step):
        g_real = g_ref[feed, 0].astype(jnp.float32)
        g_imag = g_ref[feed, 1].astype(jnp.float32)
        pieces = []
        for offset in range(TAPS + 1):
            start = pl.multiple_of((2 * (step - first_pair) + offset) * CHA, CHA)
            pieces.append(v_ref[feed, :, pl.ds(start, CHA), :].astype(jnp.float32))
        first_real, first_imag = one_frame(pieces[:TAPS])
        second_real, second_imag = one_frame(pieces[1:])
        both_real = jnp.concatenate([first_real, second_real], axis=0)
        both_imag = jnp.concatenate([first_imag, second_imag], axis=0)
        dims = (((1,), (1,)), ((), ()))
        spectrum = lax.dot_general(
            t2_real, both_real, dims, preferred_element_type=jnp.float32
        ) + lax.dot_general(t2_imag, both_imag, dims, preferred_element_type=jnp.float32)
        spec_real = spectrum[:half]
        spec_imag = spectrum[half:]
        out_real = spec_real * g_real - spec_imag * g_imag
        out_imag = spec_real * g_imag + spec_imag * g_real
        lanes = pl.ds(pl.multiple_of((step - first_pair) * 2 * CHA, 2 * CHA), 2 * CHA)
        o_ref[0, feed, :, lanes] = out_real.astype(o_ref.dtype)
        o_ref[1, feed, :, lanes] = out_imag.astype(o_ref.dtype)

    for feed in range(feeds):
        for step in range(first_pair, first_pair + pairs):
            pair(feed, step)


def beam_kernel(dish_count, carry_in, finish, lanes, *refs):
    x_ref, t_ref, c_ref, s_ref = refs[:4]
    init_ref = refs[4] if carry_in else None
    out_refs = refs[4 + carry_in : -1]
    acc_ref = refs[-1]
    step = pl.program_id(0)
    devices = x_ref.shape[0] // dish_count
    rows = x_ref.shape[2]
    grid_len = t_ref.shape[1] // 2
    lane_window = slice(None)

    @pl.when(step == 0)
    def _():
        if carry_in:
            acc_ref[...] = init_ref[...]
        else:
            acc_ref[...] = jnp.zeros_like(acc_ref)

    parts = []
    for d in range(dish_count):
        block = x_ref[pl.ds(d * devices, devices), :, :, lane_window].reshape(
            2 * rows * devices, lanes
        )
        sums = jnp.dot(t_ref[d], block, preferred_element_type=jnp.float32)
        sum_real = sums[:grid_len]
        sum_imag = sums[grid_len:]
        cos_d = c_ref[d]
        sin_d = s_ref[d]
        part_real = sum_real * cos_d - sum_imag * sin_d
        part_imag = sum_real * sin_d + sum_imag * cos_d
        parts.append(
            (
                part_real.astype(jnp.bfloat16).astype(jnp.float32),
                part_imag.astype(jnp.bfloat16).astype(jnp.float32),
            )
        )
    (a_re, a_im), (b_re, b_im), (c_re, c_im), (d_re, d_im) = parts
    beams = [
        (a_re + b_re + c_re + d_re, a_im + b_im + c_im + d_im),
        (a_re + b_im - c_re - d_im, a_im - b_re - c_im + d_re),
        (a_re - b_re + c_re - d_re, a_im - b_im + c_im - d_im),
        (a_re - b_im - c_re + d_im, a_im + b_re - c_im - d_re),
    ]
    for q in range(dish_count):
        beam_real, beam_imag = beams[q]
        acc_ref[q] += beam_real * beam_real + beam_imag * beam_imag

    @pl.when(step == pl.num_programs(0) - 1)
    def _():
        if not finish:
            out_refs[0][...] = acc_ref[...]
            return
        me = lax.axis_index("dish")
        width = out_refs[0].shape[0]
        for shift in range(dish_count):
            target = jnp.bitwise_xor(me, shift)
            beam_index = jnp.bitwise_or(
                jnp.left_shift(jnp.bitwise_and(target, 1), 1), jnp.right_shift(target, 1)
            )
            total = acc_ref[beam_index]
            folded = total[:, :CHB]
            for k in range(1, lanes // CHB):
                folded = folded + total[:, k * CHB : (k + 1) * CHB]
            folded = folded + pltpu.roll(folded, width, 1)
            flipped = jnp.transpose(folded, (1, 0))
            out_refs[shift][...] = flipped[:width] * (0.25 / FRAMES)


def body(voltages, feed_gains, block_assign, grid_rows):
    dish_rows = voltages.shape[0]
    block_count = lax.axis_size("freq")
    dish_count = lax.axis_size("dish")
    block_width = NCHAN // block_count
    quarter = block_width // dish_count
    dests = block_count * dish_count
    grid_len = dish_rows * block_count
    total_dishes = grid_len * dish_count
    samples = voltages.shape[-1]

    dest = jnp.arange(dests, dtype=jnp.int32)
    dest_quarter = dest // block_count
    dest_block = jnp.tile(block_assign, dish_count)
    dest_e = dest_block * dish_count + dest_quarter
    picks_e = (dest_e[:, None] == jnp.arange(dests, dtype=jnp.int32)[None, :]).astype(jnp.bfloat16)

    window = jnp.asarray(window_constant().reshape(TAPS, CHA, CHB))
    first_cos, first_sin = table_constant(CHA, CHA, CHA, 1.0 / math.sqrt(CHA))
    first_table = np.block([[first_cos, first_sin], [-first_sin, first_cos]])
    first_table = jnp.asarray(first_table)
    twiddle = jnp.asarray(np.stack(rotation_constant(CHA, CHB, NCHAN), axis=0))
    second_cos, second_sin = table_constant(CHB, CHB, CHB, 1.0 / math.sqrt(CHB))
    second_table = np.stack(
        [np.stack([second_cos, -second_sin], axis=0), np.stack([second_sin, second_cos], axis=0)],
        axis=0,
    )
    second_table = jnp.einsum(
        "je,qseb->qsjb", picks_e, jnp.asarray(second_table), preferred_element_type=jnp.float32
    ).astype(jnp.bfloat16).reshape(2, 2 * dests, CHB)
    gains = feed_gains[:, 0].reshape(dish_rows, 2, CHB, CHA)
    gains = jnp.einsum("je,rpec->rpjc", picks_e, gains, preferred_element_type=jnp.float32)
    gains = jnp.concatenate([gains, gains], axis=3).astype(jnp.bfloat16)

    chunk_pairs = [8]
    chunks = len(chunk_pairs)
    tables = beam_tables(grid_rows, grid_len, dish_rows)
    feed_index = jnp.arange(dish_count, dtype=jnp.int32)
    positions = jnp.arange(grid_len, dtype=jnp.int32)
    twist_cos, twist_sin = rotation_constant(dish_count, grid_len, total_dishes)
    twist_cos = jnp.asarray(twist_cos[:, :, None])
    twist_sin = jnp.asarray(twist_sin[:, :, None])
    lane_block = 4 * quarter

    volts = voltages[:, 0].reshape(dish_rows, 2, samples // CHB, CHB)

    def channelize_chunk(chunk):
        pairs = chunk_pairs[chunk]
        first_pair = sum(chunk_pairs[:chunk])
        chunk_lanes = pairs * 2 * quarter
        span = (2 * pairs + TAPS - 1) * CHA
        first_row = 2 * first_pair * CHA
        return pl.pallas_call(
            functools.partial(channelize_kernel, first_pair, pairs),
            grid=(dish_rows // FEEDS_PER_STEP,),
            in_specs=[
                pl.BlockSpec(
                    (pl.Element(FEEDS_PER_STEP), pl.Element(2), pl.Element(span), pl.Element(CHB)),
                    lambda r: (r * FEEDS_PER_STEP, 0, first_row, 0),
                ),
                pl.BlockSpec((TAPS, CHA, CHB), lambda r: (0, 0, 0)),
                pl.BlockSpec((2 * CHA, 2 * CHA), lambda r: (0, 0)),
                pl.BlockSpec((2, CHA, CHB), lambda r: (0, 0, 0)),
                pl.BlockSpec((2, 2 * dests, CHB), lambda r: (0, 0, 0)),
                pl.BlockSpec((FEEDS_PER_STEP, 2, dests, 2 * CHA), lambda r: (r, 0, 0, 0)),
            ],
            out_specs=pl.BlockSpec((2, FEEDS_PER_STEP, dests, chunk_lanes), lambda r: (0, r, 0, 0)),
            out_shape=jax.ShapeDtypeStruct((2, dish_rows, dests, chunk_lanes), jnp.bfloat16),
            cost_estimate=pl.CostEstimate(
                flops=int(dish_rows * pairs * 2 * 2 * 128 * 128 * 128 * 3),
                bytes_accessed=int(voltages.size * 2 + 2 * dish_rows * dests * chunk_lanes * 2),
                transcendentals=0,
            ),
        )(volts, window, first_table, twiddle, second_table, gains)

    def beamform_chunk(received, carried, finish):
        carry_in = carried is not None
        chunk_lanes = received.shape[3]
        in_specs = [
            pl.BlockSpec((dests, 2, dish_rows, lane_block), lambda f: (0, 0, 0, f)),
            pl.BlockSpec((dish_count, 2 * grid_len, 2 * grid_len), lambda f: (0, 0, 0)),
        ]
        in_specs += [pl.BlockSpec((dish_count, grid_len, 1), lambda f: (0, 0, 0))] * 2
        operands = [received, tables, twist_cos, twist_sin]
        if carry_in:
            in_specs.append(pl.BlockSpec((dish_count, grid_len, lane_block), lambda f: (0, 0, 0)))
            operands.append(carried)
        if finish:
            out_specs = [pl.BlockSpec((quarter, grid_len), lambda f: (0, 0))] * dish_count
            out_shape = [jax.ShapeDtypeStruct((quarter, grid_len), jnp.float32)] * dish_count
        else:
            out_specs = pl.BlockSpec((dish_count, grid_len, lane_block), lambda f: (0, 0, 0))
            out_shape = jax.ShapeDtypeStruct((dish_count, grid_len, lane_block), jnp.float32)
        return pl.pallas_call(
            functools.partial(beam_kernel, dish_count, carry_in, finish, lane_block),
            grid=(chunk_lanes // lane_block,),
            in_specs=in_specs,
            out_specs=out_specs,
            out_shape=out_shape,
            scratch_shapes=[pltpu.VMEM((dish_count, grid_len, lane_block), jnp.float32)],
            cost_estimate=pl.CostEstimate(
                flops=int(dish_count * 2 * 512 * 512 * chunk_lanes),
                bytes_accessed=int(received.size * 2 + tables.size * 2),
                transcendentals=0,
            ),
        )(*operands)

    sent = [channelize_chunk(c) for c in range(chunks)]
    arrived = [
        jnp.transpose(lax.all_to_all(s, ("dish", "freq"), 2, 2, tiled=True), (2, 0, 1, 3))
        for s in sent
    ]
    carried = None
    for c in range(chunks):
        carried = beamform_chunk(arrived[c], carried, c == chunks - 1)
    powers = carried

    me = lax.axis_index("dish")
    pieces = [powers[0]]
    for shift in range(1, dish_count):
        outgoing = powers[shift]
        pairs_list = [(i, i ^ shift) for i in range(dish_count)]
        pieces.append(lax.ppermute(outgoing, "dish", pairs_list))
    blocks = []
    for source in range(dish_count):
        shift_of = jnp.bitwise_xor(me, source)
        chosen = pieces[dish_count - 1]
        for shift in range(dish_count - 2, -1, -1):
            chosen = jnp.where(shift_of == shift, pieces[shift], chosen)
        blocks.append(chosen)
    return jnp.concatenate(blocks, axis=0)


def solution(mesh):
    placed = (P("freq", "dish", None, None), P("freq", "dish", None, None), P(), P())
    return jax.shard_map(
        body, mesh=mesh, in_specs=placed, out_specs=P("freq", "dish"), check_vma=False
    )
```

```python
import functools
import math

import jax
import jax.numpy as jnp
import ml_dtypes
import numpy as np
from jax import lax
from jax.experimental import pallas as pl
from jax.experimental.pallas import tpu as pltpu
from jax.sharding import PartitionSpec as P

NCHAN = 8192
CHA = 64
CHB = 128
TAPS = 4
FRAMES = 16
FEEDS_PER_STEP = 4


full_turn = 2.0 * math.pi


def table_constant(row_count, col_count, modulus, scaling):
    rows = np.arange(row_count, dtype=np.int64)[:, None]
    cols = np.arange(col_count, dtype=np.int64)[None, :]
    angles = np.float32(full_turn / modulus) * (rows * cols % modulus).astype(np.float32)
    cosine = (np.cos(angles.astype(np.float64)) * scaling).astype(ml_dtypes.bfloat16)
    sine = (np.sin(angles.astype(np.float64)) * scaling).astype(ml_dtypes.bfloat16)
    return cosine, sine


def window_constant():
    sample_index = np.arange(TAPS * NCHAN, dtype=np.float64)
    centred = (sample_index - TAPS * NCHAN / 2 + 0.5) / NCHAN
    taper_curve = 0.5 - 0.5 * np.cos(full_turn * (sample_index + 0.5) / (TAPS * NCHAN))
    shaped_window = (np.sinc(centred) * taper_curve).reshape(TAPS, NCHAN)
    energy = np.mean(np.sum(shaped_window * shaped_window, axis=0))
    return (shaped_window / np.sqrt(energy)).astype(np.float32)


def rotation_constant(row_count, col_count, modulus):
    rows = np.arange(row_count, dtype=np.int64)[:, None]
    cols = np.arange(col_count, dtype=np.int64)[None, :]
    angles = np.float32(-(full_turn / modulus)) * (rows * cols % modulus).astype(np.float32)
    angles = angles.astype(np.float64)
    return np.cos(angles).astype(np.float32), np.sin(angles).astype(np.float32)


def fourier_table(row_index, col_index, modulus, scaling):
    phases = row_index[:, None] * col_index[None, :] % modulus
    angles = full_turn / modulus * phases.astype(jnp.float32)
    cosine_table = (jnp.cos(angles) * scaling).astype(jnp.bfloat16)
    sine_table = (jnp.sin(angles) * scaling).astype(jnp.bfloat16)
    upper_rows = jnp.stack([cosine_table, -sine_table], axis=1)
    lower_rows = jnp.stack([sine_table, cosine_table], axis=1)
    return jnp.stack([upper_rows, lower_rows], axis=0)


def filter_window():
    sample_index = jnp.arange(TAPS * NCHAN, dtype=jnp.float32)
    centred = (sample_index - TAPS * NCHAN / 2 + 0.5) / NCHAN
    taper_curve = 0.5 - 0.5 * jnp.cos(full_turn * (sample_index + 0.5) / (TAPS * NCHAN))
    shaped_window = (jnp.sinc(centred) * taper_curve).reshape(TAPS, NCHAN)
    energy = jnp.mean(jnp.sum(shaped_window * shaped_window, axis=0))
    return shaped_window / jnp.sqrt(energy)


def beam_tables(grid_rows, grid_len, rows_per_device):
    positions = jnp.arange(grid_len, dtype=jnp.int32)
    cosine_base, sine_base = table_constant(grid_len, grid_len, grid_len, 1.0 / math.sqrt(grid_len))
    cosine_base = jnp.asarray(cosine_base)
    sine_base = jnp.asarray(sine_base)
    devices = grid_len // rows_per_device
    picks = (positions[None, :, None] == grid_rows[:, None, :]).astype(jnp.bfloat16)
    cosine_table = jnp.einsum(
        "jg,dgm->djm", cosine_base, picks, preferred_element_type=jnp.float32
    ).astype(jnp.bfloat16)
    sine_table = jnp.einsum(
        "jg,dgm->djm", sine_base, picks, preferred_element_type=jnp.float32
    ).astype(jnp.bfloat16)
    shape = (grid_rows.shape[0], grid_len, devices, 1, rows_per_device)
    cosine_table = cosine_table.reshape(shape)
    sine_table = sine_table.reshape(shape)
    real_rows = jnp.concatenate([cosine_table, sine_table], axis=3)
    imag_rows = jnp.concatenate([-sine_table, cosine_table], axis=3)
    rows = jnp.concatenate([real_rows, imag_rows], axis=1)
    return rows.reshape(grid_rows.shape[0], 2 * grid_len, 2 * grid_len)


def channelize_kernel(first_pair, pairs, v_ref, w_ref, t1_ref, tw_ref, t2_ref, g_ref, o_ref):
    cos_tw = tw_ref[0]
    sin_tw = tw_ref[1]
    t1 = t1_ref[...]
    t2_real = t2_ref[0]
    t2_imag = t2_ref[1]
    half = t2_real.shape[0] // 2
    feeds = v_ref.shape[0]

    def one_frame(pieces):
        acc = None
        for tap in range(TAPS):
            term = w_ref[tap][None] * pieces[tap]
            acc = term if acc is None else acc + term
        block = acc.astype(jnp.bfloat16).reshape(2 * CHA, CHB)
        section = jnp.dot(t1, block, preferred_element_type=jnp.float32)
        sec_real = section[:CHA]
        sec_imag = section[CHA:]
        turned_real = sec_real * cos_tw - sec_imag * sin_tw
        turned_imag = sec_real * sin_tw + sec_imag * cos_tw
        return turned_real.astype(jnp.bfloat16), turned_imag.astype(jnp.bfloat16)

    def pair(feed, step, g_real, g_imag):
        pieces = []
        for offset in range(TAPS + 1):
            start = pl.multiple_of((2 * (step - first_pair) + offset) * CHA, CHA)
            pieces.append(v_ref[feed, :, pl.ds(start, CHA), :].astype(jnp.float32))
        first_real, first_imag = one_frame(pieces[:TAPS])
        second_real, second_imag = one_frame(pieces[1:])
        both_real = jnp.concatenate([first_real, second_real], axis=0)
        both_imag = jnp.concatenate([first_imag, second_imag], axis=0)
        dims = (((1,), (1,)), ((), ()))
        spectrum = lax.dot_general(
            t2_real, both_real, dims, preferred_element_type=jnp.float32
        ) + lax.dot_general(t2_imag, both_imag, dims, preferred_element_type=jnp.float32)
        spec_real = spectrum[:half]
        spec_imag = spectrum[half:]
        out_real = spec_real * g_real - spec_imag * g_imag
        out_imag = spec_real * g_imag + spec_imag * g_real
        lanes = pl.ds(pl.multiple_of((step - first_pair) * 2 * CHA, 2 * CHA), 2 * CHA)
        o_ref[0, feed, :, lanes] = out_real.astype(o_ref.dtype)
        o_ref[1, feed, :, lanes] = out_imag.astype(o_ref.dtype)

    for feed in range(feeds):
        g_half_real = g_ref[feed, 0].astype(jnp.float32)
        g_half_imag = g_ref[feed, 1].astype(jnp.float32)
        g_real = jnp.concatenate([g_half_real, g_half_real], axis=1)
        g_imag = jnp.concatenate([g_half_imag, g_half_imag], axis=1)
        for step in range(first_pair, first_pair + pairs):
            pair(feed, step, g_real, g_imag)


def beam_kernel(dish_count, carry_in, finish, lanes, *refs):
    x_ref, t_ref, c_ref, s_ref = refs[:4]
    init_ref = refs[4] if carry_in else None
    out_refs = refs[4 + carry_in : -1]
    acc_ref = refs[-1]
    step = pl.program_id(0)
    devices = x_ref.shape[0] // dish_count
    rows = x_ref.shape[2]
    grid_len = t_ref.shape[1] // 2
    lane_window = slice(None)

    @pl.when(step == 0)
    def _():
        if carry_in:
            acc_ref[...] = init_ref[...]
        else:
            acc_ref[...] = jnp.zeros_like(acc_ref)

    parts = []
    for d in range(dish_count):
        block = x_ref[pl.ds(d * devices, devices), :, :, lane_window].reshape(
            2 * rows * devices, lanes
        )
        sums = jnp.dot(t_ref[d], block, preferred_element_type=jnp.float32)
        sum_real = sums[:grid_len]
        sum_imag = sums[grid_len:]
        cos_d = c_ref[d]
        sin_d = s_ref[d]
        part_real = sum_real * cos_d - sum_imag * sin_d
        part_imag = sum_real * sin_d + sum_imag * cos_d
        parts.append(
            (
                part_real.astype(jnp.bfloat16).astype(jnp.float32),
                part_imag.astype(jnp.bfloat16).astype(jnp.float32),
            )
        )
    (a_re, a_im), (b_re, b_im), (c_re, c_im), (d_re, d_im) = parts
    beams = [
        (a_re + b_re + c_re + d_re, a_im + b_im + c_im + d_im),
        (a_re + b_im - c_re - d_im, a_im - b_re - c_im + d_re),
        (a_re - b_re + c_re - d_re, a_im - b_im + c_im - d_im),
        (a_re - b_im - c_re + d_im, a_im + b_re - c_im - d_re),
    ]
    for q in range(dish_count):
        beam_real, beam_imag = beams[q]
        acc_ref[q] += beam_real * beam_real + beam_imag * beam_imag

    @pl.when(step == pl.num_programs(0) - 1)
    def _():
        if not finish:
            out_refs[0][...] = acc_ref[...]
            return
        me = lax.axis_index("dish")
        width = out_refs[0].shape[0]
        for shift in range(dish_count):
            target = jnp.bitwise_xor(me, shift)
            beam_index = jnp.bitwise_or(
                jnp.left_shift(jnp.bitwise_and(target, 1), 1), jnp.right_shift(target, 1)
            )
            total = acc_ref[beam_index]
            folded = total[:, :CHB]
            for k in range(1, lanes // CHB):
                folded = folded + total[:, k * CHB : (k + 1) * CHB]
            folded = folded + pltpu.roll(folded, width, 1)
            flipped = jnp.transpose(folded, (1, 0))
            out_refs[shift][...] = flipped[:width] * (0.25 / FRAMES)


def body(voltages, feed_gains, block_assign, grid_rows):
    dish_rows = voltages.shape[0]
    block_count = lax.axis_size("freq")
    dish_count = lax.axis_size("dish")
    block_width = NCHAN // block_count
    quarter = block_width // dish_count
    dests = block_count * dish_count
    grid_len = dish_rows * block_count
    total_dishes = grid_len * dish_count
    samples = voltages.shape[-1]

    dest = jnp.arange(dests, dtype=jnp.int32)
    dest_quarter = dest // block_count
    dest_block = jnp.tile(block_assign, dish_count)
    dest_e = dest_block * dish_count + dest_quarter
    picks_e = (dest_e[:, None] == jnp.arange(dests, dtype=jnp.int32)[None, :]).astype(jnp.bfloat16)

    window = jnp.asarray(window_constant().reshape(TAPS, CHA, CHB))
    first_cos, first_sin = table_constant(CHA, CHA, CHA, 1.0 / math.sqrt(CHA))
    first_table = np.block([[first_cos, first_sin], [-first_sin, first_cos]])
    first_table = jnp.asarray(first_table)
    twiddle = jnp.asarray(np.stack(rotation_constant(CHA, CHB, NCHAN), axis=0))
    second_cos, second_sin = table_constant(CHB, CHB, CHB, 1.0 / math.sqrt(CHB))
    second_table = np.stack(
        [np.stack([second_cos, -second_sin], axis=0), np.stack([second_sin, second_cos], axis=0)],
        axis=0,
    )
    second_table = jnp.einsum(
        "je,qseb->qsjb", picks_e, jnp.asarray(second_table), preferred_element_type=jnp.float32
    ).astype(jnp.bfloat16).reshape(2, 2 * dests, CHB)
    gains = feed_gains[:, 0].reshape(dish_rows, 2, CHB, CHA)
    gains = jnp.einsum("je,rpec->rpjc", picks_e, gains, preferred_element_type=jnp.float32)
    gains = gains.astype(jnp.bfloat16)

    chunk_pairs = [8]
    chunks = len(chunk_pairs)
    tables = beam_tables(grid_rows, grid_len, dish_rows)
    feed_index = jnp.arange(dish_count, dtype=jnp.int32)
    positions = jnp.arange(grid_len, dtype=jnp.int32)
    twist_cos, twist_sin = rotation_constant(dish_count, grid_len, total_dishes)
    twist_cos = jnp.asarray(twist_cos[:, :, None])
    twist_sin = jnp.asarray(twist_sin[:, :, None])
    lane_block = 4 * quarter

    volts = voltages[:, 0].reshape(dish_rows, 2, samples // CHB, CHB)

    def channelize_chunk(chunk):
        pairs = chunk_pairs[chunk]
        first_pair = sum(chunk_pairs[:chunk])
        chunk_lanes = pairs * 2 * quarter
        span = (2 * pairs + TAPS - 1) * CHA
        first_row = 2 * first_pair * CHA
        return pl.pallas_call(
            functools.partial(channelize_kernel, first_pair, pairs),
            grid=(dish_rows // FEEDS_PER_STEP,),
            in_specs=[
                pl.BlockSpec(
                    (pl.Element(FEEDS_PER_STEP), pl.Element(2), pl.Element(span), pl.Element(CHB)),
                    lambda r: (r * FEEDS_PER_STEP, 0, first_row, 0),
                ),
                pl.BlockSpec((TAPS, CHA, CHB), lambda r: (0, 0, 0)),
                pl.BlockSpec((2 * CHA, 2 * CHA), lambda r: (0, 0)),
                pl.BlockSpec((2, CHA, CHB), lambda r: (0, 0, 0)),
                pl.BlockSpec((2, 2 * dests, CHB), lambda r: (0, 0, 0)),
                pl.BlockSpec((FEEDS_PER_STEP, 2, dests, CHA), lambda r: (r, 0, 0, 0)),
            ],
            out_specs=pl.BlockSpec((2, FEEDS_PER_STEP, dests, chunk_lanes), lambda r: (0, r, 0, 0)),
            out_shape=jax.ShapeDtypeStruct((2, dish_rows, dests, chunk_lanes), jnp.bfloat16),
            cost_estimate=pl.CostEstimate(
                flops=int(dish_rows * pairs * 2 * 2 * 128 * 128 * 128 * 3),
                bytes_accessed=int(voltages.size * 2 + 2 * dish_rows * dests * chunk_lanes * 2),
                transcendentals=0,
            ),
        )(volts, window, first_table, twiddle, second_table, gains)

    def beamform_chunk(received, carried, finish):
        carry_in = carried is not None
        chunk_lanes = received.shape[3]
        in_specs = [
            pl.BlockSpec((dests, 2, dish_rows, lane_block), lambda f: (0, 0, 0, f)),
            pl.BlockSpec((dish_count, 2 * grid_len, 2 * grid_len), lambda f: (0, 0, 0)),
        ]
        in_specs += [pl.BlockSpec((dish_count, grid_len, 1), lambda f: (0, 0, 0))] * 2
        operands = [received, tables, twist_cos, twist_sin]
        if carry_in:
            in_specs.append(pl.BlockSpec((dish_count, grid_len, lane_block), lambda f: (0, 0, 0)))
            operands.append(carried)
        if finish:
            out_specs = [pl.BlockSpec((quarter, grid_len), lambda f: (0, 0))] * dish_count
            out_shape = [jax.ShapeDtypeStruct((quarter, grid_len), jnp.float32)] * dish_count
        else:
            out_specs = pl.BlockSpec((dish_count, grid_len, lane_block), lambda f: (0, 0, 0))
            out_shape = jax.ShapeDtypeStruct((dish_count, grid_len, lane_block), jnp.float32)
        return pl.pallas_call(
            functools.partial(beam_kernel, dish_count, carry_in, finish, lane_block),
            grid=(chunk_lanes // lane_block,),
            in_specs=in_specs,
            out_specs=out_specs,
            out_shape=out_shape,
            scratch_shapes=[pltpu.VMEM((dish_count, grid_len, lane_block), jnp.float32)],
            cost_estimate=pl.CostEstimate(
                flops=int(dish_count * 2 * 512 * 512 * chunk_lanes),
                bytes_accessed=int(received.size * 2 + tables.size * 2),
                transcendentals=0,
            ),
        )(*operands)

    sent = [channelize_chunk(c) for c in range(chunks)]
    arrived = [
        jnp.transpose(lax.all_to_all(s, ("dish", "freq"), 2, 2, tiled=True), (2, 0, 1, 3))
        for s in sent
    ]
    carried = None
    for c in range(chunks):
        carried = beamform_chunk(arrived[c], carried, c == chunks - 1)
    powers = carried

    me = lax.axis_index("dish")
    pieces = [powers[0]]
    for shift in range(1, dish_count):
        outgoing = powers[shift]
        pairs_list = [(i, i ^ shift) for i in range(dish_count)]
        pieces.append(lax.ppermute(outgoing, "dish", pairs_list))
    blocks = []
    for source in range(dish_count):
        shift_of = jnp.bitwise_xor(me, source)
        chosen = pieces[dish_count - 1]
        for shift in range(dish_count - 2, -1, -1):
            chosen = jnp.where(shift_of == shift, pieces[shift], chosen)
        blocks.append(chosen)
    return jnp.concatenate(blocks, axis=0)


def solution(mesh):
    placed = (P("freq", "dish", None, None), P("freq", "dish", None, None), P(), P())
    return jax.shard_map(
        body, mesh=mesh, in_specs=placed, out_specs=P("freq", "dish"), check_vma=False
    )
```

```python
import functools
import math

import jax
import jax.numpy as jnp
import ml_dtypes
import numpy as np
from jax import lax
from jax.experimental import pallas as pl
from jax.experimental.pallas import tpu as pltpu
from jax.sharding import PartitionSpec as P

NCHAN = 8192
CHA = 64
CHB = 128
TAPS = 4
FRAMES = 16
FEEDS_PER_STEP = 4


full_turn = 2.0 * math.pi


def table_constant(row_count, col_count, modulus, scaling):
    rows = np.arange(row_count, dtype=np.int64)[:, None]
    cols = np.arange(col_count, dtype=np.int64)[None, :]
    angles = np.float32(full_turn / modulus) * (rows * cols % modulus).astype(np.float32)
    cosine = (np.cos(angles.astype(np.float64)) * scaling).astype(ml_dtypes.bfloat16)
    sine = (np.sin(angles.astype(np.float64)) * scaling).astype(ml_dtypes.bfloat16)
    return cosine, sine


def window_constant():
    sample_index = np.arange(TAPS * NCHAN, dtype=np.float64)
    centred = (sample_index - TAPS * NCHAN / 2 + 0.5) / NCHAN
    taper_curve = 0.5 - 0.5 * np.cos(full_turn * (sample_index + 0.5) / (TAPS * NCHAN))
    shaped_window = (np.sinc(centred) * taper_curve).reshape(TAPS, NCHAN)
    energy = np.mean(np.sum(shaped_window * shaped_window, axis=0))
    return (shaped_window / np.sqrt(energy)).astype(np.float32)


def rotation_constant(row_count, col_count, modulus):
    rows = np.arange(row_count, dtype=np.int64)[:, None]
    cols = np.arange(col_count, dtype=np.int64)[None, :]
    angles = np.float32(-(full_turn / modulus)) * (rows * cols % modulus).astype(np.float32)
    angles = angles.astype(np.float64)
    return np.cos(angles).astype(np.float32), np.sin(angles).astype(np.float32)


def fourier_table(row_index, col_index, modulus, scaling):
    phases = row_index[:, None] * col_index[None, :] % modulus
    angles = full_turn / modulus * phases.astype(jnp.float32)
    cosine_table = (jnp.cos(angles) * scaling).astype(jnp.bfloat16)
    sine_table = (jnp.sin(angles) * scaling).astype(jnp.bfloat16)
    upper_rows = jnp.stack([cosine_table, -sine_table], axis=1)
    lower_rows = jnp.stack([sine_table, cosine_table], axis=1)
    return jnp.stack([upper_rows, lower_rows], axis=0)


def filter_window():
    sample_index = jnp.arange(TAPS * NCHAN, dtype=jnp.float32)
    centred = (sample_index - TAPS * NCHAN / 2 + 0.5) / NCHAN
    taper_curve = 0.5 - 0.5 * jnp.cos(full_turn * (sample_index + 0.5) / (TAPS * NCHAN))
    shaped_window = (jnp.sinc(centred) * taper_curve).reshape(TAPS, NCHAN)
    energy = jnp.mean(jnp.sum(shaped_window * shaped_window, axis=0))
    return shaped_window / jnp.sqrt(energy)


def beam_tables(grid_rows, grid_len, rows_per_device):
    positions = jnp.arange(grid_len, dtype=jnp.int32)
    cosine_base, sine_base = table_constant(grid_len, grid_len, grid_len, 1.0 / math.sqrt(grid_len))
    cosine_base = jnp.asarray(cosine_base)
    sine_base = jnp.asarray(sine_base)
    devices = grid_len // rows_per_device
    picks = (positions[None, :, None] == grid_rows[:, None, :]).astype(jnp.bfloat16)
    cosine_table = jnp.einsum(
        "jg,dgm->djm", cosine_base, picks, preferred_element_type=jnp.float32
    ).astype(jnp.bfloat16)
    sine_table = jnp.einsum(
        "jg,dgm->djm", sine_base, picks, preferred_element_type=jnp.float32
    ).astype(jnp.bfloat16)
    shape = (grid_rows.shape[0], grid_len, devices, 1, rows_per_device)
    cosine_table = cosine_table.reshape(shape)
    sine_table = sine_table.reshape(shape)
    real_rows = jnp.concatenate([cosine_table, sine_table], axis=3)
    imag_rows = jnp.concatenate([-sine_table, cosine_table], axis=3)
    rows = jnp.concatenate([real_rows, imag_rows], axis=1)
    return rows.reshape(grid_rows.shape[0], 2 * grid_len, 2 * grid_len)


def channelize_kernel(first_pair, pairs, v_ref, w_ref, t1_ref, tw_ref, t2_ref, g_ref, o_ref):
    cos_tw = tw_ref[0]
    sin_tw = tw_ref[1]
    t1 = t1_ref[...]
    t2_real = t2_ref[0]
    t2_imag = t2_ref[1]
    half = t2_real.shape[0] // 2
    feeds = v_ref.shape[0]

    def one_frame(pieces):
        acc = None
        for tap in range(TAPS):
            term = w_ref[tap][None] * pieces[tap]
            acc = term if acc is None else acc + term
        block = acc.astype(jnp.bfloat16).reshape(2 * CHA, CHB)
        section = jnp.dot(t1, block, preferred_element_type=jnp.float32)
        sec_real = section[:CHA]
        sec_imag = section[CHA:]
        turned_real = sec_real * cos_tw - sec_imag * sin_tw
        turned_imag = sec_real * sin_tw + sec_imag * cos_tw
        return turned_real.astype(jnp.bfloat16), turned_imag.astype(jnp.bfloat16)

    def pair(feed, step, g_real, g_imag):
        pieces = []
        for offset in range(TAPS + 1):
            start = pl.multiple_of((2 * (step - first_pair) + offset) * CHA, CHA)
            pieces.append(v_ref[feed, :, pl.ds(start, CHA), :].astype(jnp.float32))
        first_real, first_imag = one_frame(pieces[:TAPS])
        second_real, second_imag = one_frame(pieces[1:])
        both_real = jnp.concatenate([first_real, second_real], axis=0)
        both_imag = jnp.concatenate([first_imag, second_imag], axis=0)
        dims = (((1,), (1,)), ((), ()))
        spectrum = lax.dot_general(
            t2_real, both_real, dims, preferred_element_type=jnp.float32
        ) + lax.dot_general(t2_imag, both_imag, dims, preferred_element_type=jnp.float32)
        spec_real = spectrum[:half]
        spec_imag = spectrum[half:]
        out_real = spec_real * g_real - spec_imag * g_imag
        out_imag = spec_real * g_imag + spec_imag * g_real
        lanes = pl.ds(pl.multiple_of((step - first_pair) * 2 * CHA, 2 * CHA), 2 * CHA)
        o_ref[0, feed, :, lanes] = out_real.astype(o_ref.dtype)
        o_ref[1, feed, :, lanes] = out_imag.astype(o_ref.dtype)

    for feed in range(feeds):
        g_half_real = g_ref[feed, 0].astype(jnp.float32)
        g_half_imag = g_ref[feed, 1].astype(jnp.float32)
        g_real = jnp.concatenate([g_half_real, g_half_real], axis=1)
        g_imag = jnp.concatenate([g_half_imag, g_half_imag], axis=1)
        for step in range(first_pair, first_pair + pairs):
            pair(feed, step, g_real, g_imag)


def beam_kernel(dish_count, carry_in, finish, lanes, *refs):
    x_ref, t_ref, c_ref, s_ref = refs[:4]
    init_ref = refs[4] if carry_in else None
    out_refs = refs[4 + carry_in : -1]
    acc_ref = refs[-1]
    step = pl.program_id(0)
    devices = x_ref.shape[0] // dish_count
    rows = x_ref.shape[2]
    grid_len = t_ref.shape[1] // 2
    lane_window = slice(None)

    @pl.when(step == 0)
    def _():
        if carry_in:
            acc_ref[...] = init_ref[...]
        else:
            acc_ref[...] = jnp.zeros_like(acc_ref)

    parts = []
    for d in range(dish_count):
        block = x_ref[pl.ds(d * devices, devices), :, :, lane_window].reshape(
            2 * rows * devices, lanes
        )
        sums = jnp.dot(t_ref[d], block, preferred_element_type=jnp.float32)
        sum_real = sums[:grid_len]
        sum_imag = sums[grid_len:]
        cos_d = c_ref[d]
        sin_d = s_ref[d]
        part_real = sum_real * cos_d - sum_imag * sin_d
        part_imag = sum_real * sin_d + sum_imag * cos_d
        parts.append(
            (
                part_real.astype(jnp.bfloat16).astype(jnp.float32),
                part_imag.astype(jnp.bfloat16).astype(jnp.float32),
            )
        )
    (a_re, a_im), (b_re, b_im), (c_re, c_im), (d_re, d_im) = parts
    even_re, even_im = a_re + c_re, a_im + c_im
    odd_re, odd_im = a_re - c_re, a_im - c_im
    pair_re, pair_im = b_re + d_re, b_im + d_im
    cross_re, cross_im = b_re - d_re, b_im - d_im
    beams = [
        (even_re + pair_re, even_im + pair_im),
        (odd_re + cross_im, odd_im - cross_re),
        (even_re - pair_re, even_im - pair_im),
        (odd_re - cross_im, odd_im + cross_re),
    ]
    for q in range(dish_count):
        beam_real, beam_imag = beams[q]
        acc_ref[q] += beam_real * beam_real + beam_imag * beam_imag

    @pl.when(step == pl.num_programs(0) - 1)
    def _():
        if not finish:
            out_refs[0][...] = acc_ref[...]
            return
        me = lax.axis_index("dish")
        width = out_refs[0].shape[0]
        for shift in range(dish_count):
            target = jnp.bitwise_xor(me, shift)
            beam_index = jnp.bitwise_or(
                jnp.left_shift(jnp.bitwise_and(target, 1), 1), jnp.right_shift(target, 1)
            )
            total = acc_ref[beam_index]
            folded = total[:, :CHB]
            for k in range(1, lanes // CHB):
                folded = folded + total[:, k * CHB : (k + 1) * CHB]
            folded = folded + pltpu.roll(folded, width, 1)
            flipped = jnp.transpose(folded, (1, 0))
            out_refs[shift][...] = flipped[:width] * (0.25 / FRAMES)


def body(voltages, feed_gains, block_assign, grid_rows):
    dish_rows = voltages.shape[0]
    block_count = lax.axis_size("freq")
    dish_count = lax.axis_size("dish")
    block_width = NCHAN // block_count
    quarter = block_width // dish_count
    dests = block_count * dish_count
    grid_len = dish_rows * block_count
    total_dishes = grid_len * dish_count
    samples = voltages.shape[-1]

    dest = jnp.arange(dests, dtype=jnp.int32)
    dest_quarter = dest // block_count
    dest_block = jnp.tile(block_assign, dish_count)
    dest_e = dest_block * dish_count + dest_quarter
    picks_e = (dest_e[:, None] == jnp.arange(dests, dtype=jnp.int32)[None, :]).astype(jnp.bfloat16)

    window = jnp.asarray(window_constant().reshape(TAPS, CHA, CHB))
    first_cos, first_sin = table_constant(CHA, CHA, CHA, 1.0 / math.sqrt(CHA))
    first_table = np.block([[first_cos, first_sin], [-first_sin, first_cos]])
    first_table = jnp.asarray(first_table)
    twiddle = jnp.asarray(np.stack(rotation_constant(CHA, CHB, NCHAN), axis=0))
    second_cos, second_sin = table_constant(CHB, CHB, CHB, 1.0 / math.sqrt(CHB))
    second_table = np.stack(
        [np.stack([second_cos, -second_sin], axis=0), np.stack([second_sin, second_cos], axis=0)],
        axis=0,
    )
    second_table = jnp.einsum(
        "je,qseb->qsjb", picks_e, jnp.asarray(second_table), preferred_element_type=jnp.float32
    ).astype(jnp.bfloat16).reshape(2, 2 * dests, CHB)
    gains = feed_gains[:, 0].reshape(dish_rows, 2, CHB, CHA)
    gains = jnp.einsum("je,rpec->rpjc", picks_e, gains, preferred_element_type=jnp.float32)
    gains = gains.astype(jnp.bfloat16)

    chunk_pairs = [8]
    chunks = len(chunk_pairs)
    tables = beam_tables(grid_rows, grid_len, dish_rows)
    feed_index = jnp.arange(dish_count, dtype=jnp.int32)
    positions = jnp.arange(grid_len, dtype=jnp.int32)
    twist_cos, twist_sin = rotation_constant(dish_count, grid_len, total_dishes)
    twist_lanes = 4 * quarter
    lane_shape = (dish_count, grid_len, twist_lanes)
    twist_cos = jnp.broadcast_to(jnp.asarray(twist_cos[:, :, None]), lane_shape)
    twist_sin = jnp.broadcast_to(jnp.asarray(twist_sin[:, :, None]), lane_shape)
    lane_block = 4 * quarter

    volts = voltages[:, 0].reshape(dish_rows, 2, samples // CHB, CHB)

    def channelize_chunk(chunk):
        pairs = chunk_pairs[chunk]
        first_pair = sum(chunk_pairs[:chunk])
        chunk_lanes = pairs * 2 * quarter
        span = (2 * pairs + TAPS - 1) * CHA
        first_row = 2 * first_pair * CHA
        return pl.pallas_call(
            functools.partial(channelize_kernel, first_pair, pairs),
            grid=(dish_rows // FEEDS_PER_STEP,),
            in_specs=[
                pl.BlockSpec(
                    (pl.Element(FEEDS_PER_STEP), pl.Element(2), pl.Element(span), pl.Element(CHB)),
                    lambda r: (r * FEEDS_PER_STEP, 0, first_row, 0),
                ),
                pl.BlockSpec((TAPS, CHA, CHB), lambda r: (0, 0, 0)),
                pl.BlockSpec((2 * CHA, 2 * CHA), lambda r: (0, 0)),
                pl.BlockSpec((2, CHA, CHB), lambda r: (0, 0, 0)),
                pl.BlockSpec((2, 2 * dests, CHB), lambda r: (0, 0, 0)),
                pl.BlockSpec((FEEDS_PER_STEP, 2, dests, CHA), lambda r: (r, 0, 0, 0)),
            ],
            out_specs=pl.BlockSpec((2, FEEDS_PER_STEP, dests, chunk_lanes), lambda r: (0, r, 0, 0)),
            out_shape=jax.ShapeDtypeStruct((2, dish_rows, dests, chunk_lanes), jnp.bfloat16),
            cost_estimate=pl.CostEstimate(
                flops=int(dish_rows * pairs * 2 * 2 * 128 * 128 * 128 * 3),
                bytes_accessed=int(voltages.size * 2 + 2 * dish_rows * dests * chunk_lanes * 2),
                transcendentals=0,
            ),
        )(volts, window, first_table, twiddle, second_table, gains)

    def beamform_chunk(received, carried, finish):
        carry_in = carried is not None
        chunk_lanes = received.shape[3]
        in_specs = [
            pl.BlockSpec((dests, 2, dish_rows, lane_block), lambda f: (0, 0, 0, f)),
            pl.BlockSpec((dish_count, 2 * grid_len, 2 * grid_len), lambda f: (0, 0, 0)),
        ]
        in_specs += [pl.BlockSpec((dish_count, grid_len, twist_lanes), lambda f: (0, 0, 0))] * 2
        operands = [received, tables, twist_cos, twist_sin]
        if carry_in:
            in_specs.append(pl.BlockSpec((dish_count, grid_len, lane_block), lambda f: (0, 0, 0)))
            operands.append(carried)
        if finish:
            out_specs = [pl.BlockSpec((quarter, grid_len), lambda f: (0, 0))] * dish_count
            out_shape = [jax.ShapeDtypeStruct((quarter, grid_len), jnp.float32)] * dish_count
        else:
            out_specs = pl.BlockSpec((dish_count, grid_len, lane_block), lambda f: (0, 0, 0))
            out_shape = jax.ShapeDtypeStruct((dish_count, grid_len, lane_block), jnp.float32)
        return pl.pallas_call(
            functools.partial(beam_kernel, dish_count, carry_in, finish, lane_block),
            grid=(chunk_lanes // lane_block,),
            in_specs=in_specs,
            out_specs=out_specs,
            out_shape=out_shape,
            scratch_shapes=[pltpu.VMEM((dish_count, grid_len, lane_block), jnp.float32)],
            cost_estimate=pl.CostEstimate(
                flops=int(dish_count * 2 * 512 * 512 * chunk_lanes),
                bytes_accessed=int(received.size * 2 + tables.size * 2),
                transcendentals=0,
            ),
        )(*operands)

    sent = [channelize_chunk(c) for c in range(chunks)]
    arrived = [
        jnp.transpose(lax.all_to_all(s, ("dish", "freq"), 2, 2, tiled=True), (2, 0, 1, 3))
        for s in sent
    ]
    carried = None
    for c in range(chunks):
        carried = beamform_chunk(arrived[c], carried, c == chunks - 1)
    powers = carried

    me = lax.axis_index("dish")
    pieces = [powers[0]]
    for shift in range(1, dish_count):
        outgoing = powers[shift]
        pairs_list = [(i, i ^ shift) for i in range(dish_count)]
        pieces.append(lax.ppermute(outgoing, "dish", pairs_list))
    blocks = []
    for source in range(dish_count):
        shift_of = jnp.bitwise_xor(me, source)
        chosen = pieces[dish_count - 1]
        for shift in range(dish_count - 2, -1, -1):
            chosen = jnp.where(shift_of == shift, pieces[shift], chosen)
        blocks.append(chosen)
    return jnp.concatenate(blocks, axis=0)


def solution(mesh):
    placed = (P("freq", "dish", None, None), P("freq", "dish", None, None), P(), P())
    return jax.shard_map(
        body, mesh=mesh, in_specs=placed, out_specs=P("freq", "dish"), check_vma=False
    )
```

```python
import functools
import math

import jax
import jax.numpy as jnp
import ml_dtypes
import numpy as np
from jax import lax
from jax.experimental import pallas as pl
from jax.experimental.pallas import tpu as pltpu
from jax.sharding import PartitionSpec as P

NCHAN = 8192
CHA = 64
CHB = 128
TAPS = 4
FRAMES = 16
FEEDS_PER_STEP = 4


full_turn = 2.0 * math.pi


def table_constant(row_count, col_count, modulus, scaling):
    rows = np.arange(row_count, dtype=np.int64)[:, None]
    cols = np.arange(col_count, dtype=np.int64)[None, :]
    angles = np.float32(full_turn / modulus) * (rows * cols % modulus).astype(np.float32)
    cosine = (np.cos(angles.astype(np.float64)) * scaling).astype(ml_dtypes.bfloat16)
    sine = (np.sin(angles.astype(np.float64)) * scaling).astype(ml_dtypes.bfloat16)
    return cosine, sine


def window_constant():
    sample_index = np.arange(TAPS * NCHAN, dtype=np.float64)
    centred = (sample_index - TAPS * NCHAN / 2 + 0.5) / NCHAN
    taper_curve = 0.5 - 0.5 * np.cos(full_turn * (sample_index + 0.5) / (TAPS * NCHAN))
    shaped_window = (np.sinc(centred) * taper_curve).reshape(TAPS, NCHAN)
    energy = np.mean(np.sum(shaped_window * shaped_window, axis=0))
    return (shaped_window / np.sqrt(energy)).astype(np.float32)


def rotation_constant(row_count, col_count, modulus):
    rows = np.arange(row_count, dtype=np.int64)[:, None]
    cols = np.arange(col_count, dtype=np.int64)[None, :]
    angles = np.float32(-(full_turn / modulus)) * (rows * cols % modulus).astype(np.float32)
    angles = angles.astype(np.float64)
    return np.cos(angles).astype(np.float32), np.sin(angles).astype(np.float32)


def fourier_table(row_index, col_index, modulus, scaling):
    phases = row_index[:, None] * col_index[None, :] % modulus
    angles = full_turn / modulus * phases.astype(jnp.float32)
    cosine_table = (jnp.cos(angles) * scaling).astype(jnp.bfloat16)
    sine_table = (jnp.sin(angles) * scaling).astype(jnp.bfloat16)
    upper_rows = jnp.stack([cosine_table, -sine_table], axis=1)
    lower_rows = jnp.stack([sine_table, cosine_table], axis=1)
    return jnp.stack([upper_rows, lower_rows], axis=0)


def filter_window():
    sample_index = jnp.arange(TAPS * NCHAN, dtype=jnp.float32)
    centred = (sample_index - TAPS * NCHAN / 2 + 0.5) / NCHAN
    taper_curve = 0.5 - 0.5 * jnp.cos(full_turn * (sample_index + 0.5) / (TAPS * NCHAN))
    shaped_window = (jnp.sinc(centred) * taper_curve).reshape(TAPS, NCHAN)
    energy = jnp.mean(jnp.sum(shaped_window * shaped_window, axis=0))
    return shaped_window / jnp.sqrt(energy)


def beam_tables(grid_rows, grid_len, rows_per_device):
    positions = jnp.arange(grid_len, dtype=jnp.int32)
    cosine_base, sine_base = table_constant(grid_len, grid_len, grid_len, 1.0 / math.sqrt(grid_len))
    cosine_base = jnp.asarray(cosine_base)
    sine_base = jnp.asarray(sine_base)
    devices = grid_len // rows_per_device
    picks = (positions[None, :, None] == grid_rows[:, None, :]).astype(jnp.bfloat16)
    cosine_table = jnp.einsum(
        "jg,dgm->djm", cosine_base, picks, preferred_element_type=jnp.float32
    ).astype(jnp.bfloat16)
    sine_table = jnp.einsum(
        "jg,dgm->djm", sine_base, picks, preferred_element_type=jnp.float32
    ).astype(jnp.bfloat16)
    return jnp.stack([cosine_table, sine_table], axis=1)


def channelize_kernel(first_pair, pairs, v_ref, w_ref, t1_ref, tw_ref, t2_ref, g_ref, o_ref):
    cos_tw = tw_ref[0]
    sin_tw = tw_ref[1]
    t1 = t1_ref[...]
    t2_real = t2_ref[0]
    t2_imag = t2_ref[1]
    half = t2_real.shape[0] // 2
    feeds = v_ref.shape[0]

    def one_frame(pieces):
        acc = None
        for tap in range(TAPS):
            term = w_ref[tap][None] * pieces[tap]
            acc = term if acc is None else acc + term
        block = acc.astype(jnp.bfloat16).reshape(2 * CHA, CHB)
        section = jnp.dot(t1, block, preferred_element_type=jnp.float32)
        sec_real = section[:CHA]
        sec_imag = section[CHA:]
        turned_real = sec_real * cos_tw - sec_imag * sin_tw
        turned_imag = sec_real * sin_tw + sec_imag * cos_tw
        return turned_real.astype(jnp.bfloat16), turned_imag.astype(jnp.bfloat16)

    def pair(feed, step, g_real, g_imag):
        pieces = []
        for offset in range(TAPS + 1):
            start = pl.multiple_of((2 * (step - first_pair) + offset) * CHA, CHA)
            pieces.append(v_ref[feed, :, pl.ds(start, CHA), :].astype(jnp.float32))
        first_real, first_imag = one_frame(pieces[:TAPS])
        second_real, second_imag = one_frame(pieces[1:])
        both_real = jnp.concatenate([first_real, second_real], axis=0)
        both_imag = jnp.concatenate([first_imag, second_imag], axis=0)
        dims = (((1,), (1,)), ((), ()))
        spectrum = lax.dot_general(
            t2_real, both_real, dims, preferred_element_type=jnp.float32
        ) + lax.dot_general(t2_imag, both_imag, dims, preferred_element_type=jnp.float32)
        spec_real = spectrum[:half]
        spec_imag = spectrum[half:]
        out_real = spec_real * g_real - spec_imag * g_imag
        out_imag = spec_real * g_imag + spec_imag * g_real
        lanes = pl.ds(pl.multiple_of((step - first_pair) * 2 * CHA, 2 * CHA), 2 * CHA)
        o_ref[0, feed, :, lanes] = out_real.astype(o_ref.dtype)
        o_ref[1, feed, :, lanes] = out_imag.astype(o_ref.dtype)

    for feed in range(feeds):
        g_half_real = g_ref[feed, 0].astype(jnp.float32)
        g_half_imag = g_ref[feed, 1].astype(jnp.float32)
        g_real = jnp.concatenate([g_half_real, g_half_real], axis=1)
        g_imag = jnp.concatenate([g_half_imag, g_half_imag], axis=1)
        for step in range(first_pair, first_pair + pairs):
            pair(feed, step, g_real, g_imag)


def beam_kernel(dish_count, carry_in, finish, lanes, *refs):
    x_ref, t_ref, c_ref, s_ref = refs[:4]
    init_ref = refs[4] if carry_in else None
    out_refs = refs[4 + carry_in : -1]
    acc_ref = refs[-1]
    step = pl.program_id(0)
    devices = x_ref.shape[0] // dish_count
    rows = x_ref.shape[2]
    grid_len = t_ref.shape[2]
    lane_window = slice(None)

    @pl.when(step == 0)
    def _():
        if carry_in:
            acc_ref[...] = init_ref[...]
        else:
            acc_ref[...] = jnp.zeros_like(acc_ref)

    parts = []
    for d in range(dish_count):
        x_real = x_ref[pl.ds(d * devices, devices), 0, :, lane_window].reshape(rows * devices, lanes)
        x_imag = x_ref[pl.ds(d * devices, devices), 1, :, lane_window].reshape(rows * devices, lanes)
        cosine = t_ref[d, 0]
        sine = t_ref[d, 1]
        sum_real = jnp.dot(cosine, x_real, preferred_element_type=jnp.float32) + jnp.dot(
            sine, x_imag, preferred_element_type=jnp.float32
        )
        sum_imag = jnp.dot(cosine, x_imag, preferred_element_type=jnp.float32) - jnp.dot(
            sine, x_real, preferred_element_type=jnp.float32
        )
        cos_d = c_ref[d]
        sin_d = s_ref[d]
        part_real = sum_real * cos_d - sum_imag * sin_d
        part_imag = sum_real * sin_d + sum_imag * cos_d
        parts.append(
            (
                part_real.astype(jnp.bfloat16).astype(jnp.float32),
                part_imag.astype(jnp.bfloat16).astype(jnp.float32),
            )
        )
    (a_re, a_im), (b_re, b_im), (c_re, c_im), (d_re, d_im) = parts
    beams = [
        (a_re + b_re + c_re + d_re, a_im + b_im + c_im + d_im),
        (a_re + b_im - c_re - d_im, a_im - b_re - c_im + d_re),
        (a_re - b_re + c_re - d_re, a_im - b_im + c_im - d_im),
        (a_re - b_im - c_re + d_im, a_im + b_re - c_im - d_re),
    ]
    for q in range(dish_count):
        beam_real, beam_imag = beams[q]
        acc_ref[q] += beam_real * beam_real + beam_imag * beam_imag

    @pl.when(step == pl.num_programs(0) - 1)
    def _():
        if not finish:
            out_refs[0][...] = acc_ref[...]
            return
        me = lax.axis_index("dish")
        width = out_refs[0].shape[0]
        for shift in range(dish_count):
            target = jnp.bitwise_xor(me, shift)
            beam_index = jnp.bitwise_or(
                jnp.left_shift(jnp.bitwise_and(target, 1), 1), jnp.right_shift(target, 1)
            )
            total = acc_ref[beam_index]
            folded = total[:, :CHB]
            for k in range(1, lanes // CHB):
                folded = folded + total[:, k * CHB : (k + 1) * CHB]
            folded = folded + pltpu.roll(folded, width, 1)
            flipped = jnp.transpose(folded, (1, 0))
            out_refs[shift][...] = flipped[:width] * (0.25 / FRAMES)


def body(voltages, feed_gains, block_assign, grid_rows):
    dish_rows = voltages.shape[0]
    block_count = lax.axis_size("freq")
    dish_count = lax.axis_size("dish")
    block_width = NCHAN // block_count
    quarter = block_width // dish_count
    dests = block_count * dish_count
    grid_len = dish_rows * block_count
    total_dishes = grid_len * dish_count
    samples = voltages.shape[-1]

    dest = jnp.arange(dests, dtype=jnp.int32)
    dest_quarter = dest // block_count
    dest_block = jnp.tile(block_assign, dish_count)
    dest_e = dest_block * dish_count + dest_quarter
    picks_e = (dest_e[:, None] == jnp.arange(dests, dtype=jnp.int32)[None, :]).astype(jnp.bfloat16)

    window = jnp.asarray(window_constant().reshape(TAPS, CHA, CHB))
    first_cos, first_sin = table_constant(CHA, CHA, CHA, 1.0 / math.sqrt(CHA))
    first_table = np.block([[first_cos, first_sin], [-first_sin, first_cos]])
    first_table = jnp.asarray(first_table)
    twiddle = jnp.asarray(np.stack(rotation_constant(CHA, CHB, NCHAN), axis=0))
    second_cos, second_sin = table_constant(CHB, CHB, CHB, 1.0 / math.sqrt(CHB))
    second_table = np.stack(
        [np.stack([second_cos, -second_sin], axis=0), np.stack([second_sin, second_cos], axis=0)],
        axis=0,
    )
    second_table = jnp.einsum(
        "je,qseb->qsjb", picks_e, jnp.asarray(second_table), preferred_element_type=jnp.float32
    ).astype(jnp.bfloat16).reshape(2, 2 * dests, CHB)
    gains = feed_gains[:, 0].reshape(dish_rows, 2, CHB, CHA)
    gains = jnp.einsum("je,rpec->rpjc", picks_e, gains, preferred_element_type=jnp.float32)
    gains = gains.astype(jnp.bfloat16)

    chunk_pairs = [8]
    chunks = len(chunk_pairs)
    tables = beam_tables(grid_rows, grid_len, dish_rows)
    feed_index = jnp.arange(dish_count, dtype=jnp.int32)
    positions = jnp.arange(grid_len, dtype=jnp.int32)
    twist_cos, twist_sin = rotation_constant(dish_count, grid_len, total_dishes)
    twist_cos = jnp.asarray(twist_cos[:, :, None])
    twist_sin = jnp.asarray(twist_sin[:, :, None])
    lane_block = 4 * quarter

    volts = voltages[:, 0].reshape(dish_rows, 2, samples // CHB, CHB)

    def channelize_chunk(chunk):
        pairs = chunk_pairs[chunk]
        first_pair = sum(chunk_pairs[:chunk])
        chunk_lanes = pairs * 2 * quarter
        span = (2 * pairs + TAPS - 1) * CHA
        first_row = 2 * first_pair * CHA
        return pl.pallas_call(
            functools.partial(channelize_kernel, first_pair, pairs),
            grid=(dish_rows // FEEDS_PER_STEP,),
            in_specs=[
                pl.BlockSpec(
                    (pl.Element(FEEDS_PER_STEP), pl.Element(2), pl.Element(span), pl.Element(CHB)),
                    lambda r: (r * FEEDS_PER_STEP, 0, first_row, 0),
                ),
                pl.BlockSpec((TAPS, CHA, CHB), lambda r: (0, 0, 0)),
                pl.BlockSpec((2 * CHA, 2 * CHA), lambda r: (0, 0)),
                pl.BlockSpec((2, CHA, CHB), lambda r: (0, 0, 0)),
                pl.BlockSpec((2, 2 * dests, CHB), lambda r: (0, 0, 0)),
                pl.BlockSpec((FEEDS_PER_STEP, 2, dests, CHA), lambda r: (r, 0, 0, 0)),
            ],
            out_specs=pl.BlockSpec((2, FEEDS_PER_STEP, dests, chunk_lanes), lambda r: (0, r, 0, 0)),
            out_shape=jax.ShapeDtypeStruct((2, dish_rows, dests, chunk_lanes), jnp.bfloat16),
            cost_estimate=pl.CostEstimate(
                flops=int(dish_rows * pairs * 2 * 2 * 128 * 128 * 128 * 3),
                bytes_accessed=int(voltages.size * 2 + 2 * dish_rows * dests * chunk_lanes * 2),
                transcendentals=0,
            ),
        )(volts, window, first_table, twiddle, second_table, gains)

    def beamform_chunk(received, carried, finish):
        carry_in = carried is not None
        chunk_lanes = received.shape[3]
        in_specs = [
            pl.BlockSpec((dests, 2, dish_rows, lane_block), lambda f: (0, 0, 0, f)),
            pl.BlockSpec((dish_count, 2, grid_len, grid_len), lambda f: (0, 0, 0, 0)),
        ]
        in_specs += [pl.BlockSpec((dish_count, grid_len, 1), lambda f: (0, 0, 0))] * 2
        operands = [received, tables, twist_cos, twist_sin]
        if carry_in:
            in_specs.append(pl.BlockSpec((dish_count, grid_len, lane_block), lambda f: (0, 0, 0)))
            operands.append(carried)
        if finish:
            out_specs = [pl.BlockSpec((quarter, grid_len), lambda f: (0, 0))] * dish_count
            out_shape = [jax.ShapeDtypeStruct((quarter, grid_len), jnp.float32)] * dish_count
        else:
            out_specs = pl.BlockSpec((dish_count, grid_len, lane_block), lambda f: (0, 0, 0))
            out_shape = jax.ShapeDtypeStruct((dish_count, grid_len, lane_block), jnp.float32)
        return pl.pallas_call(
            functools.partial(beam_kernel, dish_count, carry_in, finish, lane_block),
            grid=(chunk_lanes // lane_block,),
            in_specs=in_specs,
            out_specs=out_specs,
            out_shape=out_shape,
            scratch_shapes=[pltpu.VMEM((dish_count, grid_len, lane_block), jnp.float32)],
            cost_estimate=pl.CostEstimate(
                flops=int(dish_count * 2 * 512 * 512 * chunk_lanes),
                bytes_accessed=int(received.size * 2 + tables.size * 2),
                transcendentals=0,
            ),
        )(*operands)

    sent = [channelize_chunk(c) for c in range(chunks)]
    arrived = [
        jnp.transpose(lax.all_to_all(s, ("dish", "freq"), 2, 2, tiled=True), (2, 0, 1, 3))
        for s in sent
    ]
    carried = None
    for c in range(chunks):
        carried = beamform_chunk(arrived[c], carried, c == chunks - 1)
    powers = carried

    me = lax.axis_index("dish")
    pieces = [powers[0]]
    for shift in range(1, dish_count):
        outgoing = powers[shift]
        pairs_list = [(i, i ^ shift) for i in range(dish_count)]
        pieces.append(lax.ppermute(outgoing, "dish", pairs_list))
    blocks = []
    for source in range(dish_count):
        shift_of = jnp.bitwise_xor(me, source)
        chosen = pieces[dish_count - 1]
        for shift in range(dish_count - 2, -1, -1):
            chosen = jnp.where(shift_of == shift, pieces[shift], chosen)
        blocks.append(chosen)
    return jnp.concatenate(blocks, axis=0)


def solution(mesh):
    placed = (P("freq", "dish", None, None), P("freq", "dish", None, None), P(), P())
    return jax.shard_map(
        body, mesh=mesh, in_specs=placed, out_specs=P("freq", "dish"), check_vma=False
    )
```

```python
import functools
import math

import jax
import jax.numpy as jnp
import ml_dtypes
import numpy as np
from jax import lax
from jax.experimental import pallas as pl
from jax.experimental.pallas import tpu as pltpu
from jax.sharding import PartitionSpec as P

NCHAN = 8192
CHA = 64
CHB = 128
TAPS = 4
FRAMES = 16
FEEDS_PER_STEP = 4


full_turn = 2.0 * math.pi


def table_constant(row_count, col_count, modulus, scaling):
    rows = np.arange(row_count, dtype=np.int64)[:, None]
    cols = np.arange(col_count, dtype=np.int64)[None, :]
    angles = np.float32(full_turn / modulus) * (rows * cols % modulus).astype(np.float32)
    cosine = (np.cos(angles.astype(np.float64)) * scaling).astype(ml_dtypes.bfloat16)
    sine = (np.sin(angles.astype(np.float64)) * scaling).astype(ml_dtypes.bfloat16)
    return cosine, sine


def window_constant():
    sample_index = np.arange(TAPS * NCHAN, dtype=np.float64)
    centred = (sample_index - TAPS * NCHAN / 2 + 0.5) / NCHAN
    taper_curve = 0.5 - 0.5 * np.cos(full_turn * (sample_index + 0.5) / (TAPS * NCHAN))
    shaped_window = (np.sinc(centred) * taper_curve).reshape(TAPS, NCHAN)
    energy = np.mean(np.sum(shaped_window * shaped_window, axis=0))
    return (shaped_window / np.sqrt(energy)).astype(np.float32)


def rotation_constant(row_count, col_count, modulus):
    rows = np.arange(row_count, dtype=np.int64)[:, None]
    cols = np.arange(col_count, dtype=np.int64)[None, :]
    angles = np.float32(-(full_turn / modulus)) * (rows * cols % modulus).astype(np.float32)
    angles = angles.astype(np.float64)
    return np.cos(angles).astype(np.float32), np.sin(angles).astype(np.float32)


def fourier_table(row_index, col_index, modulus, scaling):
    phases = row_index[:, None] * col_index[None, :] % modulus
    angles = full_turn / modulus * phases.astype(jnp.float32)
    cosine_table = (jnp.cos(angles) * scaling).astype(jnp.bfloat16)
    sine_table = (jnp.sin(angles) * scaling).astype(jnp.bfloat16)
    upper_rows = jnp.stack([cosine_table, -sine_table], axis=1)
    lower_rows = jnp.stack([sine_table, cosine_table], axis=1)
    return jnp.stack([upper_rows, lower_rows], axis=0)


def filter_window():
    sample_index = jnp.arange(TAPS * NCHAN, dtype=jnp.float32)
    centred = (sample_index - TAPS * NCHAN / 2 + 0.5) / NCHAN
    taper_curve = 0.5 - 0.5 * jnp.cos(full_turn * (sample_index + 0.5) / (TAPS * NCHAN))
    shaped_window = (jnp.sinc(centred) * taper_curve).reshape(TAPS, NCHAN)
    energy = jnp.mean(jnp.sum(shaped_window * shaped_window, axis=0))
    return shaped_window / jnp.sqrt(energy)


def beam_tables(grid_rows, grid_len, rows_per_device):
    positions = jnp.arange(grid_len, dtype=jnp.int32)
    cosine_base, sine_base = table_constant(grid_len, grid_len, grid_len, 1.0 / math.sqrt(grid_len))
    cosine_base = jnp.asarray(cosine_base)
    sine_base = jnp.asarray(sine_base)
    devices = grid_len // rows_per_device
    picks = (positions[None, :, None] == grid_rows[:, None, :]).astype(jnp.bfloat16)
    cosine_table = jnp.einsum(
        "jg,dgm->djm", cosine_base, picks, preferred_element_type=jnp.float32
    ).astype(jnp.bfloat16)
    sine_table = jnp.einsum(
        "jg,dgm->djm", sine_base, picks, preferred_element_type=jnp.float32
    ).astype(jnp.bfloat16)
    return jnp.stack([cosine_table, sine_table], axis=1)


def channelize_kernel(first_pair, pairs, v_ref, w_ref, t1_ref, tw_ref, t2_ref, g_ref, o_ref):
    cos_tw = tw_ref[0]
    sin_tw = tw_ref[1]
    t1 = t1_ref[...]
    t2_real = t2_ref[0]
    t2_imag = t2_ref[1]
    half = t2_real.shape[0] // 2
    feeds = v_ref.shape[0]

    def one_frame(pieces):
        acc = None
        for tap in range(TAPS):
            term = w_ref[tap][None] * pieces[tap]
            acc = term if acc is None else acc + term
        block = acc.astype(jnp.bfloat16).reshape(2 * CHA, CHB)
        section = jnp.dot(t1, block, preferred_element_type=jnp.float32)
        sec_real = section[:CHA]
        sec_imag = section[CHA:]
        turned_real = sec_real * cos_tw - sec_imag * sin_tw
        turned_imag = sec_real * sin_tw + sec_imag * cos_tw
        return turned_real.astype(jnp.bfloat16), turned_imag.astype(jnp.bfloat16)

    def pair(feed, step, g_real, g_imag):
        pieces = []
        for offset in range(TAPS + 1):
            start = pl.multiple_of((2 * (step - first_pair) + offset) * CHA, CHA)
            pieces.append(v_ref[feed, :, pl.ds(start, CHA), :].astype(jnp.float32))
        first_real, first_imag = one_frame(pieces[:TAPS])
        second_real, second_imag = one_frame(pieces[1:])
        both_real = jnp.concatenate([first_real, second_real], axis=0)
        both_imag = jnp.concatenate([first_imag, second_imag], axis=0)
        dims = (((1,), (1,)), ((), ()))
        spectrum = lax.dot_general(
            t2_real, both_real, dims, preferred_element_type=jnp.float32
        ) + lax.dot_general(t2_imag, both_imag, dims, preferred_element_type=jnp.float32)
        spec_real = spectrum[:half]
        spec_imag = spectrum[half:]
        out_real = spec_real * g_real - spec_imag * g_imag
        out_imag = spec_real * g_imag + spec_imag * g_real
        lanes = pl.ds(pl.multiple_of((step - first_pair) * 2 * CHA, 2 * CHA), 2 * CHA)
        o_ref[0, feed, :, lanes] = out_real.astype(o_ref.dtype)
        o_ref[1, feed, :, lanes] = out_imag.astype(o_ref.dtype)

    for feed in range(feeds):
        g_half_real = g_ref[feed, 0].astype(jnp.float32)
        g_half_imag = g_ref[feed, 1].astype(jnp.float32)
        g_real = jnp.concatenate([g_half_real, g_half_real], axis=1)
        g_imag = jnp.concatenate([g_half_imag, g_half_imag], axis=1)
        for step in range(first_pair, first_pair + pairs):
            pair(feed, step, g_real, g_imag)


def beam_kernel(dish_count, carry_in, finish, lanes, *refs):
    x_ref, t_ref, c_ref, s_ref = refs[:4]
    init_ref = refs[4] if carry_in else None
    out_refs = refs[4 + carry_in : -1]
    acc_ref = refs[-1]
    step = pl.program_id(0)
    devices = x_ref.shape[0] // dish_count
    rows = x_ref.shape[2]
    grid_len = t_ref.shape[2]
    lane_window = slice(None)

    @pl.when(step == 0)
    def _():
        if carry_in:
            acc_ref[...] = init_ref[...]
        else:
            acc_ref[...] = jnp.zeros_like(acc_ref)

    parts = []
    for d in range(dish_count):
        x_real = x_ref[pl.ds(d * devices, devices), 0, :, lane_window].reshape(rows * devices, lanes)
        x_imag = x_ref[pl.ds(d * devices, devices), 1, :, lane_window].reshape(rows * devices, lanes)
        cosine = t_ref[d, 0]
        sine = t_ref[d, 1]
        sum_real = jnp.dot(cosine, x_real, preferred_element_type=jnp.float32) + jnp.dot(
            sine, x_imag, preferred_element_type=jnp.float32
        )
        sum_imag = jnp.dot(cosine, x_imag, preferred_element_type=jnp.float32) - jnp.dot(
            sine, x_real, preferred_element_type=jnp.float32
        )
        cos_d = c_ref[d]
        sin_d = s_ref[d]
        part_real = sum_real * cos_d - sum_imag * sin_d
        part_imag = sum_real * sin_d + sum_imag * cos_d
        parts.append(
            (
                part_real.astype(jnp.bfloat16).astype(jnp.float32),
                part_imag.astype(jnp.bfloat16).astype(jnp.float32),
            )
        )
    (a_re, a_im), (b_re, b_im), (c_re, c_im), (d_re, d_im) = parts
    beams = [
        (a_re + b_re + c_re + d_re, a_im + b_im + c_im + d_im),
        (a_re + b_im - c_re - d_im, a_im - b_re - c_im + d_re),
        (a_re - b_re + c_re - d_re, a_im - b_im + c_im - d_im),
        (a_re - b_im - c_re + d_im, a_im + b_re - c_im - d_re),
    ]
    for q in range(dish_count):
        beam_real, beam_imag = beams[q]
        acc_ref[q] += beam_real * beam_real + beam_imag * beam_imag

    @pl.when(step == pl.num_programs(0) - 1)
    def _():
        if not finish:
            out_refs[0][...] = acc_ref[...]
            return
        me = lax.axis_index("dish")
        width = out_refs[0].shape[0]
        for shift in range(dish_count):
            target = jnp.bitwise_xor(me, shift)
            beam_index = jnp.bitwise_or(
                jnp.left_shift(jnp.bitwise_and(target, 1), 1), jnp.right_shift(target, 1)
            )
            total = acc_ref[beam_index]
            folded = total[:, :CHB]
            for k in range(1, lanes // CHB):
                folded = folded + total[:, k * CHB : (k + 1) * CHB]
            folded = folded + pltpu.roll(folded, width, 1)
            flipped = jnp.transpose(folded, (1, 0))
            out_refs[shift][...] = flipped[:width] * (0.25 / FRAMES)


def body(voltages, feed_gains, block_assign, grid_rows):
    dish_rows = voltages.shape[0]
    block_count = lax.axis_size("freq")
    dish_count = lax.axis_size("dish")
    block_width = NCHAN // block_count
    quarter = block_width // dish_count
    dests = block_count * dish_count
    grid_len = dish_rows * block_count
    total_dishes = grid_len * dish_count
    samples = voltages.shape[-1]

    dest = jnp.arange(dests, dtype=jnp.int32)
    dest_quarter = dest // block_count
    dest_block = jnp.tile(block_assign, dish_count)
    dest_e = dest_block * dish_count + dest_quarter
    picks_e = (dest_e[:, None] == jnp.arange(dests, dtype=jnp.int32)[None, :]).astype(jnp.bfloat16)

    window = jnp.asarray(window_constant().reshape(TAPS, CHA, CHB))
    first_cos, first_sin = table_constant(CHA, CHA, CHA, 1.0 / math.sqrt(CHA))
    first_table = np.block([[first_cos, first_sin], [-first_sin, first_cos]])
    first_table = jnp.asarray(first_table)
    twiddle = jnp.asarray(np.stack(rotation_constant(CHA, CHB, NCHAN), axis=0))
    second_cos, second_sin = table_constant(CHB, CHB, CHB, 1.0 / math.sqrt(CHB))
    second_table = np.stack(
        [np.stack([second_cos, -second_sin], axis=0), np.stack([second_sin, second_cos], axis=0)],
        axis=0,
    )
    second_table = jnp.einsum(
        "je,qseb->qsjb", picks_e, jnp.asarray(second_table), preferred_element_type=jnp.float32
    ).astype(jnp.bfloat16).reshape(2, 2 * dests, CHB)
    gains = feed_gains[:, 0].reshape(dish_rows, 2, CHB, CHA)
    gains = jnp.einsum("je,rpec->rpjc", picks_e, gains, preferred_element_type=jnp.float32)
    gains = gains.astype(jnp.bfloat16)

    chunk_pairs = [8]
    chunks = len(chunk_pairs)
    tables = beam_tables(grid_rows, grid_len, dish_rows)
    feed_index = jnp.arange(dish_count, dtype=jnp.int32)
    positions = jnp.arange(grid_len, dtype=jnp.int32)
    twist_cos, twist_sin = rotation_constant(dish_count, grid_len, total_dishes)
    twist_cos = jnp.asarray(twist_cos[:, :, None])
    twist_sin = jnp.asarray(twist_sin[:, :, None])
    lane_block = 2 * quarter

    volts = voltages[:, 0].reshape(dish_rows, 2, samples // CHB, CHB)

    def channelize_chunk(chunk):
        pairs = chunk_pairs[chunk]
        first_pair = sum(chunk_pairs[:chunk])
        chunk_lanes = pairs * 2 * quarter
        span = (2 * pairs + TAPS - 1) * CHA
        first_row = 2 * first_pair * CHA
        return pl.pallas_call(
            functools.partial(channelize_kernel, first_pair, pairs),
            grid=(dish_rows // FEEDS_PER_STEP,),
            in_specs=[
                pl.BlockSpec(
                    (pl.Element(FEEDS_PER_STEP), pl.Element(2), pl.Element(span), pl.Element(CHB)),
                    lambda r: (r * FEEDS_PER_STEP, 0, first_row, 0),
                ),
                pl.BlockSpec((TAPS, CHA, CHB), lambda r: (0, 0, 0)),
                pl.BlockSpec((2 * CHA, 2 * CHA), lambda r: (0, 0)),
                pl.BlockSpec((2, CHA, CHB), lambda r: (0, 0, 0)),
                pl.BlockSpec((2, 2 * dests, CHB), lambda r: (0, 0, 0)),
                pl.BlockSpec((FEEDS_PER_STEP, 2, dests, CHA), lambda r: (r, 0, 0, 0)),
            ],
            out_specs=pl.BlockSpec((2, FEEDS_PER_STEP, dests, chunk_lanes), lambda r: (0, r, 0, 0)),
            out_shape=jax.ShapeDtypeStruct((2, dish_rows, dests, chunk_lanes), jnp.bfloat16),
            cost_estimate=pl.CostEstimate(
                flops=int(dish_rows * pairs * 2 * 2 * 128 * 128 * 128 * 3),
                bytes_accessed=int(voltages.size * 2 + 2 * dish_rows * dests * chunk_lanes * 2),
                transcendentals=0,
            ),
        )(volts, window, first_table, twiddle, second_table, gains)

    def beamform_chunk(received, carried, finish):
        carry_in = carried is not None
        chunk_lanes = received.shape[3]
        in_specs = [
            pl.BlockSpec((dests, 2, dish_rows, lane_block), lambda f: (0, 0, 0, f)),
            pl.BlockSpec((dish_count, 2, grid_len, grid_len), lambda f: (0, 0, 0, 0)),
        ]
        in_specs += [pl.BlockSpec((dish_count, grid_len, 1), lambda f: (0, 0, 0))] * 2
        operands = [received, tables, twist_cos, twist_sin]
        if carry_in:
            in_specs.append(pl.BlockSpec((dish_count, grid_len, lane_block), lambda f: (0, 0, 0)))
            operands.append(carried)
        if finish:
            out_specs = [pl.BlockSpec((quarter, grid_len), lambda f: (0, 0))] * dish_count
            out_shape = [jax.ShapeDtypeStruct((quarter, grid_len), jnp.float32)] * dish_count
        else:
            out_specs = pl.BlockSpec((dish_count, grid_len, lane_block), lambda f: (0, 0, 0))
            out_shape = jax.ShapeDtypeStruct((dish_count, grid_len, lane_block), jnp.float32)
        return pl.pallas_call(
            functools.partial(beam_kernel, dish_count, carry_in, finish, lane_block),
            grid=(chunk_lanes // lane_block,),
            in_specs=in_specs,
            out_specs=out_specs,
            out_shape=out_shape,
            scratch_shapes=[pltpu.VMEM((dish_count, grid_len, lane_block), jnp.float32)],
            cost_estimate=pl.CostEstimate(
                flops=int(dish_count * 2 * 512 * 512 * chunk_lanes),
                bytes_accessed=int(received.size * 2 + tables.size * 2),
                transcendentals=0,
            ),
        )(*operands)

    sent = [channelize_chunk(c) for c in range(chunks)]
    arrived = [
        jnp.transpose(lax.all_to_all(s, ("dish", "freq"), 2, 2, tiled=True), (2, 0, 1, 3))
        for s in sent
    ]
    carried = None
    for c in range(chunks):
        carried = beamform_chunk(arrived[c], carried, c == chunks - 1)
    powers = carried

    me = lax.axis_index("dish")
    pieces = [powers[0]]
    for shift in range(1, dish_count):
        outgoing = powers[shift]
        pairs_list = [(i, i ^ shift) for i in range(dish_count)]
        pieces.append(lax.ppermute(outgoing, "dish", pairs_list))
    blocks = []
    for source in range(dish_count):
        shift_of = jnp.bitwise_xor(me, source)
        chosen = pieces[dish_count - 1]
        for shift in range(dish_count - 2, -1, -1):
            chosen = jnp.where(shift_of == shift, pieces[shift], chosen)
        blocks.append(chosen)
    return jnp.concatenate(blocks, axis=0)


def solution(mesh):
    placed = (P("freq", "dish", None, None), P("freq", "dish", None, None), P(), P())
    return jax.shard_map(
        body, mesh=mesh, in_specs=placed, out_specs=P("freq", "dish"), check_vma=False
    )
```

```python
import functools
import math

import jax
import jax.numpy as jnp
import ml_dtypes
import numpy as np
from jax import lax
from jax.experimental import pallas as pl
from jax.experimental.pallas import tpu as pltpu
from jax.sharding import PartitionSpec as P

NCHAN = 8192
CHA = 64
CHB = 128
TAPS = 4
FRAMES = 16
FEEDS_PER_STEP = 4


full_turn = 2.0 * math.pi


def table_constant(row_count, col_count, modulus, scaling):
    rows = np.arange(row_count, dtype=np.int64)[:, None]
    cols = np.arange(col_count, dtype=np.int64)[None, :]
    angles = np.float32(full_turn / modulus) * (rows * cols % modulus).astype(np.float32)
    cosine = (np.cos(angles.astype(np.float64)) * scaling).astype(ml_dtypes.bfloat16)
    sine = (np.sin(angles.astype(np.float64)) * scaling).astype(ml_dtypes.bfloat16)
    return cosine, sine


def window_constant():
    sample_index = np.arange(TAPS * NCHAN, dtype=np.float64)
    centred = (sample_index - TAPS * NCHAN / 2 + 0.5) / NCHAN
    taper_curve = 0.5 - 0.5 * np.cos(full_turn * (sample_index + 0.5) / (TAPS * NCHAN))
    shaped_window = (np.sinc(centred) * taper_curve).reshape(TAPS, NCHAN)
    energy = np.mean(np.sum(shaped_window * shaped_window, axis=0))
    return (shaped_window / np.sqrt(energy)).astype(np.float32)


def rotation_constant(row_count, col_count, modulus):
    rows = np.arange(row_count, dtype=np.int64)[:, None]
    cols = np.arange(col_count, dtype=np.int64)[None, :]
    angles = np.float32(-(full_turn / modulus)) * (rows * cols % modulus).astype(np.float32)
    angles = angles.astype(np.float64)
    return np.cos(angles).astype(np.float32), np.sin(angles).astype(np.float32)


def fourier_table(row_index, col_index, modulus, scaling):
    phases = row_index[:, None] * col_index[None, :] % modulus
    angles = full_turn / modulus * phases.astype(jnp.float32)
    cosine_table = (jnp.cos(angles) * scaling).astype(jnp.bfloat16)
    sine_table = (jnp.sin(angles) * scaling).astype(jnp.bfloat16)
    upper_rows = jnp.stack([cosine_table, -sine_table], axis=1)
    lower_rows = jnp.stack([sine_table, cosine_table], axis=1)
    return jnp.stack([upper_rows, lower_rows], axis=0)


def filter_window():
    sample_index = jnp.arange(TAPS * NCHAN, dtype=jnp.float32)
    centred = (sample_index - TAPS * NCHAN / 2 + 0.5) / NCHAN
    taper_curve = 0.5 - 0.5 * jnp.cos(full_turn * (sample_index + 0.5) / (TAPS * NCHAN))
    shaped_window = (jnp.sinc(centred) * taper_curve).reshape(TAPS, NCHAN)
    energy = jnp.mean(jnp.sum(shaped_window * shaped_window, axis=0))
    return shaped_window / jnp.sqrt(energy)


def beam_tables(grid_rows, grid_len, rows_per_device):
    positions = jnp.arange(grid_len, dtype=jnp.int32)
    cosine_base, sine_base = table_constant(grid_len, grid_len, grid_len, 1.0 / math.sqrt(grid_len))
    cosine_base = jnp.asarray(cosine_base)
    sine_base = jnp.asarray(sine_base)
    devices = grid_len // rows_per_device
    picks = (positions[None, :, None] == grid_rows[:, None, :]).astype(jnp.bfloat16)
    cosine_table = jnp.einsum(
        "jg,dgm->djm", cosine_base, picks, preferred_element_type=jnp.float32
    ).astype(jnp.bfloat16)
    sine_table = jnp.einsum(
        "jg,dgm->djm", sine_base, picks, preferred_element_type=jnp.float32
    ).astype(jnp.bfloat16)
    return jnp.stack([cosine_table, sine_table], axis=1)


def channelize_kernel(first_pair, pairs, v_ref, w_ref, t1_ref, tw_ref, t2_ref, g_ref, o_ref):
    cos_tw = tw_ref[0]
    sin_tw = tw_ref[1]
    t1 = t1_ref[...]
    t2_real = t2_ref[0]
    t2_imag = t2_ref[1]
    half = t2_real.shape[0] // 2
    feeds = v_ref.shape[0]

    def one_frame(pieces):
        acc = None
        for tap in range(TAPS):
            term = w_ref[tap][None] * pieces[tap]
            acc = term if acc is None else acc + term
        block = acc.astype(jnp.bfloat16).reshape(2 * CHA, CHB)
        section = jnp.dot(t1, block, preferred_element_type=jnp.float32)
        sec_real = section[:CHA]
        sec_imag = section[CHA:]
        turned_real = sec_real * cos_tw - sec_imag * sin_tw
        turned_imag = sec_real * sin_tw + sec_imag * cos_tw
        return turned_real.astype(jnp.bfloat16), turned_imag.astype(jnp.bfloat16)

    def pair(feed, step, g_real, g_imag):
        pieces = []
        for offset in range(TAPS + 1):
            start = pl.multiple_of((2 * (step - first_pair) + offset) * CHA, CHA)
            pieces.append(v_ref[feed, :, pl.ds(start, CHA), :].astype(jnp.float32))
        first_real, first_imag = one_frame(pieces[:TAPS])
        second_real, second_imag = one_frame(pieces[1:])
        both_real = jnp.concatenate([first_real, second_real], axis=0)
        both_imag = jnp.concatenate([first_imag, second_imag], axis=0)
        dims = (((1,), (1,)), ((), ()))
        spectrum = lax.dot_general(
            t2_real, both_real, dims, preferred_element_type=jnp.float32
        ) + lax.dot_general(t2_imag, both_imag, dims, preferred_element_type=jnp.float32)
        spec_real = spectrum[:half]
        spec_imag = spectrum[half:]
        out_real = spec_real * g_real - spec_imag * g_imag
        out_imag = spec_real * g_imag + spec_imag * g_real
        lanes = pl.ds(pl.multiple_of((step - first_pair) * 2 * CHA, 2 * CHA), 2 * CHA)
        o_ref[0, feed, :, lanes] = out_real.astype(o_ref.dtype)
        o_ref[1, feed, :, lanes] = out_imag.astype(o_ref.dtype)

    for feed in range(feeds):
        g_half_real = g_ref[feed, 0].astype(jnp.float32)
        g_half_imag = g_ref[feed, 1].astype(jnp.float32)
        g_real = jnp.concatenate([g_half_real, g_half_real], axis=1)
        g_imag = jnp.concatenate([g_half_imag, g_half_imag], axis=1)
        for step in range(first_pair, first_pair + pairs):
            pair(feed, step, g_real, g_imag)


def beam_kernel(dish_count, carry_in, finish, lanes, *refs):
    x_ref, t_ref, c_ref, s_ref = refs[:4]
    init_ref = refs[4] if carry_in else None
    out_refs = refs[4 + carry_in : -1]
    acc_ref = refs[-1]
    step = pl.program_id(0)
    devices = x_ref.shape[0] // dish_count
    rows = x_ref.shape[2]
    grid_len = t_ref.shape[2]
    lane_window = slice(None)

    @pl.when(step == 0)
    def _():
        if carry_in:
            acc_ref[...] = init_ref[...]
        else:
            acc_ref[...] = jnp.zeros_like(acc_ref)

    parts = []
    for d in range(dish_count):
        x_real = x_ref[pl.ds(d * devices, devices), 0, :, lane_window].reshape(rows * devices, lanes)
        x_imag = x_ref[pl.ds(d * devices, devices), 1, :, lane_window].reshape(rows * devices, lanes)
        cosine = t_ref[d, 0]
        sine = t_ref[d, 1]
        sum_real = jnp.dot(cosine, x_real, preferred_element_type=jnp.float32) + jnp.dot(
            sine, x_imag, preferred_element_type=jnp.float32
        )
        sum_imag = jnp.dot(cosine, x_imag, preferred_element_type=jnp.float32) - jnp.dot(
            sine, x_real, preferred_element_type=jnp.float32
        )
        cos_d = c_ref[d]
        sin_d = s_ref[d]
        part_real = sum_real * cos_d - sum_imag * sin_d
        part_imag = sum_real * sin_d + sum_imag * cos_d
        parts.append(
            (
                part_real.astype(jnp.bfloat16).astype(jnp.float32),
                part_imag.astype(jnp.bfloat16).astype(jnp.float32),
            )
        )
    (a_re, a_im), (b_re, b_im), (c_re, c_im), (d_re, d_im) = parts
    beams = [
        (a_re + b_re + c_re + d_re, a_im + b_im + c_im + d_im),
        (a_re + b_im - c_re - d_im, a_im - b_re - c_im + d_re),
        (a_re - b_re + c_re - d_re, a_im - b_im + c_im - d_im),
        (a_re - b_im - c_re + d_im, a_im + b_re - c_im - d_re),
    ]
    for q in range(dish_count):
        beam_real, beam_imag = beams[q]
        acc_ref[q] += beam_real * beam_real + beam_imag * beam_imag

    @pl.when(step == pl.num_programs(0) - 1)
    def _():
        if not finish:
            out_refs[0][...] = acc_ref[...]
            return
        me = lax.axis_index("dish")
        width = out_refs[0].shape[0]
        for shift in range(dish_count):
            target = jnp.bitwise_xor(me, shift)
            beam_index = jnp.bitwise_or(
                jnp.left_shift(jnp.bitwise_and(target, 1), 1), jnp.right_shift(target, 1)
            )
            total = acc_ref[beam_index]
            folded = total[:, :CHB]
            for k in range(1, lanes // CHB):
                folded = folded + total[:, k * CHB : (k + 1) * CHB]
            folded = folded + pltpu.roll(folded, width, 1)
            flipped = jnp.transpose(folded, (1, 0))
            out_refs[shift][...] = flipped[:width] * (0.25 / FRAMES)


def body(voltages, feed_gains, block_assign, grid_rows):
    dish_rows = voltages.shape[0]
    block_count = lax.axis_size("freq")
    dish_count = lax.axis_size("dish")
    block_width = NCHAN // block_count
    quarter = block_width // dish_count
    dests = block_count * dish_count
    grid_len = dish_rows * block_count
    total_dishes = grid_len * dish_count
    samples = voltages.shape[-1]

    dest = jnp.arange(dests, dtype=jnp.int32)
    dest_quarter = dest // block_count
    dest_block = jnp.tile(block_assign, dish_count)
    dest_e = dest_block * dish_count + dest_quarter
    picks_e = (dest_e[:, None] == jnp.arange(dests, dtype=jnp.int32)[None, :]).astype(jnp.bfloat16)

    window = jnp.asarray(window_constant().reshape(TAPS, CHA, CHB))
    first_cos, first_sin = table_constant(CHA, CHA, CHA, 1.0 / math.sqrt(CHA))
    first_table = np.block([[first_cos, first_sin], [-first_sin, first_cos]])
    first_table = jnp.asarray(first_table)
    twiddle = jnp.asarray(np.stack(rotation_constant(CHA, CHB, NCHAN), axis=0))
    second_cos, second_sin = table_constant(CHB, CHB, CHB, 1.0 / math.sqrt(CHB))
    second_table = np.stack(
        [np.stack([second_cos, -second_sin], axis=0), np.stack([second_sin, second_cos], axis=0)],
        axis=0,
    )
    second_table = jnp.einsum(
        "je,qseb->qsjb", picks_e, jnp.asarray(second_table), preferred_element_type=jnp.float32
    ).astype(jnp.bfloat16).reshape(2, 2 * dests, CHB)
    gains = feed_gains[:, 0].reshape(dish_rows, 2, CHB, CHA)
    gains = jnp.einsum("je,rpec->rpjc", picks_e, gains, preferred_element_type=jnp.float32)
    gains = gains.astype(jnp.bfloat16)

    chunk_pairs = [8]
    chunks = len(chunk_pairs)
    tables = beam_tables(grid_rows, grid_len, dish_rows)
    feed_index = jnp.arange(dish_count, dtype=jnp.int32)
    positions = jnp.arange(grid_len, dtype=jnp.int32)
    twist_cos, twist_sin = rotation_constant(dish_count, grid_len, total_dishes)
    twist_cos = jnp.asarray(twist_cos[:, :, None])
    twist_sin = jnp.asarray(twist_sin[:, :, None])
    lane_block = 8 * quarter

    volts = voltages[:, 0].reshape(dish_rows, 2, samples // CHB, CHB)

    def channelize_chunk(chunk):
        pairs = chunk_pairs[chunk]
        first_pair = sum(chunk_pairs[:chunk])
        chunk_lanes = pairs * 2 * quarter
        span = (2 * pairs + TAPS - 1) * CHA
        first_row = 2 * first_pair * CHA
        return pl.pallas_call(
            functools.partial(channelize_kernel, first_pair, pairs),
            grid=(dish_rows // FEEDS_PER_STEP,),
            in_specs=[
                pl.BlockSpec(
                    (pl.Element(FEEDS_PER_STEP), pl.Element(2), pl.Element(span), pl.Element(CHB)),
                    lambda r: (r * FEEDS_PER_STEP, 0, first_row, 0),
                ),
                pl.BlockSpec((TAPS, CHA, CHB), lambda r: (0, 0, 0)),
                pl.BlockSpec((2 * CHA, 2 * CHA), lambda r: (0, 0)),
                pl.BlockSpec((2, CHA, CHB), lambda r: (0, 0, 0)),
                pl.BlockSpec((2, 2 * dests, CHB), lambda r: (0, 0, 0)),
                pl.BlockSpec((FEEDS_PER_STEP, 2, dests, CHA), lambda r: (r, 0, 0, 0)),
            ],
            out_specs=pl.BlockSpec((2, FEEDS_PER_STEP, dests, chunk_lanes), lambda r: (0, r, 0, 0)),
            out_shape=jax.ShapeDtypeStruct((2, dish_rows, dests, chunk_lanes), jnp.bfloat16),
            cost_estimate=pl.CostEstimate(
                flops=int(dish_rows * pairs * 2 * 2 * 128 * 128 * 128 * 3),
                bytes_accessed=int(voltages.size * 2 + 2 * dish_rows * dests * chunk_lanes * 2),
                transcendentals=0,
            ),
        )(volts, window, first_table, twiddle, second_table, gains)

    def beamform_chunk(received, carried, finish):
        carry_in = carried is not None
        chunk_lanes = received.shape[3]
        in_specs = [
            pl.BlockSpec((dests, 2, dish_rows, lane_block), lambda f: (0, 0, 0, f)),
            pl.BlockSpec((dish_count, 2, grid_len, grid_len), lambda f: (0, 0, 0, 0)),
        ]
        in_specs += [pl.BlockSpec((dish_count, grid_len, 1), lambda f: (0, 0, 0))] * 2
        operands = [received, tables, twist_cos, twist_sin]
        if carry_in:
            in_specs.append(pl.BlockSpec((dish_count, grid_len, lane_block), lambda f: (0, 0, 0)))
            operands.append(carried)
        if finish:
            out_specs = [pl.BlockSpec((quarter, grid_len), lambda f: (0, 0))] * dish_count
            out_shape = [jax.ShapeDtypeStruct((quarter, grid_len), jnp.float32)] * dish_count
        else:
            out_specs = pl.BlockSpec((dish_count, grid_len, lane_block), lambda f: (0, 0, 0))
            out_shape = jax.ShapeDtypeStruct((dish_count, grid_len, lane_block), jnp.float32)
        return pl.pallas_call(
            functools.partial(beam_kernel, dish_count, carry_in, finish, lane_block),
            grid=(chunk_lanes // lane_block,),
            in_specs=in_specs,
            out_specs=out_specs,
            out_shape=out_shape,
            scratch_shapes=[pltpu.VMEM((dish_count, grid_len, lane_block), jnp.float32)],
            cost_estimate=pl.CostEstimate(
                flops=int(dish_count * 2 * 512 * 512 * chunk_lanes),
                bytes_accessed=int(received.size * 2 + tables.size * 2),
                transcendentals=0,
            ),
        )(*operands)

    sent = [channelize_chunk(c) for c in range(chunks)]
    arrived = [
        jnp.transpose(lax.all_to_all(s, ("dish", "freq"), 2, 2, tiled=True), (2, 0, 1, 3))
        for s in sent
    ]
    carried = None
    for c in range(chunks):
        carried = beamform_chunk(arrived[c], carried, c == chunks - 1)
    powers = carried

    me = lax.axis_index("dish")
    pieces = [powers[0]]
    for shift in range(1, dish_count):
        outgoing = powers[shift]
        pairs_list = [(i, i ^ shift) for i in range(dish_count)]
        pieces.append(lax.ppermute(outgoing, "dish", pairs_list))
    blocks = []
    for source in range(dish_count):
        shift_of = jnp.bitwise_xor(me, source)
        chosen = pieces[dish_count - 1]
        for shift in range(dish_count - 2, -1, -1):
            chosen = jnp.where(shift_of == shift, pieces[shift], chosen)
        blocks.append(chosen)
    return jnp.concatenate(blocks, axis=0)


def solution(mesh):
    placed = (P("freq", "dish", None, None), P("freq", "dish", None, None), P(), P())
    return jax.shard_map(
        body, mesh=mesh, in_specs=placed, out_specs=P("freq", "dish"), check_vma=False
    )
```

```python
import functools
import math

import jax
import jax.numpy as jnp
import ml_dtypes
import numpy as np
from jax import lax
from jax.experimental import pallas as pl
from jax.experimental.pallas import tpu as pltpu
from jax.sharding import PartitionSpec as P

NCHAN = 8192
CHA = 64
CHB = 128
TAPS = 4
FRAMES = 16
FEEDS_PER_STEP = 2


full_turn = 2.0 * math.pi


def table_constant(row_count, col_count, modulus, scaling):
    rows = np.arange(row_count, dtype=np.int64)[:, None]
    cols = np.arange(col_count, dtype=np.int64)[None, :]
    angles = np.float32(full_turn / modulus) * (rows * cols % modulus).astype(np.float32)
    cosine = (np.cos(angles.astype(np.float64)) * scaling).astype(ml_dtypes.bfloat16)
    sine = (np.sin(angles.astype(np.float64)) * scaling).astype(ml_dtypes.bfloat16)
    return cosine, sine


def window_constant():
    sample_index = np.arange(TAPS * NCHAN, dtype=np.float64)
    centred = (sample_index - TAPS * NCHAN / 2 + 0.5) / NCHAN
    taper_curve = 0.5 - 0.5 * np.cos(full_turn * (sample_index + 0.5) / (TAPS * NCHAN))
    shaped_window = (np.sinc(centred) * taper_curve).reshape(TAPS, NCHAN)
    energy = np.mean(np.sum(shaped_window * shaped_window, axis=0))
    return (shaped_window / np.sqrt(energy)).astype(np.float32)


def rotation_constant(row_count, col_count, modulus):
    rows = np.arange(row_count, dtype=np.int64)[:, None]
    cols = np.arange(col_count, dtype=np.int64)[None, :]
    angles = np.float32(-(full_turn / modulus)) * (rows * cols % modulus).astype(np.float32)
    angles = angles.astype(np.float64)
    return np.cos(angles).astype(np.float32), np.sin(angles).astype(np.float32)


def fourier_table(row_index, col_index, modulus, scaling):
    phases = row_index[:, None] * col_index[None, :] % modulus
    angles = full_turn / modulus * phases.astype(jnp.float32)
    cosine_table = (jnp.cos(angles) * scaling).astype(jnp.bfloat16)
    sine_table = (jnp.sin(angles) * scaling).astype(jnp.bfloat16)
    upper_rows = jnp.stack([cosine_table, -sine_table], axis=1)
    lower_rows = jnp.stack([sine_table, cosine_table], axis=1)
    return jnp.stack([upper_rows, lower_rows], axis=0)


def filter_window():
    sample_index = jnp.arange(TAPS * NCHAN, dtype=jnp.float32)
    centred = (sample_index - TAPS * NCHAN / 2 + 0.5) / NCHAN
    taper_curve = 0.5 - 0.5 * jnp.cos(full_turn * (sample_index + 0.5) / (TAPS * NCHAN))
    shaped_window = (jnp.sinc(centred) * taper_curve).reshape(TAPS, NCHAN)
    energy = jnp.mean(jnp.sum(shaped_window * shaped_window, axis=0))
    return shaped_window / jnp.sqrt(energy)


def beam_tables(grid_rows, grid_len, rows_per_device):
    positions = jnp.arange(grid_len, dtype=jnp.int32)
    cosine_base, sine_base = table_constant(grid_len, grid_len, grid_len, 1.0 / math.sqrt(grid_len))
    cosine_base = jnp.asarray(cosine_base)
    sine_base = jnp.asarray(sine_base)
    devices = grid_len // rows_per_device
    picks = (positions[None, :, None] == grid_rows[:, None, :]).astype(jnp.bfloat16)
    cosine_table = jnp.einsum(
        "jg,dgm->djm", cosine_base, picks, preferred_element_type=jnp.float32
    ).astype(jnp.bfloat16)
    sine_table = jnp.einsum(
        "jg,dgm->djm", sine_base, picks, preferred_element_type=jnp.float32
    ).astype(jnp.bfloat16)
    return jnp.stack([cosine_table, sine_table], axis=1)


def channelize_kernel(first_pair, pairs, v_ref, w_ref, t1_ref, tw_ref, t2_ref, g_ref, o_ref):
    cos_tw = tw_ref[0]
    sin_tw = tw_ref[1]
    t1 = t1_ref[...]
    t2_real = t2_ref[0]
    t2_imag = t2_ref[1]
    half = t2_real.shape[0] // 2
    feeds = v_ref.shape[0]

    def one_frame(pieces):
        acc = None
        for tap in range(TAPS):
            term = w_ref[tap][None] * pieces[tap]
            acc = term if acc is None else acc + term
        block = acc.astype(jnp.bfloat16).reshape(2 * CHA, CHB)
        section = jnp.dot(t1, block, preferred_element_type=jnp.float32)
        sec_real = section[:CHA]
        sec_imag = section[CHA:]
        turned_real = sec_real * cos_tw - sec_imag * sin_tw
        turned_imag = sec_real * sin_tw + sec_imag * cos_tw
        return turned_real.astype(jnp.bfloat16), turned_imag.astype(jnp.bfloat16)

    def pair(feed, step, g_real, g_imag):
        pieces = []
        for offset in range(TAPS + 1):
            start = pl.multiple_of((2 * (step - first_pair) + offset) * CHA, CHA)
            pieces.append(v_ref[feed, :, pl.ds(start, CHA), :].astype(jnp.float32))
        first_real, first_imag = one_frame(pieces[:TAPS])
        second_real, second_imag = one_frame(pieces[1:])
        both_real = jnp.concatenate([first_real, second_real], axis=0)
        both_imag = jnp.concatenate([first_imag, second_imag], axis=0)
        dims = (((1,), (1,)), ((), ()))
        spectrum = lax.dot_general(
            t2_real, both_real, dims, preferred_element_type=jnp.float32
        ) + lax.dot_general(t2_imag, both_imag, dims, preferred_element_type=jnp.float32)
        spec_real = spectrum[:half]
        spec_imag = spectrum[half:]
        out_real = spec_real * g_real - spec_imag * g_imag
        out_imag = spec_real * g_imag + spec_imag * g_real
        lanes = pl.ds(pl.multiple_of((step - first_pair) * 2 * CHA, 2 * CHA), 2 * CHA)
        o_ref[0, feed, :, lanes] = out_real.astype(o_ref.dtype)
        o_ref[1, feed, :, lanes] = out_imag.astype(o_ref.dtype)

    for feed in range(feeds):
        g_half_real = g_ref[feed, 0].astype(jnp.float32)
        g_half_imag = g_ref[feed, 1].astype(jnp.float32)
        g_real = jnp.concatenate([g_half_real, g_half_real], axis=1)
        g_imag = jnp.concatenate([g_half_imag, g_half_imag], axis=1)
        for step in range(first_pair, first_pair + pairs):
            pair(feed, step, g_real, g_imag)


def beam_kernel(dish_count, carry_in, finish, lanes, *refs):
    x_ref, t_ref, c_ref, s_ref = refs[:4]
    init_ref = refs[4] if carry_in else None
    out_refs = refs[4 + carry_in : -1]
    acc_ref = refs[-1]
    step = pl.program_id(0)
    devices = x_ref.shape[0] // dish_count
    rows = x_ref.shape[2]
    grid_len = t_ref.shape[2]
    lane_window = slice(None)

    @pl.when(step == 0)
    def _():
        if carry_in:
            acc_ref[...] = init_ref[...]
        else:
            acc_ref[...] = jnp.zeros_like(acc_ref)

    parts = []
    for d in range(dish_count):
        x_real = x_ref[pl.ds(d * devices, devices), 0, :, lane_window].reshape(rows * devices, lanes)
        x_imag = x_ref[pl.ds(d * devices, devices), 1, :, lane_window].reshape(rows * devices, lanes)
        cosine = t_ref[d, 0]
        sine = t_ref[d, 1]
        sum_real = jnp.dot(cosine, x_real, preferred_element_type=jnp.float32) + jnp.dot(
            sine, x_imag, preferred_element_type=jnp.float32
        )
        sum_imag = jnp.dot(cosine, x_imag, preferred_element_type=jnp.float32) - jnp.dot(
            sine, x_real, preferred_element_type=jnp.float32
        )
        cos_d = c_ref[d]
        sin_d = s_ref[d]
        part_real = sum_real * cos_d - sum_imag * sin_d
        part_imag = sum_real * sin_d + sum_imag * cos_d
        parts.append(
            (
                part_real.astype(jnp.bfloat16).astype(jnp.float32),
                part_imag.astype(jnp.bfloat16).astype(jnp.float32),
            )
        )
    (a_re, a_im), (b_re, b_im), (c_re, c_im), (d_re, d_im) = parts
    beams = [
        (a_re + b_re + c_re + d_re, a_im + b_im + c_im + d_im),
        (a_re + b_im - c_re - d_im, a_im - b_re - c_im + d_re),
        (a_re - b_re + c_re - d_re, a_im - b_im + c_im - d_im),
        (a_re - b_im - c_re + d_im, a_im + b_re - c_im - d_re),
    ]
    for q in range(dish_count):
        beam_real, beam_imag = beams[q]
        acc_ref[q] += beam_real * beam_real + beam_imag * beam_imag

    @pl.when(step == pl.num_programs(0) - 1)
    def _():
        if not finish:
            out_refs[0][...] = acc_ref[...]
            return
        me = lax.axis_index("dish")
        width = out_refs[0].shape[0]
        for shift in range(dish_count):
            target = jnp.bitwise_xor(me, shift)
            beam_index = jnp.bitwise_or(
                jnp.left_shift(jnp.bitwise_and(target, 1), 1), jnp.right_shift(target, 1)
            )
            total = acc_ref[beam_index]
            folded = total[:, :CHB]
            for k in range(1, lanes // CHB):
                folded = folded + total[:, k * CHB : (k + 1) * CHB]
            folded = folded + pltpu.roll(folded, width, 1)
            flipped = jnp.transpose(folded, (1, 0))
            out_refs[shift][...] = flipped[:width] * (0.25 / FRAMES)


def body(voltages, feed_gains, block_assign, grid_rows):
    dish_rows = voltages.shape[0]
    block_count = lax.axis_size("freq")
    dish_count = lax.axis_size("dish")
    block_width = NCHAN // block_count
    quarter = block_width // dish_count
    dests = block_count * dish_count
    grid_len = dish_rows * block_count
    total_dishes = grid_len * dish_count
    samples = voltages.shape[-1]

    dest = jnp.arange(dests, dtype=jnp.int32)
    dest_quarter = dest // block_count
    dest_block = jnp.tile(block_assign, dish_count)
    dest_e = dest_block * dish_count + dest_quarter
    picks_e = (dest_e[:, None] == jnp.arange(dests, dtype=jnp.int32)[None, :]).astype(jnp.bfloat16)

    window = jnp.asarray(window_constant().reshape(TAPS, CHA, CHB))
    first_cos, first_sin = table_constant(CHA, CHA, CHA, 1.0 / math.sqrt(CHA))
    first_table = np.block([[first_cos, first_sin], [-first_sin, first_cos]])
    first_table = jnp.asarray(first_table)
    twiddle = jnp.asarray(np.stack(rotation_constant(CHA, CHB, NCHAN), axis=0))
    second_cos, second_sin = table_constant(CHB, CHB, CHB, 1.0 / math.sqrt(CHB))
    second_table = np.stack(
        [np.stack([second_cos, -second_sin], axis=0), np.stack([second_sin, second_cos], axis=0)],
        axis=0,
    )
    second_table = jnp.einsum(
        "je,qseb->qsjb", picks_e, jnp.asarray(second_table), preferred_element_type=jnp.float32
    ).astype(jnp.bfloat16).reshape(2, 2 * dests, CHB)
    gains = feed_gains[:, 0].reshape(dish_rows, 2, CHB, CHA)
    gains = jnp.einsum("je,rpec->rpjc", picks_e, gains, preferred_element_type=jnp.float32)
    gains = gains.astype(jnp.bfloat16)

    chunk_pairs = [8]
    chunks = len(chunk_pairs)
    tables = beam_tables(grid_rows, grid_len, dish_rows)
    feed_index = jnp.arange(dish_count, dtype=jnp.int32)
    positions = jnp.arange(grid_len, dtype=jnp.int32)
    twist_cos, twist_sin = rotation_constant(dish_count, grid_len, total_dishes)
    twist_cos = jnp.asarray(twist_cos[:, :, None])
    twist_sin = jnp.asarray(twist_sin[:, :, None])
    lane_block = 4 * quarter

    volts = voltages[:, 0].reshape(dish_rows, 2, samples // CHB, CHB)

    def channelize_chunk(chunk):
        pairs = chunk_pairs[chunk]
        first_pair = sum(chunk_pairs[:chunk])
        chunk_lanes = pairs * 2 * quarter
        span = (2 * pairs + TAPS - 1) * CHA
        first_row = 2 * first_pair * CHA
        return pl.pallas_call(
            functools.partial(channelize_kernel, first_pair, pairs),
            grid=(dish_rows // FEEDS_PER_STEP,),
            in_specs=[
                pl.BlockSpec(
                    (pl.Element(FEEDS_PER_STEP), pl.Element(2), pl.Element(span), pl.Element(CHB)),
                    lambda r: (r * FEEDS_PER_STEP, 0, first_row, 0),
                ),
                pl.BlockSpec((TAPS, CHA, CHB), lambda r: (0, 0, 0)),
                pl.BlockSpec((2 * CHA, 2 * CHA), lambda r: (0, 0)),
                pl.BlockSpec((2, CHA, CHB), lambda r: (0, 0, 0)),
                pl.BlockSpec((2, 2 * dests, CHB), lambda r: (0, 0, 0)),
                pl.BlockSpec((FEEDS_PER_STEP, 2, dests, CHA), lambda r: (r, 0, 0, 0)),
            ],
            out_specs=pl.BlockSpec((2, FEEDS_PER_STEP, dests, chunk_lanes), lambda r: (0, r, 0, 0)),
            out_shape=jax.ShapeDtypeStruct((2, dish_rows, dests, chunk_lanes), jnp.bfloat16),
            cost_estimate=pl.CostEstimate(
                flops=int(dish_rows * pairs * 2 * 2 * 128 * 128 * 128 * 3),
                bytes_accessed=int(voltages.size * 2 + 2 * dish_rows * dests * chunk_lanes * 2),
                transcendentals=0,
            ),
        )(volts, window, first_table, twiddle, second_table, gains)

    def beamform_chunk(received, carried, finish):
        carry_in = carried is not None
        chunk_lanes = received.shape[3]
        in_specs = [
            pl.BlockSpec((dests, 2, dish_rows, lane_block), lambda f: (0, 0, 0, f)),
            pl.BlockSpec((dish_count, 2, grid_len, grid_len), lambda f: (0, 0, 0, 0)),
        ]
        in_specs += [pl.BlockSpec((dish_count, grid_len, 1), lambda f: (0, 0, 0))] * 2
        operands = [received, tables, twist_cos, twist_sin]
        if carry_in:
            in_specs.append(pl.BlockSpec((dish_count, grid_len, lane_block), lambda f: (0, 0, 0)))
            operands.append(carried)
        if finish:
            out_specs = [pl.BlockSpec((quarter, grid_len), lambda f: (0, 0))] * dish_count
            out_shape = [jax.ShapeDtypeStruct((quarter, grid_len), jnp.float32)] * dish_count
        else:
            out_specs = pl.BlockSpec((dish_count, grid_len, lane_block), lambda f: (0, 0, 0))
            out_shape = jax.ShapeDtypeStruct((dish_count, grid_len, lane_block), jnp.float32)
        return pl.pallas_call(
            functools.partial(beam_kernel, dish_count, carry_in, finish, lane_block),
            grid=(chunk_lanes // lane_block,),
            in_specs=in_specs,
            out_specs=out_specs,
            out_shape=out_shape,
            scratch_shapes=[pltpu.VMEM((dish_count, grid_len, lane_block), jnp.float32)],
            cost_estimate=pl.CostEstimate(
                flops=int(dish_count * 2 * 512 * 512 * chunk_lanes),
                bytes_accessed=int(received.size * 2 + tables.size * 2),
                transcendentals=0,
            ),
        )(*operands)

    sent = [channelize_chunk(c) for c in range(chunks)]
    arrived = [
        jnp.transpose(lax.all_to_all(s, ("dish", "freq"), 2, 2, tiled=True), (2, 0, 1, 3))
        for s in sent
    ]
    carried = None
    for c in range(chunks):
        carried = beamform_chunk(arrived[c], carried, c == chunks - 1)
    powers = carried

    me = lax.axis_index("dish")
    pieces = [powers[0]]
    for shift in range(1, dish_count):
        outgoing = powers[shift]
        pairs_list = [(i, i ^ shift) for i in range(dish_count)]
        pieces.append(lax.ppermute(outgoing, "dish", pairs_list))
    blocks = []
    for source in range(dish_count):
        shift_of = jnp.bitwise_xor(me, source)
        chosen = pieces[dish_count - 1]
        for shift in range(dish_count - 2, -1, -1):
            chosen = jnp.where(shift_of == shift, pieces[shift], chosen)
        blocks.append(chosen)
    return jnp.concatenate(blocks, axis=0)


def solution(mesh):
    placed = (P("freq", "dish", None, None), P("freq", "dish", None, None), P(), P())
    return jax.shard_map(
        body, mesh=mesh, in_specs=placed, out_specs=P("freq", "dish"), check_vma=False
    )
```
